32 devices in a mesh: clips: 2 (over y), tm: 4 (over x, core), rows: 4 (over z).
Axes of the slice: x: 2, y: 2, z: 4, core: 2. Of those that a mesh axis runs over, the one named last changes fastest.
Arguments:
- segment_input: bfloat16 [4, 8, 4, 32, 384], P('clips', 'tm', 'rows'), parts along dimension 0, may hold values from -6 to 6
- inner_input: bfloat16 [4, 8, 4, 32, 384], P('clips', 'tm', 'rows'), parts along dimension 0, may hold values from -6 to 6
- lengths: int32 [4, 4], P('clips', 'tm'), parts along dimension 0, may hold values from 1 to 2
- inner_gain: float32 [384], replicated, may hold values from 0.25 to 1.75
- causal_weight: bfloat16 [3, 3, 3, 384, 384], replicated, may hold values from -0.0625 to 0.0625
- causal_bias: float32 [384], replicated, may hold values from -3 to 3
- attention_gain: float32 [384], replicated, may hold values from 0.25 to 1.75
- triple_weight: bfloat16 [384, 1152], replicated, may hold values from -0.4375 to 0.4375
- triple_bias: float32 [1152], replicated, may hold values from -150 to 150
- output_weight: bfloat16 [384, 384], replicated, may hold values from -0.3125 to 0.3125
- output_bias: float32 [384], replicated, may hold values from -3 to 3
Outputs:
- encoded: bfloat16 [4, 8, 4, 32, 384], P('clips', 'tm', 'rows'), parts along dimension 0
The draws below stay inside these ranges and needn't reach their ends.
There are 2 independent parts, one for each index of `clips`. The reference program is written for one: setup_inputs(seed, part) draws one part's arguments, and reference() takes and returns one part's arrays. A program takes and returns all parts, laid end to end along the dimension named above; an argument that names none is the same for every part. Nothing has to cross between parts.
Inputs may be any that keep to these rules, and one draw needn't show every extreme that they name: The valid frames of a clip in a section are that section's first lengths[b, s] frame slots.
All inputs are finite; a program needn't handle non-finite values.
Results may differ from the reference program's by a relative error of at most 0.0062.
Values may be sent and summed in bfloat16 or wider, within the bound.
No kernel may reach another device: no remote copies, remote signals or barrier semaphores. Data moves between devices by JAX's collectives and lax.ppermute only.
A program may use at most 128 MiB of HBM per device.

```python
import math
import jax
import jax.numpy as jnp
from jax import lax

CH = 384
SEC_FRAMES = 2
COLS = 32
CLIPS = 2
FRAMES = 8
HEIGHT = 4
N_TM = 4


def draw_triple_bias(key, part):
    first_key = jax.random.fold_in(key, 11)
    return 0.5 * jax.random.truncated_normal(first_key, -6.0, 6.0, (3 * CH,), jnp.float32)


def with_ends(drawn, key, low, largest):
    shape = drawn.shape
    spot = [jax.random.randint(jax.random.fold_in(key, axis), (), 0, shape[axis]) for axis in range(len(shape))]
    drawn = drawn.at[tuple(spot)].set(low)
    longest = shape.index(max(shape))
    spot[longest] = (spot[longest] + 1) % shape[longest]
    return drawn.at[tuple(spot)].set(largest)


def block_levels(stream_key, extent, cuts, low, high):
    def one(dim, parts):
        heights = jax.random.uniform(jax.random.fold_in(jax.random.fold_in(stream_key, 6), dim), (parts,), jnp.float32, low / len(cuts), high / len(cuts))
        return jnp.repeat(jnp.exp(heights), extent[dim] // parts).reshape((-1,) + (1,) * (len(extent) - dim - 1))

    factor_of = one(*cuts[0])
    for cut in cuts[1:]:
        factor_of = factor_of * one(*cut)
    return factor_of


def bell_draw(rng, dims, spread, most, shards=(), held_as=jnp.bfloat16):
    entries = spread * jax.random.normal(rng, dims, jnp.float32)
    if shards:
        entries = entries * block_levels(rng, dims, shards, -0.22, 0.18)
    return jnp.clip(entries, -most, most).astype(held_as)


def setup_inputs(seed: int = 0, part: int = 0) -> dict:
    streams_of = jax.random.split(jax.random.key(seed), 12)
    part_keys = jax.random.split(jax.random.fold_in(streams_of[11], part), 12)
    segment_input = bell_draw(part_keys[0], (CLIPS, FRAMES, HEIGHT, COLS, CH), 1.0, 6.0, ((1, 4), (2, 4)))
    inner_input = bell_draw(part_keys[1], (CLIPS, FRAMES, HEIGHT, COLS, CH), 1.0, 6.0, ((1, 4), (2, 4)))
    lengths = with_ends(jax.random.randint(part_keys[2], (CLIPS, N_TM), 1, SEC_FRAMES + 1), jax.random.fold_in(part_keys[2], 1), 1, SEC_FRAMES).astype(jnp.int32)
    inner_gain = jnp.clip(1.0 + 0.15 * jax.random.normal(streams_of[3], (CH,), jnp.float32), 0.25, 1.75)
    causal_weight = bell_draw(streams_of[4], (3, 3, 3, CH, CH), (27 * CH) ** -0.5, 0.0625)
    causal_bias = bell_draw(streams_of[5], (CH,), 0.5, 3.0, (), jnp.float32)
    attention_gain = jnp.clip(1.0 + 0.15 * jax.random.normal(streams_of[6], (CH,), jnp.float32), 0.25, 1.75)
    triple_weight = bell_draw(streams_of[7], (CH, 3 * CH), (CH // 2) ** -0.5, 0.4375)
    triple_bias = draw_triple_bias(jax.random.fold_in(streams_of[11], 71), part)
    output_weight = bell_draw(streams_of[9], (CH, CH), CH ** -0.5, 0.3125)
    output_bias = bell_draw(streams_of[10], (CH,), 0.5, 3.0, (), jnp.float32)
    return dict(segment_input=segment_input, inner_input=inner_input, lengths=lengths, inner_gain=inner_gain, causal_weight=causal_weight, causal_bias=causal_bias, attention_gain=attention_gain, triple_weight=triple_weight, triple_bias=triple_bias, output_weight=output_weight, output_bias=output_bias)


EPSILON = 1e-06

def normalize(field, gain):
    widened = field.astype(jnp.float32)
    return widened * lax.rsqrt(lax.optimization_barrier(jnp.mean(widened * widened, axis=-1, keepdims=True)) + EPSILON) * gain

def last_two(extended, counts):
    slot_total = extended.shape[1]
    chosen = []
    for position in range(2):
        target = counts + position
        picked = jnp.zeros_like(extended[:, 0])
        for slot_index in range(slot_total):
            matches = (target == slot_index)[:, None, None, None]
            picked = jnp.where(matches, extended[:, slot_index], picked)
        chosen.append(picked)
    return jnp.stack(chosen, axis=1)

def convolve(padded, causal_weight, causal_bias):
    clip_count, slot_total, rows_padded, column_count, channels = padded.shape
    frame_count = slot_total - 2
    row_count = rows_padded - 2
    widened = jnp.pad(padded, ((0, 0), (0, 0), (0, 0), (1, 1), (0, 0)))
    summed = jnp.zeros((clip_count * frame_count * row_count * column_count, channels), jnp.float32)
    for delta_time in range(3):
        for delta_row in range(3):
            window = widened[:, delta_time:delta_time + frame_count, delta_row:delta_row + row_count]
            columns = jnp.concatenate([window[:, :, :, delta_col:delta_col + column_count] for delta_col in range(3)], axis=-1)
            kernel = causal_weight[delta_time, delta_row].reshape(3 * channels, channels)
            summed = summed + jnp.dot(columns.reshape(-1, 3 * channels), kernel, preferred_element_type=jnp.float32)
    return summed.reshape(clip_count, frame_count, row_count, column_count, channels) + causal_bias

def attend(normed, triple_weight, triple_bias, output_weight, output_bias):
    frame_count, places, channels = normed.shape
    packed = jnp.dot(normed.reshape(-1, channels), triple_weight, preferred_element_type=jnp.float32) + triple_bias
    packed = packed.reshape(frame_count, places, 3 * channels)
    queries = packed[:, :, :channels]
    key_vectors = packed[:, :, channels:2 * channels]
    values = packed[:, :, 2 * channels:].astype(jnp.bfloat16)
    scores = jnp.einsum('nqc,nkc->nqk', queries, key_vectors, precision=lax.Precision.HIGHEST) / math.sqrt(channels)
    row_max = lax.optimization_barrier(jnp.max(scores, axis=-1, keepdims=True))
    exponent = jnp.exp(scores - row_max)
    weights = (exponent / lax.optimization_barrier(jnp.sum(exponent, axis=-1, keepdims=True))).astype(jnp.bfloat16)
    weights, values = lax.optimization_barrier((weights, values))
    attended = jnp.einsum('nqk,nkc->nqc', weights.astype(jnp.float32), values.astype(jnp.float32), precision=lax.Precision.HIGHEST).astype(jnp.bfloat16)
    projected = jnp.dot(attended.reshape(-1, channels), output_weight, preferred_element_type=jnp.float32) + output_bias
    return projected.reshape(frame_count, places, channels).astype(jnp.bfloat16)

def reference(segment_input, inner_input, lengths, inner_gain, causal_weight, causal_bias, attention_gain, triple_weight, triple_bias, output_weight, output_bias):
    activated = jax.nn.silu(normalize(inner_input, inner_gain)).astype(jnp.bfloat16)
    clip_count = activated.shape[0]
    carried = jnp.zeros((clip_count, 2) + activated.shape[2:], jnp.bfloat16)
    outputs = []
    for section in range(N_TM):
        own_frames = activated[:, section * SEC_FRAMES:(section + 1) * SEC_FRAMES]
        extended = jnp.concatenate([carried, own_frames], axis=1)
        padded = jnp.pad(extended, ((0, 0), (0, 0), (1, 1), (0, 0), (0, 0)))
        outputs.append(convolve(padded, causal_weight, causal_bias))
        carried = last_two(extended, lengths[:, section].astype(jnp.int32))
    convolved = jnp.concatenate(outputs, axis=1)
    residual = (segment_input.astype(jnp.float32) + convolved).astype(jnp.bfloat16)
    residual = lax.optimization_barrier(residual)
    normed = normalize(residual, attention_gain).astype(jnp.bfloat16)
    clip_count, frame_count, height, column_count, channels = normed.shape
    blocks = normed.reshape(clip_count, frame_count, height * column_count, channels)
    projected = lax.map(lambda clip_block: attend(clip_block, triple_weight, triple_bias, output_weight, output_bias), blocks)
    projected = lax.optimization_barrier(projected.reshape(normed.shape))
    slot_index = jnp.arange(frame_count, dtype=jnp.int32)[None, :] % SEC_FRAMES
    live_mask = (slot_index < jnp.repeat(lengths.astype(jnp.int32), SEC_FRAMES, axis=1)).astype(jnp.float32)
    summed = (residual.astype(jnp.float32) + projected.astype(jnp.float32)) * live_mask[:, :, None, None, None]
    return summed.astype(jnp.bfloat16)
```

```python
import math

import jax
import jax.numpy as jnp
from jax import lax
from jax.sharding import PartitionSpec as P

EPSILON = 1e-06


def prefix(part, axis, combine, identity):
    place = lax.axis_index(axis)
    gathered = jax.tree.map(lambda a: lax.all_gather(a, axis), part)
    state = jax.tree.map(lambda a, e: jnp.zeros_like(a) + jnp.asarray(e, a.dtype), part, identity)

    def one(step, state):
        return combine(
            state, jax.tree.map(lambda a: lax.dynamic_index_in_dim(a, step, 0, False), gathered)
        )

    return lax.fori_loop(0, place, one, state)


def as_sent(x):

    def short(part):
        return part.astype(jnp.bfloat16) if part.dtype == jnp.float32 else part

    return jax.tree.map(short, x)


def with_halo(cells, sides, width):
    for axis, dim in sides:
        count = lax.axis_size(axis)
        ends = count - 1
        head = lax.slice_in_dim(cells, 0, width, axis=dim)
        tail = lax.slice_in_dim(cells, cells.shape[dim] - width, cells.shape[dim], axis=dim)
        cells = jnp.concatenate(
            [
                lax.ppermute(tail, axis, [(i, (i + 1) % count) for i in range(ends)]),
                cells,
                lax.ppermute(head, axis, [((i + 1) % count, i) for i in range(ends)]),
            ],
            axis=dim,
        )
    return cells


def normalize(field, gain):
    widened = field.astype(jnp.float32)
    return widened * lax.rsqrt(jnp.mean(widened * widened, axis=-1, keepdims=True) + EPSILON) * gain


def last_two(extended, counts):
    slot_total = extended.shape[1]
    chosen = []
    for position in range(2):
        target = counts + position
        picked = jnp.zeros_like(extended[:, 0])
        for slot_index in range(slot_total):
            matches = (target == slot_index)[:, None, None, None]
            picked = jnp.where(matches, extended[:, slot_index], picked)
        chosen.append(picked)
    return jnp.stack(chosen, axis=1)


def summarize(activated, counts):
    blanks = jnp.zeros((activated.shape[0], 2) + activated.shape[2:], activated.dtype)
    summary = last_two(jnp.concatenate([blanks, activated], axis=1), counts)
    return (summary, jnp.minimum(counts, 2).astype(jnp.bfloat16))


def join_later(earlier, later):
    early_frames, early_count = earlier
    late_frames, late_count = later
    complete = (late_count > 1.5)[:, None, None, None, None]
    single = (late_count > 0.5)[:, None, None, None, None]
    shifted = jnp.concatenate([early_frames[:, 1:], late_frames[:, 1:]], axis=1)
    frames = jnp.where(complete, late_frames, jnp.where(single, shifted, early_frames))
    total_count = jnp.minimum(early_count + late_count, 2.0).astype(early_count.dtype)
    return (frames, total_count)


def incoming_cache(summary, counts):
    starting = (jnp.zeros_like(summary), jnp.zeros_like(counts))
    combined = prefix((summary, counts), "tm", join_later, starting)
    return combined[0]


def convolve(padded, causal_weight, causal_bias):
    clip_count, slot_total, rows_padded, column_count, channels = padded.shape
    frame_count = slot_total - 2
    row_count = rows_padded - 2
    widened = jnp.pad(padded, ((0, 0), (0, 0), (0, 0), (1, 1), (0, 0)))
    summed = jnp.zeros((clip_count * frame_count * row_count * column_count, channels), jnp.float32)
    for delta_time in range(3):
        for delta_row in range(3):
            window = widened[
                :, delta_time : delta_time + frame_count, delta_row : delta_row + row_count
            ]
            columns = jnp.concatenate(
                [window[:, :, :, delta_col : delta_col + column_count] for delta_col in range(3)],
                axis=-1,
            )
            kernel = causal_weight[delta_time, delta_row].reshape(3 * channels, channels)
            summed = summed + jnp.dot(
                columns.reshape(-1, 3 * channels), kernel, preferred_element_type=jnp.float32
            )
    return summed.reshape(clip_count, frame_count, row_count, column_count, channels) + causal_bias


def attend(normed, triple_weight, triple_bias, output_weight, output_bias):
    frame_count, places, channels = normed.shape
    packed = (
        jnp.dot(normed.reshape(-1, channels), triple_weight, preferred_element_type=jnp.float32)
        + triple_bias
    )
    packed = packed.reshape(frame_count, places, 3 * channels)
    queries = packed[:, :, :channels]
    key_vectors = packed[:, :, channels : 2 * channels]
    values = packed[:, :, 2 * channels :].astype(jnp.bfloat16)
    scores = jnp.einsum(
        "nqc,nkc->nqk", queries, key_vectors, precision=lax.Precision.HIGHEST
    ) / math.sqrt(channels)
    row_max = jnp.max(scores, axis=-1, keepdims=True)
    exponent = jnp.exp(scores - row_max)
    weights = (exponent / jnp.sum(exponent, axis=-1, keepdims=True)).astype(jnp.bfloat16)
    attended = jnp.einsum(
        "nqk,nkc->nqc", weights, values, preferred_element_type=jnp.float32
    ).astype(jnp.bfloat16)
    projected = (
        jnp.dot(attended.reshape(-1, channels), output_weight, preferred_element_type=jnp.float32)
        + output_bias
    )
    return projected.reshape(frame_count, places, channels).astype(jnp.bfloat16)


def body(
    segment_input,
    inner_input,
    lengths,
    inner_gain,
    causal_weight,
    causal_bias,
    attention_gain,
    triple_weight,
    triple_bias,
    output_weight,
    output_bias,
):
    clip_count, frame_count, row_count, column_count, channels = segment_input.shape
    activated = jax.nn.silu(normalize(inner_input, inner_gain)).astype(jnp.bfloat16)
    counts = lengths[:, 0]
    live_mask = (jnp.arange(frame_count, dtype=jnp.int32)[None, :] < counts[:, None]).astype(
        jnp.float32
    )
    carried = incoming_cache(*summarize(activated, counts))
    extended = jnp.concatenate([carried, activated], axis=1)
    padded = with_halo(as_sent(extended), (("rows", 2),), 1).astype(extended.dtype)
    convolved = convolve(padded, causal_weight, causal_bias)
    residual = (segment_input.astype(jnp.float32) + convolved).astype(jnp.bfloat16)
    residual = lax.optimization_barrier(residual)
    normed = normalize(residual, attention_gain).astype(jnp.bfloat16)
    row_devices = lax.axis_size("rows")
    per_device = clip_count * frame_count // row_devices
    grouped = normed.reshape(row_devices, per_device, row_count, column_count, channels)
    portion = lax.all_to_all(grouped, "rows", split_axis=0, concat_axis=2, tiled=True)
    owned = portion.shape[1]
    height = portion.shape[2]
    flat = portion.reshape(owned, height * column_count, channels)
    result = attend(flat, triple_weight, triple_bias, output_weight, output_bias)
    result = result.reshape(1, owned, height, column_count, channels)
    projected = lax.all_to_all(result, "rows", split_axis=2, concat_axis=0, tiled=True)
    projected = projected.reshape(clip_count, frame_count, row_count, column_count, channels)
    projected = lax.optimization_barrier(projected)
    summed = residual.astype(jnp.float32) + projected.astype(jnp.float32)
    return (summed * live_mask[:, :, None, None, None]).astype(jnp.bfloat16)


def activate(field, gain):
    return jax.nn.silu(normalize(field, gain)).astype(jnp.bfloat16)


def gathered_body(
    segment_input,
    inner_input,
    lengths,
    inner_gain,
    causal_weight,
    causal_bias,
    attention_gain,
    triple_weight,
    triple_bias,
    output_weight,
    output_bias,
):
    clip_count, frame_count, row_count, column_count, channels = segment_input.shape
    sections = lax.axis_size("tm")
    inner_all = lax.all_gather(inner_input, "rows", axis=2, tiled=True)
    segment_all = lax.all_gather(segment_input, "rows", axis=2, tiled=True)
    counts = lengths[:, 0]
    wide = (counts > 1)[:, None, None, None]
    last_raw = jnp.where(wide, inner_all[:, frame_count - 1], inner_all[:, 0])
    prev_raw = lax.ppermute(inner_all, "tm", [(i, i + 1) for i in range(sections - 1)])
    prev_counts = lax.ppermute(counts, "tm", [(i, i + 1) for i in range(sections - 1)])
    before_raw = lax.ppermute(last_raw, "tm", [(i, i + 2) for i in range(sections - 2)])
    own = activate(inner_all, inner_gain)
    prev = activate(prev_raw, inner_gain)
    before = activate(before_raw, inner_gain)
    prev_wide = (prev_counts > 1)[:, None, None, None]
    carried = jnp.stack(
        [
            jnp.where(prev_wide, prev[:, frame_count - 2], before),
            jnp.where(prev_wide, prev[:, frame_count - 1], prev[:, 0]),
        ],
        axis=1,
    )
    extended = jnp.concatenate([carried, own], axis=1)
    padded = jnp.pad(extended, ((0, 0), (0, 0), (1, 1), (0, 0), (0, 0)))
    convolved = convolve(padded, causal_weight, causal_bias)
    residual = (segment_all.astype(jnp.float32) + convolved).astype(jnp.bfloat16)
    normed = normalize(residual, attention_gain).astype(jnp.bfloat16)
    height = normed.shape[2]
    frames = clip_count * frame_count
    places = height * column_count
    flat = normed.reshape(frames * places, channels)
    packed = (
        jnp.dot(flat, triple_weight[:, channels:], preferred_element_type=jnp.float32)
        + triple_bias[channels:]
    ).reshape(frames, places, 2 * channels)
    key_vectors = packed[:, :, :channels]
    values = packed[:, :, channels:].astype(jnp.bfloat16)
    start = lax.axis_index("rows") * row_count
    mine = lax.dynamic_slice_in_dim(normed, start, row_count, axis=2)
    queries = (
        jnp.dot(
            mine.reshape(-1, channels), triple_weight[:, :channels],
            preferred_element_type=jnp.float32,
        )
        + triple_bias[:channels]
    ).reshape(frames, row_count * column_count, channels)
    scores = jnp.einsum(
        "nqc,nkc->nqk", queries, key_vectors, precision=lax.Precision.HIGHEST
    ) / math.sqrt(channels)
    row_max = jnp.max(scores, axis=-1, keepdims=True)
    exponent = jnp.exp(scores - row_max)
    weights = (exponent / jnp.sum(exponent, axis=-1, keepdims=True)).astype(jnp.bfloat16)
    attended = jnp.einsum(
        "nqk,nkc->nqc", weights, values, preferred_element_type=jnp.float32
    ).astype(jnp.bfloat16)
    projected = (
        jnp.dot(attended.reshape(-1, channels), output_weight, preferred_element_type=jnp.float32)
        + output_bias
    ).astype(jnp.bfloat16)
    projected = projected.reshape(clip_count, frame_count, row_count, column_count, channels)
    residual_mine = lax.dynamic_slice_in_dim(residual, start, row_count, axis=2)
    live_mask = (jnp.arange(frame_count, dtype=jnp.int32)[None, :] < counts[:, None]).astype(
        jnp.float32
    )
    summed = residual_mine.astype(jnp.float32) + projected.astype(jnp.float32)
    return (summed * live_mask[:, :, None, None, None]).astype(jnp.bfloat16)


GATHER_LIMIT = 1 << 22


def chosen_body(segment_input, inner_input, *rest):
    gathered = inner_input.size * inner_input.dtype.itemsize * lax.axis_size("rows")
    if gathered <= GATHER_LIMIT:
        return gathered_body(segment_input, inner_input, *rest)
    return body(segment_input, inner_input, *rest)


def solution(mesh):
    placed = (
        P("clips", "tm", "rows", None, None),
        P("clips", "tm", "rows", None, None),
        P("clips", "tm"),
        P(),
        P(),
        P(),
        P(),
        P(),
        P(),
        P(),
        P(),
    )
    return jax.shard_map(
        chosen_body,
        mesh=mesh,
        in_specs=placed,
        out_specs=P("clips", "tm", "rows", None, None),
        check_vma=False,
    )
```

```python
import math

import jax
import jax.numpy as jnp
from jax import lax
from jax.sharding import PartitionSpec as P

EPSILON = 1e-06


def prefix(part, axis, combine, identity):
    place = lax.axis_index(axis)
    gathered = jax.tree.map(lambda a: lax.all_gather(a, axis), part)
    state = jax.tree.map(lambda a, e: jnp.zeros_like(a) + jnp.asarray(e, a.dtype), part, identity)

    def one(step, state):
        return combine(
            state, jax.tree.map(lambda a: lax.dynamic_index_in_dim(a, step, 0, False), gathered)
        )

    return lax.fori_loop(0, place, one, state)


def as_sent(x):

    def short(part):
        return part.astype(jnp.bfloat16) if part.dtype == jnp.float32 else part

    return jax.tree.map(short, x)


def with_halo(cells, sides, width):
    for axis, dim in sides:
        count = lax.axis_size(axis)
        ends = count - 1
        head = lax.slice_in_dim(cells, 0, width, axis=dim)
        tail = lax.slice_in_dim(cells, cells.shape[dim] - width, cells.shape[dim], axis=dim)
        cells = jnp.concatenate(
            [
                lax.ppermute(tail, axis, [(i, (i + 1) % count) for i in range(ends)]),
                cells,
                lax.ppermute(head, axis, [((i + 1) % count, i) for i in range(ends)]),
            ],
            axis=dim,
        )
    return cells


def normalize(field, gain):
    widened = field.astype(jnp.float32)
    return widened * lax.rsqrt(jnp.mean(widened * widened, axis=-1, keepdims=True) + EPSILON) * gain


def last_two(extended, counts):
    slot_total = extended.shape[1]
    chosen = []
    for position in range(2):
        target = counts + position
        picked = jnp.zeros_like(extended[:, 0])
        for slot_index in range(slot_total):
            matches = (target == slot_index)[:, None, None, None]
            picked = jnp.where(matches, extended[:, slot_index], picked)
        chosen.append(picked)
    return jnp.stack(chosen, axis=1)


def summarize(activated, counts):
    blanks = jnp.zeros((activated.shape[0], 2) + activated.shape[2:], activated.dtype)
    summary = last_two(jnp.concatenate([blanks, activated], axis=1), counts)
    return (summary, jnp.minimum(counts, 2).astype(jnp.bfloat16))


def join_later(earlier, later):
    early_frames, early_count = earlier
    late_frames, late_count = later
    complete = (late_count > 1.5)[:, None, None, None, None]
    single = (late_count > 0.5)[:, None, None, None, None]
    shifted = jnp.concatenate([early_frames[:, 1:], late_frames[:, 1:]], axis=1)
    frames = jnp.where(complete, late_frames, jnp.where(single, shifted, early_frames))
    total_count = jnp.minimum(early_count + late_count, 2.0).astype(early_count.dtype)
    return (frames, total_count)


def incoming_cache(summary, counts):
    starting = (jnp.zeros_like(summary), jnp.zeros_like(counts))
    combined = prefix((summary, counts), "tm", join_later, starting)
    return combined[0]


def convolve(padded, causal_weight, causal_bias):
    clip_count, slot_total, rows_padded, column_count, channels = padded.shape
    frame_count = slot_total - 2
    row_count = rows_padded - 2
    widened = jnp.pad(padded, ((0, 0), (0, 0), (0, 0), (1, 1), (0, 0)))
    summed = jnp.zeros((clip_count * frame_count * row_count * column_count, channels), jnp.float32)
    for delta_time in range(3):
        for delta_row in range(3):
            window = widened[
                :, delta_time : delta_time + frame_count, delta_row : delta_row + row_count
            ]
            columns = jnp.concatenate(
                [window[:, :, :, delta_col : delta_col + column_count] for delta_col in range(3)],
                axis=-1,
            )
            kernel = causal_weight[delta_time, delta_row].reshape(3 * channels, channels)
            summed = summed + jnp.dot(
                columns.reshape(-1, 3 * channels), kernel, preferred_element_type=jnp.float32
            )
    return summed.reshape(clip_count, frame_count, row_count, column_count, channels) + causal_bias


def attend(normed, triple_weight, triple_bias, output_weight, output_bias):
    frame_count, places, channels = normed.shape
    packed = (
        jnp.dot(normed.reshape(-1, channels), triple_weight, preferred_element_type=jnp.float32)
        + triple_bias
    )
    packed = packed.reshape(frame_count, places, 3 * channels)
    queries = packed[:, :, :channels]
    key_vectors = packed[:, :, channels : 2 * channels]
    values = packed[:, :, 2 * channels :].astype(jnp.bfloat16)
    scores = jnp.einsum(
        "nqc,nkc->nqk", queries, key_vectors, precision=lax.Precision.HIGHEST
    ) / math.sqrt(channels)
    row_max = jnp.max(scores, axis=-1, keepdims=True)
    exponent = jnp.exp(scores - row_max)
    weights = (exponent / jnp.sum(exponent, axis=-1, keepdims=True)).astype(jnp.bfloat16)
    attended = jnp.einsum(
        "nqk,nkc->nqc", weights, values, preferred_element_type=jnp.float32
    ).astype(jnp.bfloat16)
    projected = (
        jnp.dot(attended.reshape(-1, channels), output_weight, preferred_element_type=jnp.float32)
        + output_bias
    )
    return projected.reshape(frame_count, places, channels).astype(jnp.bfloat16)


def body(
    segment_input,
    inner_input,
    lengths,
    inner_gain,
    causal_weight,
    causal_bias,
    attention_gain,
    triple_weight,
    triple_bias,
    output_weight,
    output_bias,
):
    clip_count, frame_count, row_count, column_count, channels = segment_input.shape
    activated = jax.nn.silu(normalize(inner_input, inner_gain)).astype(jnp.bfloat16)
    counts = lengths[:, 0]
    live_mask = (jnp.arange(frame_count, dtype=jnp.int32)[None, :] < counts[:, None]).astype(
        jnp.float32
    )
    carried = incoming_cache(*summarize(activated, counts))
    extended = jnp.concatenate([carried, activated], axis=1)
    padded = with_halo(as_sent(extended), (("rows", 2),), 1).astype(extended.dtype)
    convolved = convolve(padded, causal_weight, causal_bias)
    residual = (segment_input.astype(jnp.float32) + convolved).astype(jnp.bfloat16)
    residual = lax.optimization_barrier(residual)
    normed = normalize(residual, attention_gain).astype(jnp.bfloat16)
    row_devices = lax.axis_size("rows")
    per_device = clip_count * frame_count // row_devices
    grouped = normed.reshape(row_devices, per_device, row_count, column_count, channels)
    portion = lax.all_to_all(grouped, "rows", split_axis=0, concat_axis=2, tiled=True)
    owned = portion.shape[1]
    height = portion.shape[2]
    flat = portion.reshape(owned, height * column_count, channels)
    result = attend(flat, triple_weight, triple_bias, output_weight, output_bias)
    result = result.reshape(1, owned, height, column_count, channels)
    projected = lax.all_to_all(result, "rows", split_axis=2, concat_axis=0, tiled=True)
    projected = projected.reshape(clip_count, frame_count, row_count, column_count, channels)
    projected = lax.optimization_barrier(projected)
    summed = residual.astype(jnp.float32) + projected.astype(jnp.float32)
    return (summed * live_mask[:, :, None, None, None]).astype(jnp.bfloat16)


def activate(field, gain):
    return jax.nn.silu(normalize(field, gain)).astype(jnp.bfloat16)


def conv3d(frames, causal_weight, time_padding):
    return lax.conv_general_dilated(
        frames,
        causal_weight,
        window_strides=(1, 1, 1),
        padding=(time_padding, (1, 1), (1, 1)),
        dimension_numbers=("NDHWC", "DHWIO", "NDHWC"),
        preferred_element_type=jnp.float32,
    )


def gathered_body(
    segment_input,
    inner_input,
    lengths,
    inner_gain,
    causal_weight,
    causal_bias,
    attention_gain,
    triple_weight,
    triple_bias,
    output_weight,
    output_bias,
):
    clip_count, frame_count, row_count, column_count, channels = segment_input.shape
    sections = lax.axis_size("tm")
    counts = lengths[:, 0]
    ahead = [(i, i + 1) for i in range(sections - 1)]
    prev_counts = lax.ppermute(counts, "tm", ahead)
    both = jnp.concatenate([inner_input, segment_input], axis=0)
    both_all = lax.all_gather(both, "rows", axis=2, tiled=True)
    inner_all = both_all[:clip_count]
    segment_all = both_all[clip_count:]
    wide = (counts > 1)[:, None, None, None]
    last_raw = jnp.where(wide, inner_all[:, frame_count - 1], inner_all[:, 0])
    prev_raw = lax.ppermute(inner_all, "tm", ahead)
    before_raw = lax.ppermute(last_raw, "tm", [(i, i + 2) for i in range(sections - 2)])
    own = activate(inner_all, inner_gain)
    own_part = conv3d(own, causal_weight, (2, 0))
    prev = activate(prev_raw, inner_gain)
    before = activate(before_raw, inner_gain)
    prev_wide = (prev_counts > 1)[:, None, None, None]
    carried = jnp.stack(
        [
            jnp.where(prev_wide, prev[:, frame_count - 2], before),
            jnp.where(prev_wide, prev[:, frame_count - 1], prev[:, 0]),
        ],
        axis=1,
    )
    carried_part = conv3d(carried, causal_weight, (0, frame_count))
    convolved = own_part + carried_part + causal_bias
    residual = (segment_all.astype(jnp.float32) + convolved).astype(jnp.bfloat16)
    normed = normalize(residual, attention_gain).astype(jnp.bfloat16)
    height = normed.shape[2]
    frames = clip_count * frame_count
    places = height * column_count
    flat = normed.reshape(frames * places, channels)
    packed = (
        jnp.dot(flat, triple_weight[:, channels:], preferred_element_type=jnp.float32)
        + triple_bias[channels:]
    ).reshape(frames, places, 2 * channels)
    key_vectors = packed[:, :, :channels]
    values = packed[:, :, channels:].astype(jnp.bfloat16)
    start = lax.axis_index("rows") * row_count
    mine = lax.dynamic_slice_in_dim(normed, start, row_count, axis=2)
    queries = (
        jnp.dot(
            mine.reshape(-1, channels), triple_weight[:, :channels],
            preferred_element_type=jnp.float32,
        )
        + triple_bias[:channels]
    ).reshape(frames, row_count * column_count, channels)
    scores = jnp.einsum(
        "nqc,nkc->nqk", queries, key_vectors, precision=lax.Precision.HIGHEST
    ) / math.sqrt(channels)
    row_max = jnp.max(scores, axis=-1, keepdims=True)
    exponent = jnp.exp(scores - row_max)
    weights = (exponent / jnp.sum(exponent, axis=-1, keepdims=True)).astype(jnp.bfloat16)
    attended = jnp.einsum(
        "nqk,nkc->nqc", weights, values, preferred_element_type=jnp.float32
    ).astype(jnp.bfloat16)
    projected = (
        jnp.dot(attended.reshape(-1, channels), output_weight, preferred_element_type=jnp.float32)
        + output_bias
    ).astype(jnp.bfloat16)
    projected = projected.reshape(clip_count, frame_count, row_count, column_count, channels)
    residual_mine = lax.dynamic_slice_in_dim(residual, start, row_count, axis=2)
    live_mask = (jnp.arange(frame_count, dtype=jnp.int32)[None, :] < counts[:, None]).astype(
        jnp.float32
    )
    summed = residual_mine.astype(jnp.float32) + projected.astype(jnp.float32)
    return (summed * live_mask[:, :, None, None, None]).astype(jnp.bfloat16)


GATHER_LIMIT = 1 << 22


def chosen_body(segment_input, inner_input, *rest):
    gathered = inner_input.size * inner_input.dtype.itemsize * lax.axis_size("rows")
    if gathered <= GATHER_LIMIT:
        return gathered_body(segment_input, inner_input, *rest)
    return body(segment_input, inner_input, *rest)


def solution(mesh):
    placed = (
        P("clips", "tm", "rows", None, None),
        P("clips", "tm", "rows", None, None),
        P("clips", "tm"),
        P(),
        P(),
        P(),
        P(),
        P(),
        P(),
        P(),
        P(),
    )
    return jax.shard_map(
        chosen_body,
        mesh=mesh,
        in_specs=placed,
        out_specs=P("clips", "tm", "rows", None, None),
        check_vma=False,
    )
```

```python
import math

import jax
import jax.numpy as jnp
from jax import lax
from jax.sharding import PartitionSpec as P
from jax.experimental import pallas as pl
from jax.experimental.pallas import tpu as pltpu

EPSILON = 1e-06


def prefix(part, axis, combine, identity):
    place = lax.axis_index(axis)
    gathered = jax.tree.map(lambda a: lax.all_gather(a, axis), part)
    state = jax.tree.map(lambda a, e: jnp.zeros_like(a) + jnp.asarray(e, a.dtype), part, identity)

    def one(step, state):
        return combine(
            state, jax.tree.map(lambda a: lax.dynamic_index_in_dim(a, step, 0, False), gathered)
        )

    return lax.fori_loop(0, place, one, state)


def as_sent(x):

    def short(part):
        return part.astype(jnp.bfloat16) if part.dtype == jnp.float32 else part

    return jax.tree.map(short, x)


def with_halo(cells, sides, width):
    for axis, dim in sides:
        count = lax.axis_size(axis)
        ends = count - 1
        head = lax.slice_in_dim(cells, 0, width, axis=dim)
        tail = lax.slice_in_dim(cells, cells.shape[dim] - width, cells.shape[dim], axis=dim)
        cells = jnp.concatenate(
            [
                lax.ppermute(tail, axis, [(i, (i + 1) % count) for i in range(ends)]),
                cells,
                lax.ppermute(head, axis, [((i + 1) % count, i) for i in range(ends)]),
            ],
            axis=dim,
        )
    return cells


def normalize(field, gain):
    widened = field.astype(jnp.float32)
    return widened * lax.rsqrt(jnp.mean(widened * widened, axis=-1, keepdims=True) + EPSILON) * gain


def last_two(extended, counts):
    slot_total = extended.shape[1]
    chosen = []
    for position in range(2):
        target = counts + position
        picked = jnp.zeros_like(extended[:, 0])
        for slot_index in range(slot_total):
            matches = (target == slot_index)[:, None, None, None]
            picked = jnp.where(matches, extended[:, slot_index], picked)
        chosen.append(picked)
    return jnp.stack(chosen, axis=1)


def summarize(activated, counts):
    blanks = jnp.zeros((activated.shape[0], 2) + activated.shape[2:], activated.dtype)
    summary = last_two(jnp.concatenate([blanks, activated], axis=1), counts)
    return (summary, jnp.minimum(counts, 2).astype(jnp.bfloat16))


def join_later(earlier, later):
    early_frames, early_count = earlier
    late_frames, late_count = later
    complete = (late_count > 1.5)[:, None, None, None, None]
    single = (late_count > 0.5)[:, None, None, None, None]
    shifted = jnp.concatenate([early_frames[:, 1:], late_frames[:, 1:]], axis=1)
    frames = jnp.where(complete, late_frames, jnp.where(single, shifted, early_frames))
    total_count = jnp.minimum(early_count + late_count, 2.0).astype(early_count.dtype)
    return (frames, total_count)


def incoming_cache(summary, counts):
    starting = (jnp.zeros_like(summary), jnp.zeros_like(counts))
    combined = prefix((summary, counts), "tm", join_later, starting)
    return combined[0]


def convolve(padded, causal_weight, causal_bias):
    clip_count, slot_total, rows_padded, column_count, channels = padded.shape
    frame_count = slot_total - 2
    row_count = rows_padded - 2
    widened = jnp.pad(padded, ((0, 0), (0, 0), (0, 0), (1, 1), (0, 0)))
    summed = jnp.zeros((clip_count * frame_count * row_count * column_count, channels), jnp.float32)
    for delta_time in range(3):
        for delta_row in range(3):
            window = widened[
                :, delta_time : delta_time + frame_count, delta_row : delta_row + row_count
            ]
            columns = jnp.concatenate(
                [window[:, :, :, delta_col : delta_col + column_count] for delta_col in range(3)],
                axis=-1,
            )
            kernel = causal_weight[delta_time, delta_row].reshape(3 * channels, channels)
            summed = summed + jnp.dot(
                columns.reshape(-1, 3 * channels), kernel, preferred_element_type=jnp.float32
            )
    return summed.reshape(clip_count, frame_count, row_count, column_count, channels) + causal_bias


def attend(normed, triple_weight, triple_bias, output_weight, output_bias):
    frame_count, places, channels = normed.shape
    packed = (
        jnp.dot(normed.reshape(-1, channels), triple_weight, preferred_element_type=jnp.float32)
        + triple_bias
    )
    packed = packed.reshape(frame_count, places, 3 * channels)
    queries = packed[:, :, :channels]
    key_vectors = packed[:, :, channels : 2 * channels]
    values = packed[:, :, 2 * channels :].astype(jnp.bfloat16)
    scores = jnp.einsum(
        "nqc,nkc->nqk", queries, key_vectors, precision=lax.Precision.HIGHEST
    ) / math.sqrt(channels)
    row_max = jnp.max(scores, axis=-1, keepdims=True)
    exponent = jnp.exp(scores - row_max)
    weights = (exponent / jnp.sum(exponent, axis=-1, keepdims=True)).astype(jnp.bfloat16)
    attended = jnp.einsum(
        "nqk,nkc->nqc", weights, values, preferred_element_type=jnp.float32
    ).astype(jnp.bfloat16)
    projected = (
        jnp.dot(attended.reshape(-1, channels), output_weight, preferred_element_type=jnp.float32)
        + output_bias
    )
    return projected.reshape(frame_count, places, channels).astype(jnp.bfloat16)


def body(
    segment_input,
    inner_input,
    lengths,
    inner_gain,
    causal_weight,
    causal_bias,
    attention_gain,
    triple_weight,
    triple_bias,
    output_weight,
    output_bias,
):
    clip_count, frame_count, row_count, column_count, channels = segment_input.shape
    activated = jax.nn.silu(normalize(inner_input, inner_gain)).astype(jnp.bfloat16)
    counts = lengths[:, 0]
    live_mask = (jnp.arange(frame_count, dtype=jnp.int32)[None, :] < counts[:, None]).astype(
        jnp.float32
    )
    carried = incoming_cache(*summarize(activated, counts))
    extended = jnp.concatenate([carried, activated], axis=1)
    padded = with_halo(as_sent(extended), (("rows", 2),), 1).astype(extended.dtype)
    convolved = convolve(padded, causal_weight, causal_bias)
    residual = (segment_input.astype(jnp.float32) + convolved).astype(jnp.bfloat16)
    residual = lax.optimization_barrier(residual)
    normed = normalize(residual, attention_gain).astype(jnp.bfloat16)
    row_devices = lax.axis_size("rows")
    per_device = clip_count * frame_count // row_devices
    grouped = normed.reshape(row_devices, per_device, row_count, column_count, channels)
    portion = lax.all_to_all(grouped, "rows", split_axis=0, concat_axis=2, tiled=True)
    owned = portion.shape[1]
    height = portion.shape[2]
    flat = portion.reshape(owned, height * column_count, channels)
    result = attend(flat, triple_weight, triple_bias, output_weight, output_bias)
    result = result.reshape(1, owned, height, column_count, channels)
    projected = lax.all_to_all(result, "rows", split_axis=2, concat_axis=0, tiled=True)
    projected = projected.reshape(clip_count, frame_count, row_count, column_count, channels)
    projected = lax.optimization_barrier(projected)
    summed = residual.astype(jnp.float32) + projected.astype(jnp.float32)
    return (summed * live_mask[:, :, None, None, None]).astype(jnp.bfloat16)


def activate(field, gain):
    return jax.nn.silu(normalize(field, gain)).astype(jnp.bfloat16)


def conv_kernel(x_ref, w_ref, b_ref, o_ref, acc_ref):
    kt = pl.program_id(0)
    kh = pl.program_id(1)
    clips, slots, rows, columns, width = x_ref.shape
    frames = slots - 2
    height = rows - 2

    @pl.when((kt == 0) & (kh == 0))
    def _():
        acc_ref[...] = jnp.zeros_like(acc_ref)

    window = x_ref[:, pl.ds(kt, frames), pl.ds(kh, height), :, :]
    lhs = window.reshape(clips * frames * height * columns, width)
    weight = w_ref[...].reshape(width, w_ref.shape[-1])
    acc_ref[...] += jnp.dot(lhs, weight, preferred_element_type=jnp.float32)

    @pl.when((kt == 2) & (kh == 2))
    def _():
        o_ref[...] = acc_ref[...] + b_ref[...]


def conv_all_rows(extended, causal_weight, causal_bias):
    clips, slots, height, columns, channels = extended.shape
    frames = slots - 2
    padded = jnp.pad(extended, ((0, 0), (0, 0), (1, 1), (1, 1), (0, 0)))
    taps = jnp.concatenate(
        [padded[:, :, :, kw : kw + columns] for kw in range(3)], axis=-1
    )
    places = clips * frames * height * columns
    out = pl.pallas_call(
        conv_kernel,
        grid=(3, 3),
        in_specs=[
            pl.BlockSpec(taps.shape, lambda kt, kh: (0, 0, 0, 0, 0)),
            pl.BlockSpec((None, None, 3, channels, channels), lambda kt, kh: (kt, kh, 0, 0, 0)),
            pl.BlockSpec((1, channels), lambda kt, kh: (0, 0)),
        ],
        out_specs=pl.BlockSpec((places, channels), lambda kt, kh: (0, 0)),
        out_shape=jax.ShapeDtypeStruct((places, channels), jnp.float32),
        scratch_shapes=[pltpu.VMEM((places, channels), jnp.float32)],
        compiler_params=pltpu.CompilerParams(
            dimension_semantics=("arbitrary", "arbitrary"),
            vmem_limit_bytes=48 * 1024 * 1024,
        ),
        cost_estimate=pl.CostEstimate(
            flops=2 * places * 27 * channels * channels,
            transcendentals=0,
            bytes_accessed=causal_weight.size * 2 + taps.size * 2 + places * channels * 4,
        ),
    )(taps, causal_weight, causal_bias.reshape(1, channels))
    return out.reshape(clips, frames, height, columns, channels)


def gathered_body(
    segment_input,
    inner_input,
    lengths,
    inner_gain,
    causal_weight,
    causal_bias,
    attention_gain,
    triple_weight,
    triple_bias,
    output_weight,
    output_bias,
):
    clip_count, frame_count, row_count, column_count, channels = segment_input.shape
    sections = lax.axis_size("tm")
    counts = lengths[:, 0]
    ahead = [(i, i + 1) for i in range(sections - 1)]
    prev_counts = lax.ppermute(counts, "tm", ahead)
    both = jnp.concatenate([inner_input, segment_input], axis=0)
    both_all = lax.all_gather(both, "rows", axis=2, tiled=True)
    inner_all = both_all[:clip_count]
    segment_all = both_all[clip_count:]
    wide = (counts > 1)[:, None, None, None]
    last_raw = jnp.where(wide, inner_all[:, frame_count - 1], inner_all[:, 0])
    prev_raw = lax.ppermute(inner_all, "tm", ahead)
    before_raw = lax.ppermute(last_raw, "tm", [(i, i + 2) for i in range(sections - 2)])
    own = activate(inner_all, inner_gain)
    prev = activate(prev_raw, inner_gain)
    before = activate(before_raw, inner_gain)
    prev_wide = (prev_counts > 1)[:, None, None, None]
    carried = jnp.stack(
        [
            jnp.where(prev_wide, prev[:, frame_count - 2], before),
            jnp.where(prev_wide, prev[:, frame_count - 1], prev[:, 0]),
        ],
        axis=1,
    )
    extended = jnp.concatenate([carried, own], axis=1)
    convolved = conv_all_rows(extended, causal_weight, causal_bias)
    residual = (segment_all.astype(jnp.float32) + convolved).astype(jnp.bfloat16)
    normed = normalize(residual, attention_gain).astype(jnp.bfloat16)
    height = normed.shape[2]
    frames = clip_count * frame_count
    places = height * column_count
    flat = normed.reshape(frames * places, channels)
    packed = (
        jnp.dot(flat, triple_weight[:, channels:], preferred_element_type=jnp.float32)
        + triple_bias[channels:]
    ).reshape(frames, places, 2 * channels)
    key_vectors = packed[:, :, :channels]
    values = packed[:, :, channels:].astype(jnp.bfloat16)
    start = lax.axis_index("rows") * row_count
    mine = lax.dynamic_slice_in_dim(normed, start, row_count, axis=2)
    queries = (
        jnp.dot(
            mine.reshape(-1, channels), triple_weight[:, :channels],
            preferred_element_type=jnp.float32,
        )
        + triple_bias[:channels]
    ).reshape(frames, row_count * column_count, channels)
    scores = jnp.einsum(
        "nqc,nkc->nqk", queries, key_vectors, precision=lax.Precision.HIGHEST
    ) / math.sqrt(channels)
    row_max = jnp.max(scores, axis=-1, keepdims=True)
    exponent = jnp.exp(scores - row_max)
    weights = (exponent / jnp.sum(exponent, axis=-1, keepdims=True)).astype(jnp.bfloat16)
    attended = jnp.einsum(
        "nqk,nkc->nqc", weights, values, preferred_element_type=jnp.float32
    ).astype(jnp.bfloat16)
    projected = (
        jnp.dot(attended.reshape(-1, channels), output_weight, preferred_element_type=jnp.float32)
        + output_bias
    ).astype(jnp.bfloat16)
    projected = projected.reshape(clip_count, frame_count, row_count, column_count, channels)
    residual_mine = lax.dynamic_slice_in_dim(residual, start, row_count, axis=2)
    live_mask = (jnp.arange(frame_count, dtype=jnp.int32)[None, :] < counts[:, None]).astype(
        jnp.float32
    )
    summed = residual_mine.astype(jnp.float32) + projected.astype(jnp.float32)
    return (summed * live_mask[:, :, None, None, None]).astype(jnp.bfloat16)


GATHER_LIMIT = 1 << 22


def chosen_body(segment_input, inner_input, *rest):
    gathered = inner_input.size * inner_input.dtype.itemsize * lax.axis_size("rows")
    if gathered <= GATHER_LIMIT:
        return gathered_body(segment_input, inner_input, *rest)
    return body(segment_input, inner_input, *rest)


def solution(mesh):
    placed = (
        P("clips", "tm", "rows", None, None),
        P("clips", "tm", "rows", None, None),
        P("clips", "tm"),
        P(),
        P(),
        P(),
        P(),
        P(),
        P(),
        P(),
        P(),
    )
    return jax.shard_map(
        chosen_body,
        mesh=mesh,
        in_specs=placed,
        out_specs=P("clips", "tm", "rows", None, None),
        check_vma=False,
    )
```

```python
import functools
import math

import jax
import jax.numpy as jnp
from jax import lax
from jax.sharding import PartitionSpec as P
from jax.experimental import pallas as pl
from jax.experimental.pallas import tpu as pltpu

EPSILON = 1e-06


def prefix(part, axis, combine, identity):
    place = lax.axis_index(axis)
    gathered = jax.tree.map(lambda a: lax.all_gather(a, axis), part)
    state = jax.tree.map(lambda a, e: jnp.zeros_like(a) + jnp.asarray(e, a.dtype), part, identity)

    def one(step, state):
        return combine(
            state, jax.tree.map(lambda a: lax.dynamic_index_in_dim(a, step, 0, False), gathered)
        )

    return lax.fori_loop(0, place, one, state)


def as_sent(x):

    def short(part):
        return part.astype(jnp.bfloat16) if part.dtype == jnp.float32 else part

    return jax.tree.map(short, x)


def with_halo(cells, sides, width):
    for axis, dim in sides:
        count = lax.axis_size(axis)
        ends = count - 1
        head = lax.slice_in_dim(cells, 0, width, axis=dim)
        tail = lax.slice_in_dim(cells, cells.shape[dim] - width, cells.shape[dim], axis=dim)
        cells = jnp.concatenate(
            [
                lax.ppermute(tail, axis, [(i, (i + 1) % count) for i in range(ends)]),
                cells,
                lax.ppermute(head, axis, [((i + 1) % count, i) for i in range(ends)]),
            ],
            axis=dim,
        )
    return cells


def normalize(field, gain):
    widened = field.astype(jnp.float32)
    return widened * lax.rsqrt(jnp.mean(widened * widened, axis=-1, keepdims=True) + EPSILON) * gain


def last_two(extended, counts):
    slot_total = extended.shape[1]
    chosen = []
    for position in range(2):
        target = counts + position
        picked = jnp.zeros_like(extended[:, 0])
        for slot_index in range(slot_total):
            matches = (target == slot_index)[:, None, None, None]
            picked = jnp.where(matches, extended[:, slot_index], picked)
        chosen.append(picked)
    return jnp.stack(chosen, axis=1)


def summarize(activated, counts):
    blanks = jnp.zeros((activated.shape[0], 2) + activated.shape[2:], activated.dtype)
    summary = last_two(jnp.concatenate([blanks, activated], axis=1), counts)
    return (summary, jnp.minimum(counts, 2).astype(jnp.bfloat16))


def join_later(earlier, later):
    early_frames, early_count = earlier
    late_frames, late_count = later
    complete = (late_count > 1.5)[:, None, None, None, None]
    single = (late_count > 0.5)[:, None, None, None, None]
    shifted = jnp.concatenate([early_frames[:, 1:], late_frames[:, 1:]], axis=1)
    frames = jnp.where(complete, late_frames, jnp.where(single, shifted, early_frames))
    total_count = jnp.minimum(early_count + late_count, 2.0).astype(early_count.dtype)
    return (frames, total_count)


def incoming_cache(summary, counts):
    starting = (jnp.zeros_like(summary), jnp.zeros_like(counts))
    combined = prefix((summary, counts), "tm", join_later, starting)
    return combined[0]


def convolve(padded, causal_weight, causal_bias):
    clip_count, slot_total, rows_padded, column_count, channels = padded.shape
    frame_count = slot_total - 2
    row_count = rows_padded - 2
    widened = jnp.pad(padded, ((0, 0), (0, 0), (0, 0), (1, 1), (0, 0)))
    summed = jnp.zeros((clip_count * frame_count * row_count * column_count, channels), jnp.float32)
    for delta_time in range(3):
        for delta_row in range(3):
            window = widened[
                :, delta_time : delta_time + frame_count, delta_row : delta_row + row_count
            ]
            columns = jnp.concatenate(
                [window[:, :, :, delta_col : delta_col + column_count] for delta_col in range(3)],
                axis=-1,
            )
            kernel = causal_weight[delta_time, delta_row].reshape(3 * channels, channels)
            summed = summed + jnp.dot(
                columns.reshape(-1, 3 * channels), kernel, preferred_element_type=jnp.float32
            )
    return summed.reshape(clip_count, frame_count, row_count, column_count, channels) + causal_bias


def attend(normed, triple_weight, triple_bias, output_weight, output_bias):
    frame_count, places, channels = normed.shape
    packed = (
        jnp.dot(normed.reshape(-1, channels), triple_weight, preferred_element_type=jnp.float32)
        + triple_bias
    )
    packed = packed.reshape(frame_count, places, 3 * channels)
    queries = packed[:, :, :channels]
    key_vectors = packed[:, :, channels : 2 * channels]
    values = packed[:, :, 2 * channels :].astype(jnp.bfloat16)
    scores = jnp.einsum(
        "nqc,nkc->nqk", queries, key_vectors, precision=lax.Precision.HIGHEST
    ) / math.sqrt(channels)
    row_max = jnp.max(scores, axis=-1, keepdims=True)
    exponent = jnp.exp(scores - row_max)
    weights = (exponent / jnp.sum(exponent, axis=-1, keepdims=True)).astype(jnp.bfloat16)
    attended = jnp.einsum(
        "nqk,nkc->nqc", weights, values, preferred_element_type=jnp.float32
    ).astype(jnp.bfloat16)
    projected = (
        jnp.dot(attended.reshape(-1, channels), output_weight, preferred_element_type=jnp.float32)
        + output_bias
    )
    return projected.reshape(frame_count, places, channels).astype(jnp.bfloat16)


def body(
    segment_input,
    inner_input,
    lengths,
    inner_gain,
    causal_weight,
    causal_bias,
    attention_gain,
    triple_weight,
    triple_bias,
    output_weight,
    output_bias,
):
    clip_count, frame_count, row_count, column_count, channels = segment_input.shape
    activated = jax.nn.silu(normalize(inner_input, inner_gain)).astype(jnp.bfloat16)
    counts = lengths[:, 0]
    live_mask = (jnp.arange(frame_count, dtype=jnp.int32)[None, :] < counts[:, None]).astype(
        jnp.float32
    )
    carried = incoming_cache(*summarize(activated, counts))
    extended = jnp.concatenate([carried, activated], axis=1)
    padded = with_halo(as_sent(extended), (("rows", 2),), 1).astype(extended.dtype)
    convolved = convolve(padded, causal_weight, causal_bias)
    residual = (segment_input.astype(jnp.float32) + convolved).astype(jnp.bfloat16)
    residual = lax.optimization_barrier(residual)
    normed = normalize(residual, attention_gain).astype(jnp.bfloat16)
    row_devices = lax.axis_size("rows")
    per_device = clip_count * frame_count // row_devices
    grouped = normed.reshape(row_devices, per_device, row_count, column_count, channels)
    portion = lax.all_to_all(grouped, "rows", split_axis=0, concat_axis=2, tiled=True)
    owned = portion.shape[1]
    height = portion.shape[2]
    flat = portion.reshape(owned, height * column_count, channels)
    result = attend(flat, triple_weight, triple_bias, output_weight, output_bias)
    result = result.reshape(1, owned, height, column_count, channels)
    projected = lax.all_to_all(result, "rows", split_axis=2, concat_axis=0, tiled=True)
    projected = projected.reshape(clip_count, frame_count, row_count, column_count, channels)
    projected = lax.optimization_barrier(projected)
    summed = residual.astype(jnp.float32) + projected.astype(jnp.float32)
    return (summed * live_mask[:, :, None, None, None]).astype(jnp.bfloat16)


def activate(field, gain):
    return jax.nn.silu(normalize(field, gain)).astype(jnp.bfloat16)


def conv_part_kernel(plan, x_ref, w_ref, o_ref, acc_ref):
    step = pl.program_id(0)
    clips, held, rows, columns, width = x_ref.shape
    height = rows - 2
    places = clips * height * columns

    @pl.when(step == 0)
    def _():
        acc_ref[...] = jnp.zeros_like(acc_ref)

    for index, pairs in enumerate(plan):

        @pl.when(step == index)
        def _():
            for frame, slot in pairs:
                for kh in range(3):
                    lhs = x_ref[:, frame, kh : kh + height, :, :].reshape(places, width)
                    weight = w_ref[kh].reshape(width, w_ref.shape[-1])
                    acc_ref[slot] += jnp.dot(lhs, weight, preferred_element_type=jnp.float32)

    @pl.when(step == len(plan) - 1)
    def _():
        o_ref[...] = acc_ref[...]


def conv_part(frames, causal_weight, plan, first_tap, slots):
    clips, held, height, columns, channels = frames.shape
    padded = jnp.pad(frames, ((0, 0), (0, 0), (1, 1), (1, 1), (0, 0)))
    taps = jnp.concatenate(
        [padded[:, :, :, kw : kw + columns] for kw in range(3)], axis=-1
    )
    places = clips * height * columns
    dots = sum(len(pairs) for pairs in plan) * 3
    return pl.pallas_call(
        functools.partial(conv_part_kernel, plan),
        grid=(len(plan),),
        in_specs=[
            pl.BlockSpec(taps.shape, lambda i: (0, 0, 0, 0, 0)),
            pl.BlockSpec(
                (None, 3, 3, channels, channels), lambda i: (first_tap + i, 0, 0, 0, 0)
            ),
        ],
        out_specs=pl.BlockSpec((slots, places, channels), lambda i: (0, 0, 0)),
        out_shape=jax.ShapeDtypeStruct((slots, places, channels), jnp.float32),
        scratch_shapes=[pltpu.VMEM((slots, places, channels), jnp.float32)],
        compiler_params=pltpu.CompilerParams(
            dimension_semantics=("arbitrary",),
            vmem_limit_bytes=48 * 1024 * 1024,
        ),
        cost_estimate=pl.CostEstimate(
            flops=2 * places * dots * 3 * channels * channels,
            transcendentals=0,
            bytes_accessed=len(plan) * 9 * channels * channels * 2
            + taps.size * 2
            + slots * places * channels * 4,
        ),
    )(taps, causal_weight)


def conv_plans(slots):
    own, carried = {}, {}
    for kt in range(3):
        for slot in range(slots):
            source = slot + kt
            if source >= 2:
                own.setdefault(kt, []).append((source - 2, slot))
            else:
                carried.setdefault(kt, []).append((source, slot))
    return own, carried


def plan_of(table):
    taps = sorted(table)
    assert taps == list(range(taps[0], taps[-1] + 1))
    return tuple(tuple(table[kt]) for kt in taps), taps[0]


def own_conv(own_frames, causal_weight):
    own_table, _ = conv_plans(own_frames.shape[1])
    own_plan, own_first = plan_of(own_table)
    return conv_part(own_frames, causal_weight, own_plan, own_first, own_frames.shape[1])


def carried_conv(carried_frames, causal_weight, slots):
    _, carried_table = conv_plans(slots)
    carried_plan, carried_first = plan_of(carried_table)
    return conv_part(carried_frames, causal_weight, carried_plan, carried_first, slots)


def frame_major(total, clips, height, columns):
    slots, places, channels = total.shape
    total = total.reshape(slots, clips, height, columns, channels)
    return jnp.transpose(total, (1, 0, 2, 3, 4))


def gathered_body(
    segment_input,
    inner_input,
    lengths,
    inner_gain,
    causal_weight,
    causal_bias,
    attention_gain,
    triple_weight,
    triple_bias,
    output_weight,
    output_bias,
):
    clip_count, frame_count, row_count, column_count, channels = segment_input.shape
    sections = lax.axis_size("tm")
    counts = lengths[:, 0]
    ahead = [(i, i + 1) for i in range(sections - 1)]
    prev_counts = lax.ppermute(counts, "tm", ahead)
    both = jnp.concatenate([inner_input, segment_input], axis=0)
    both_all = lax.all_gather(both, "rows", axis=2, tiled=True)
    inner_all = both_all[:clip_count]
    segment_all = both_all[clip_count:]
    wide = (counts > 1)[:, None, None, None]
    last_raw = jnp.where(wide, inner_all[:, frame_count - 1], inner_all[:, 0])
    prev_raw = lax.ppermute(inner_all, "tm", ahead)
    before_raw = lax.ppermute(last_raw, "tm", [(i, i + 2) for i in range(sections - 2)])
    own = activate(inner_all, inner_gain)
    own_sum = own_conv(own, causal_weight)
    own_sum, prev_raw, before_raw, prev_counts = lax.optimization_barrier(
        (own_sum, prev_raw, before_raw, prev_counts)
    )
    prev = activate(prev_raw, inner_gain)
    before = activate(before_raw, inner_gain)
    prev_wide = (prev_counts > 1)[:, None, None, None]
    carried = jnp.stack(
        [
            jnp.where(prev_wide, prev[:, frame_count - 2], before),
            jnp.where(prev_wide, prev[:, frame_count - 1], prev[:, 0]),
        ],
        axis=1,
    )
    carried_sum = carried_conv(carried, causal_weight, frame_count)
    height = inner_all.shape[2]
    convolved = frame_major(own_sum + carried_sum, clip_count, height, column_count) + causal_bias
    residual = (segment_all.astype(jnp.float32) + convolved).astype(jnp.bfloat16)
    normed = normalize(residual, attention_gain).astype(jnp.bfloat16)
    height = normed.shape[2]
    frames = clip_count * frame_count
    places = height * column_count
    flat = normed.reshape(frames * places, channels)
    packed = (
        jnp.dot(flat, triple_weight[:, channels:], preferred_element_type=jnp.float32)
        + triple_bias[channels:]
    ).reshape(frames, places, 2 * channels)
    key_vectors = packed[:, :, :channels]
    values = packed[:, :, channels:].astype(jnp.bfloat16)
    start = lax.axis_index("rows") * row_count
    mine = lax.dynamic_slice_in_dim(normed, start, row_count, axis=2)
    queries = (
        jnp.dot(
            mine.reshape(-1, channels), triple_weight[:, :channels],
            preferred_element_type=jnp.float32,
        )
        + triple_bias[:channels]
    ).reshape(frames, row_count * column_count, channels)
    scores = jnp.einsum(
        "nqc,nkc->nqk", queries, key_vectors, precision=lax.Precision.HIGHEST
    ) / math.sqrt(channels)
    row_max = jnp.max(scores, axis=-1, keepdims=True)
    exponent = jnp.exp(scores - row_max)
    weights = (exponent / jnp.sum(exponent, axis=-1, keepdims=True)).astype(jnp.bfloat16)
    attended = jnp.einsum(
        "nqk,nkc->nqc", weights, values, preferred_element_type=jnp.float32
    ).astype(jnp.bfloat16)
    projected = (
        jnp.dot(attended.reshape(-1, channels), output_weight, preferred_element_type=jnp.float32)
        + output_bias
    ).astype(jnp.bfloat16)
    projected = projected.reshape(clip_count, frame_count, row_count, column_count, channels)
    residual_mine = lax.dynamic_slice_in_dim(residual, start, row_count, axis=2)
    live_mask = (jnp.arange(frame_count, dtype=jnp.int32)[None, :] < counts[:, None]).astype(
        jnp.float32
    )
    summed = residual_mine.astype(jnp.float32) + projected.astype(jnp.float32)
    return (summed * live_mask[:, :, None, None, None]).astype(jnp.bfloat16)


GATHER_LIMIT = 1 << 22


def chosen_body(segment_input, inner_input, *rest):
    gathered = inner_input.size * inner_input.dtype.itemsize * lax.axis_size("rows")
    if gathered <= GATHER_LIMIT:
        return gathered_body(segment_input, inner_input, *rest)
    return body(segment_input, inner_input, *rest)


def solution(mesh):
    placed = (
        P("clips", "tm", "rows", None, None),
        P("clips", "tm", "rows", None, None),
        P("clips", "tm"),
        P(),
        P(),
        P(),
        P(),
        P(),
        P(),
        P(),
        P(),
    )
    return jax.shard_map(
        chosen_body,
        mesh=mesh,
        in_specs=placed,
        out_specs=P("clips", "tm", "rows", None, None),
        check_vma=False,
    )
```

```python
import functools
import math

import jax
import jax.numpy as jnp
from jax import lax
from jax.sharding import PartitionSpec as P
from jax.experimental import pallas as pl
from jax.experimental.pallas import tpu as pltpu

EPSILON = 1e-06


def prefix(part, axis, combine, identity):
    place = lax.axis_index(axis)
    gathered = jax.tree.map(lambda a: lax.all_gather(a, axis), part)
    state = jax.tree.map(lambda a, e: jnp.zeros_like(a) + jnp.asarray(e, a.dtype), part, identity)

    def one(step, state):
        return combine(
            state, jax.tree.map(lambda a: lax.dynamic_index_in_dim(a, step, 0, False), gathered)
        )

    return lax.fori_loop(0, place, one, state)


def as_sent(x):

    def short(part):
        return part.astype(jnp.bfloat16) if part.dtype == jnp.float32 else part

    return jax.tree.map(short, x)


def with_halo(cells, sides, width):
    for axis, dim in sides:
        count = lax.axis_size(axis)
        ends = count - 1
        head = lax.slice_in_dim(cells, 0, width, axis=dim)
        tail = lax.slice_in_dim(cells, cells.shape[dim] - width, cells.shape[dim], axis=dim)
        cells = jnp.concatenate(
            [
                lax.ppermute(tail, axis, [(i, (i + 1) % count) for i in range(ends)]),
                cells,
                lax.ppermute(head, axis, [((i + 1) % count, i) for i in range(ends)]),
            ],
            axis=dim,
        )
    return cells


def normalize(field, gain):
    widened = field.astype(jnp.float32)
    return widened * lax.rsqrt(jnp.mean(widened * widened, axis=-1, keepdims=True) + EPSILON) * gain


def last_two(extended, counts):
    slot_total = extended.shape[1]
    chosen = []
    for position in range(2):
        target = counts + position
        picked = jnp.zeros_like(extended[:, 0])
        for slot_index in range(slot_total):
            matches = (target == slot_index)[:, None, None, None]
            picked = jnp.where(matches, extended[:, slot_index], picked)
        chosen.append(picked)
    return jnp.stack(chosen, axis=1)


def summarize(activated, counts):
    blanks = jnp.zeros((activated.shape[0], 2) + activated.shape[2:], activated.dtype)
    summary = last_two(jnp.concatenate([blanks, activated], axis=1), counts)
    return (summary, jnp.minimum(counts, 2).astype(jnp.bfloat16))


def join_later(earlier, later):
    early_frames, early_count = earlier
    late_frames, late_count = later
    complete = (late_count > 1.5)[:, None, None, None, None]
    single = (late_count > 0.5)[:, None, None, None, None]
    shifted = jnp.concatenate([early_frames[:, 1:], late_frames[:, 1:]], axis=1)
    frames = jnp.where(complete, late_frames, jnp.where(single, shifted, early_frames))
    total_count = jnp.minimum(early_count + late_count, 2.0).astype(early_count.dtype)
    return (frames, total_count)


def incoming_cache(summary, counts):
    starting = (jnp.zeros_like(summary), jnp.zeros_like(counts))
    combined = prefix((summary, counts), "tm", join_later, starting)
    return combined[0]


def convolve(padded, causal_weight, causal_bias):
    clip_count, slot_total, rows_padded, column_count, channels = padded.shape
    frame_count = slot_total - 2
    row_count = rows_padded - 2
    widened = jnp.pad(padded, ((0, 0), (0, 0), (0, 0), (1, 1), (0, 0)))
    summed = jnp.zeros((clip_count * frame_count * row_count * column_count, channels), jnp.float32)
    for delta_time in range(3):
        for delta_row in range(3):
            window = widened[
                :, delta_time : delta_time + frame_count, delta_row : delta_row + row_count
            ]
            columns = jnp.concatenate(
                [window[:, :, :, delta_col : delta_col + column_count] for delta_col in range(3)],
                axis=-1,
            )
            kernel = causal_weight[delta_time, delta_row].reshape(3 * channels, channels)
            summed = summed + jnp.dot(
                columns.reshape(-1, 3 * channels), kernel, preferred_element_type=jnp.float32
            )
    return summed.reshape(clip_count, frame_count, row_count, column_count, channels) + causal_bias


def attend(normed, triple_weight, triple_bias, output_weight, output_bias):
    frame_count, places, channels = normed.shape
    packed = (
        jnp.dot(normed.reshape(-1, channels), triple_weight, preferred_element_type=jnp.float32)
        + triple_bias
    )
    packed = packed.reshape(frame_count, places, 3 * channels)
    queries = packed[:, :, :channels]
    key_vectors = packed[:, :, channels : 2 * channels]
    values = packed[:, :, 2 * channels :].astype(jnp.bfloat16)
    scores = jnp.einsum(
        "nqc,nkc->nqk", queries, key_vectors, precision=lax.Precision.HIGHEST
    ) / math.sqrt(channels)
    row_max = jnp.max(scores, axis=-1, keepdims=True)
    exponent = jnp.exp(scores - row_max)
    weights = (exponent / jnp.sum(exponent, axis=-1, keepdims=True)).astype(jnp.bfloat16)
    attended = jnp.einsum(
        "nqk,nkc->nqc", weights, values, preferred_element_type=jnp.float32
    ).astype(jnp.bfloat16)
    projected = (
        jnp.dot(attended.reshape(-1, channels), output_weight, preferred_element_type=jnp.float32)
        + output_bias
    )
    return projected.reshape(frame_count, places, channels).astype(jnp.bfloat16)


def body(
    segment_input,
    inner_input,
    lengths,
    inner_gain,
    causal_weight,
    causal_bias,
    attention_gain,
    triple_weight,
    triple_bias,
    output_weight,
    output_bias,
):
    clip_count, frame_count, row_count, column_count, channels = segment_input.shape
    activated = jax.nn.silu(normalize(inner_input, inner_gain)).astype(jnp.bfloat16)
    counts = lengths[:, 0]
    live_mask = (jnp.arange(frame_count, dtype=jnp.int32)[None, :] < counts[:, None]).astype(
        jnp.float32
    )
    carried = incoming_cache(*summarize(activated, counts))
    extended = jnp.concatenate([carried, activated], axis=1)
    padded = with_halo(as_sent(extended), (("rows", 2),), 1).astype(extended.dtype)
    convolved = convolve(padded, causal_weight, causal_bias)
    residual = (segment_input.astype(jnp.float32) + convolved).astype(jnp.bfloat16)
    residual = lax.optimization_barrier(residual)
    normed = normalize(residual, attention_gain).astype(jnp.bfloat16)
    row_devices = lax.axis_size("rows")
    per_device = clip_count * frame_count // row_devices
    grouped = normed.reshape(row_devices, per_device, row_count, column_count, channels)
    portion = lax.all_to_all(grouped, "rows", split_axis=0, concat_axis=2, tiled=True)
    owned = portion.shape[1]
    height = portion.shape[2]
    flat = portion.reshape(owned, height * column_count, channels)
    result = attend(flat, triple_weight, triple_bias, output_weight, output_bias)
    result = result.reshape(1, owned, height, column_count, channels)
    projected = lax.all_to_all(result, "rows", split_axis=2, concat_axis=0, tiled=True)
    projected = projected.reshape(clip_count, frame_count, row_count, column_count, channels)
    projected = lax.optimization_barrier(projected)
    summed = residual.astype(jnp.float32) + projected.astype(jnp.float32)
    return (summed * live_mask[:, :, None, None, None]).astype(jnp.bfloat16)


def activate(field, gain):
    return jax.nn.silu(normalize(field, gain)).astype(jnp.bfloat16)


def conv_part_kernel(plan, first_tap, x_ref, w_hbm, o_ref, w_vmem, sems):
    clips, held, rows, columns, width = x_ref.shape
    height = rows - 2
    places = clips * height * columns
    channels = w_vmem.shape[-1]
    copies = []
    for index in range(len(plan)):
        for kh in range(3):
            slot_index = index * 3 + kh
            copy = pltpu.make_async_copy(
                w_hbm.at[first_tap + index, kh], w_vmem.at[slot_index], sems.at[slot_index]
            )
            copy.start()
            copies.append(copy)
    totals = [None] * o_ref.shape[0]
    for index, pairs in enumerate(plan):
        for kh in range(3):
            slot_index = index * 3 + kh
            copies[slot_index].wait()
            weight = w_vmem[slot_index].reshape(width, channels)
            for frame, slot in pairs:
                lhs = x_ref[:, frame, kh : kh + height, :, :].reshape(places, width)
                term = jnp.dot(lhs, weight, preferred_element_type=jnp.float32)
                totals[slot] = term if totals[slot] is None else totals[slot] + term
    for slot, total in enumerate(totals):
        o_ref[slot] = total


def conv_part(frames, causal_weight, plan, first_tap, slots):
    clips, held, height, columns, channels = frames.shape
    padded = jnp.pad(frames, ((0, 0), (0, 0), (1, 1), (1, 1), (0, 0)))
    taps = jnp.concatenate(
        [padded[:, :, :, kw : kw + columns] for kw in range(3)], axis=-1
    )
    places = clips * height * columns
    dots = sum(len(pairs) for pairs in plan) * 3
    blocks = len(plan) * 3
    return pl.pallas_call(
        functools.partial(conv_part_kernel, plan, first_tap),
        in_specs=[
            pl.BlockSpec(memory_space=pltpu.VMEM),
            pl.BlockSpec(memory_space=pl.ANY),
        ],
        out_specs=pl.BlockSpec(memory_space=pltpu.VMEM),
        out_shape=jax.ShapeDtypeStruct((slots, places, channels), jnp.float32),
        scratch_shapes=[
            pltpu.VMEM((blocks, 3, channels, channels), causal_weight.dtype),
            pltpu.SemaphoreType.DMA((blocks,)),
        ],
        compiler_params=pltpu.CompilerParams(vmem_limit_bytes=48 * 1024 * 1024),
        cost_estimate=pl.CostEstimate(
            flops=2 * places * dots * 3 * channels * channels,
            transcendentals=0,
            bytes_accessed=blocks * 3 * channels * channels * 2
            + taps.size * 2
            + slots * places * channels * 4,
        ),
    )(taps, causal_weight)


def conv_plans(slots):
    own, carried = {}, {}
    for kt in range(3):
        for slot in range(slots):
            source = slot + kt
            if source >= 2:
                own.setdefault(kt, []).append((source - 2, slot))
            else:
                carried.setdefault(kt, []).append((source, slot))
    return own, carried


def plan_of(table):
    taps = sorted(table)
    assert taps == list(range(taps[0], taps[-1] + 1))
    return tuple(tuple(table[kt]) for kt in taps), taps[0]


def own_conv(own_frames, causal_weight):
    own_table, _ = conv_plans(own_frames.shape[1])
    own_plan, own_first = plan_of(own_table)
    return conv_part(own_frames, causal_weight, own_plan, own_first, own_frames.shape[1])


def carried_conv(carried_frames, causal_weight, slots):
    _, carried_table = conv_plans(slots)
    carried_plan, carried_first = plan_of(carried_table)
    return conv_part(carried_frames, causal_weight, carried_plan, carried_first, slots)


def frame_major(total, clips, height, columns):
    slots, places, channels = total.shape
    total = total.reshape(slots, clips, height, columns, channels)
    return jnp.transpose(total, (1, 0, 2, 3, 4))


def gathered_body(
    segment_input,
    inner_input,
    lengths,
    inner_gain,
    causal_weight,
    causal_bias,
    attention_gain,
    triple_weight,
    triple_bias,
    output_weight,
    output_bias,
):
    clip_count, frame_count, row_count, column_count, channels = segment_input.shape
    sections = lax.axis_size("tm")
    counts = lengths[:, 0]
    ahead = [(i, i + 1) for i in range(sections - 1)]
    prev_counts = lax.ppermute(counts, "tm", ahead)
    both = jnp.concatenate([inner_input, segment_input], axis=0)
    both_all = lax.all_gather(both, "rows", axis=2, tiled=True)
    inner_all = both_all[:clip_count]
    segment_all = both_all[clip_count:]
    wide = (counts > 1)[:, None, None, None]
    last_raw = jnp.where(wide, inner_all[:, frame_count - 1], inner_all[:, 0])
    prev_raw = lax.ppermute(inner_all, "tm", ahead)
    before_raw = lax.ppermute(last_raw, "tm", [(i, i + 2) for i in range(sections - 2)])
    own = activate(inner_all, inner_gain)
    own_sum = own_conv(own, causal_weight)
    own_sum, prev_raw, before_raw, prev_counts = lax.optimization_barrier(
        (own_sum, prev_raw, before_raw, prev_counts)
    )
    prev = activate(prev_raw, inner_gain)
    before = activate(before_raw, inner_gain)
    prev_wide = (prev_counts > 1)[:, None, None, None]
    carried = jnp.stack(
        [
            jnp.where(prev_wide, prev[:, frame_count - 2], before),
            jnp.where(prev_wide, prev[:, frame_count - 1], prev[:, 0]),
        ],
        axis=1,
    )
    carried_sum = carried_conv(carried, causal_weight, frame_count)
    height = inner_all.shape[2]
    convolved = frame_major(own_sum + carried_sum, clip_count, height, column_count) + causal_bias
    residual = (segment_all.astype(jnp.float32) + convolved).astype(jnp.bfloat16)
    normed = normalize(residual, attention_gain).astype(jnp.bfloat16)
    height = normed.shape[2]
    frames = clip_count * frame_count
    places = height * column_count
    flat = normed.reshape(frames * places, channels)
    packed = (
        jnp.dot(flat, triple_weight[:, channels:], preferred_element_type=jnp.float32)
        + triple_bias[channels:]
    ).reshape(frames, places, 2 * channels)
    key_vectors = packed[:, :, :channels]
    values = packed[:, :, channels:].astype(jnp.bfloat16)
    start = lax.axis_index("rows") * row_count
    mine = lax.dynamic_slice_in_dim(normed, start, row_count, axis=2)
    queries = (
        jnp.dot(
            mine.reshape(-1, channels), triple_weight[:, :channels],
            preferred_element_type=jnp.float32,
        )
        + triple_bias[:channels]
    ).reshape(frames, row_count * column_count, channels)
    scores = jnp.einsum(
        "nqc,nkc->nqk", queries, key_vectors, precision=lax.Precision.HIGHEST
    ) / math.sqrt(channels)
    row_max = jnp.max(scores, axis=-1, keepdims=True)
    exponent = jnp.exp(scores - row_max)
    weights = (exponent / jnp.sum(exponent, axis=-1, keepdims=True)).astype(jnp.bfloat16)
    attended = jnp.einsum(
        "nqk,nkc->nqc", weights, values, preferred_element_type=jnp.float32
    ).astype(jnp.bfloat16)
    projected = (
        jnp.dot(attended.reshape(-1, channels), output_weight, preferred_element_type=jnp.float32)
        + output_bias
    ).astype(jnp.bfloat16)
    projected = projected.reshape(clip_count, frame_count, row_count, column_count, channels)
    residual_mine = lax.dynamic_slice_in_dim(residual, start, row_count, axis=2)
    live_mask = (jnp.arange(frame_count, dtype=jnp.int32)[None, :] < counts[:, None]).astype(
        jnp.float32
    )
    summed = residual_mine.astype(jnp.float32) + projected.astype(jnp.float32)
    return (summed * live_mask[:, :, None, None, None]).astype(jnp.bfloat16)


GATHER_LIMIT = 1 << 22


def chosen_body(segment_input, inner_input, *rest):
    gathered = inner_input.size * inner_input.dtype.itemsize * lax.axis_size("rows")
    if gathered <= GATHER_LIMIT:
        return gathered_body(segment_input, inner_input, *rest)
    return body(segment_input, inner_input, *rest)


def solution(mesh):
    placed = (
        P("clips", "tm", "rows", None, None),
        P("clips", "tm", "rows", None, None),
        P("clips", "tm"),
        P(),
        P(),
        P(),
        P(),
        P(),
        P(),
        P(),
        P(),
    )
    return jax.shard_map(
        chosen_body,
        mesh=mesh,
        in_specs=placed,
        out_specs=P("clips", "tm", "rows", None, None),
        check_vma=False,
    )
```

```python
import functools
import math

import jax
import jax.numpy as jnp
from jax import lax
from jax.sharding import PartitionSpec as P
from jax.experimental import pallas as pl
from jax.experimental.pallas import tpu as pltpu

EPSILON = 1e-06


def prefix(part, axis, combine, identity):
    place = lax.axis_index(axis)
    gathered = jax.tree.map(lambda a: lax.all_gather(a, axis), part)
    state = jax.tree.map(lambda a, e: jnp.zeros_like(a) + jnp.asarray(e, a.dtype), part, identity)

    def one(step, state):
        return combine(
            state, jax.tree.map(lambda a: lax.dynamic_index_in_dim(a, step, 0, False), gathered)
        )

    return lax.fori_loop(0, place, one, state)


def as_sent(x):

    def short(part):
        return part.astype(jnp.bfloat16) if part.dtype == jnp.float32 else part

    return jax.tree.map(short, x)


def with_halo(cells, sides, width):
    for axis, dim in sides:
        count = lax.axis_size(axis)
        ends = count - 1
        head = lax.slice_in_dim(cells, 0, width, axis=dim)
        tail = lax.slice_in_dim(cells, cells.shape[dim] - width, cells.shape[dim], axis=dim)
        cells = jnp.concatenate(
            [
                lax.ppermute(tail, axis, [(i, (i + 1) % count) for i in range(ends)]),
                cells,
                lax.ppermute(head, axis, [((i + 1) % count, i) for i in range(ends)]),
            ],
            axis=dim,
        )
    return cells


def normalize(field, gain):
    widened = field.astype(jnp.float32)
    return widened * lax.rsqrt(jnp.mean(widened * widened, axis=-1, keepdims=True) + EPSILON) * gain


def last_two(extended, counts):
    slot_total = extended.shape[1]
    chosen = []
    for position in range(2):
        target = counts + position
        picked = jnp.zeros_like(extended[:, 0])
        for slot_index in range(slot_total):
            matches = (target == slot_index)[:, None, None, None]
            picked = jnp.where(matches, extended[:, slot_index], picked)
        chosen.append(picked)
    return jnp.stack(chosen, axis=1)


def summarize(activated, counts):
    blanks = jnp.zeros((activated.shape[0], 2) + activated.shape[2:], activated.dtype)
    summary = last_two(jnp.concatenate([blanks, activated], axis=1), counts)
    return (summary, jnp.minimum(counts, 2).astype(jnp.bfloat16))


def join_later(earlier, later):
    early_frames, early_count = earlier
    late_frames, late_count = later
    complete = (late_count > 1.5)[:, None, None, None, None]
    single = (late_count > 0.5)[:, None, None, None, None]
    shifted = jnp.concatenate([early_frames[:, 1:], late_frames[:, 1:]], axis=1)
    frames = jnp.where(complete, late_frames, jnp.where(single, shifted, early_frames))
    total_count = jnp.minimum(early_count + late_count, 2.0).astype(early_count.dtype)
    return (frames, total_count)


def incoming_cache(summary, counts):
    starting = (jnp.zeros_like(summary), jnp.zeros_like(counts))
    combined = prefix((summary, counts), "tm", join_later, starting)
    return combined[0]


def convolve(padded, causal_weight, causal_bias):
    clip_count, slot_total, rows_padded, column_count, channels = padded.shape
    frame_count = slot_total - 2
    row_count = rows_padded - 2
    widened = jnp.pad(padded, ((0, 0), (0, 0), (0, 0), (1, 1), (0, 0)))
    summed = jnp.zeros((clip_count * frame_count * row_count * column_count, channels), jnp.float32)
    for delta_time in range(3):
        for delta_row in range(3):
            window = widened[
                :, delta_time : delta_time + frame_count, delta_row : delta_row + row_count
            ]
            columns = jnp.concatenate(
                [window[:, :, :, delta_col : delta_col + column_count] for delta_col in range(3)],
                axis=-1,
            )
            kernel = causal_weight[delta_time, delta_row].reshape(3 * channels, channels)
            summed = summed + jnp.dot(
                columns.reshape(-1, 3 * channels), kernel, preferred_element_type=jnp.float32
            )
    return summed.reshape(clip_count, frame_count, row_count, column_count, channels) + causal_bias


def attend(normed, triple_weight, triple_bias, output_weight, output_bias):
    frame_count, places, channels = normed.shape
    packed = (
        jnp.dot(normed.reshape(-1, channels), triple_weight, preferred_element_type=jnp.float32)
        + triple_bias
    )
    packed = packed.reshape(frame_count, places, 3 * channels)
    queries = packed[:, :, :channels]
    key_vectors = packed[:, :, channels : 2 * channels]
    values = packed[:, :, 2 * channels :].astype(jnp.bfloat16)
    scores = jnp.einsum(
        "nqc,nkc->nqk", queries, key_vectors, precision=lax.Precision.HIGHEST
    ) / math.sqrt(channels)
    row_max = jnp.max(scores, axis=-1, keepdims=True)
    exponent = jnp.exp(scores - row_max)
    weights = (exponent / jnp.sum(exponent, axis=-1, keepdims=True)).astype(jnp.bfloat16)
    attended = jnp.einsum(
        "nqk,nkc->nqc", weights, values, preferred_element_type=jnp.float32
    ).astype(jnp.bfloat16)
    projected = (
        jnp.dot(attended.reshape(-1, channels), output_weight, preferred_element_type=jnp.float32)
        + output_bias
    )
    return projected.reshape(frame_count, places, channels).astype(jnp.bfloat16)


def body(
    segment_input,
    inner_input,
    lengths,
    inner_gain,
    causal_weight,
    causal_bias,
    attention_gain,
    triple_weight,
    triple_bias,
    output_weight,
    output_bias,
):
    clip_count, frame_count, row_count, column_count, channels = segment_input.shape
    activated = jax.nn.silu(normalize(inner_input, inner_gain)).astype(jnp.bfloat16)
    counts = lengths[:, 0]
    live_mask = (jnp.arange(frame_count, dtype=jnp.int32)[None, :] < counts[:, None]).astype(
        jnp.float32
    )
    carried = incoming_cache(*summarize(activated, counts))
    extended = jnp.concatenate([carried, activated], axis=1)
    padded = with_halo(as_sent(extended), (("rows", 2),), 1).astype(extended.dtype)
    convolved = convolve(padded, causal_weight, causal_bias)
    residual = (segment_input.astype(jnp.float32) + convolved).astype(jnp.bfloat16)
    residual = lax.optimization_barrier(residual)
    normed = normalize(residual, attention_gain).astype(jnp.bfloat16)
    row_devices = lax.axis_size("rows")
    per_device = clip_count * frame_count // row_devices
    grouped = normed.reshape(row_devices, per_device, row_count, column_count, channels)
    portion = lax.all_to_all(grouped, "rows", split_axis=0, concat_axis=2, tiled=True)
    owned = portion.shape[1]
    height = portion.shape[2]
    flat = portion.reshape(owned, height * column_count, channels)
    result = attend(flat, triple_weight, triple_bias, output_weight, output_bias)
    result = result.reshape(1, owned, height, column_count, channels)
    projected = lax.all_to_all(result, "rows", split_axis=2, concat_axis=0, tiled=True)
    projected = projected.reshape(clip_count, frame_count, row_count, column_count, channels)
    projected = lax.optimization_barrier(projected)
    summed = residual.astype(jnp.float32) + projected.astype(jnp.float32)
    return (summed * live_mask[:, :, None, None, None]).astype(jnp.bfloat16)


def activate(field, gain):
    return jax.nn.silu(normalize(field, gain)).astype(jnp.bfloat16)


def conv_part_kernel(plan, first_tap, x_ref, w_hbm, o_ref, w_vmem, sems):
    clips, held, rows, columns, width = x_ref.shape
    height = rows - 2
    places = height * columns
    channels = w_vmem.shape[-1]
    copies = []
    for index in range(len(plan)):
        for kh in range(3):
            slot_index = index * 3 + kh
            copy = pltpu.make_async_copy(
                w_hbm.at[first_tap + index, kh], w_vmem.at[slot_index], sems.at[slot_index]
            )
            copy.start()
            copies.append(copy)
    written = set()
    for index, (frame, slot, count) in enumerate(plan):
        for kh in range(3):
            slot_index = index * 3 + kh
            copies[slot_index].wait()
            weight = w_vmem[slot_index].reshape(width, channels)
            lhs = x_ref[:, frame : frame + count, kh : kh + height, :, :]
            lhs = lhs.reshape(clips * count * places, width)
            term = jnp.dot(lhs, weight, preferred_element_type=jnp.float32)
            term = term.reshape(clips, count, places, channels)
            for part in range(count):
                target = slot + part
                if target in written:
                    o_ref[:, target] += term[:, part]
                else:
                    o_ref[:, target] = term[:, part]
                    written.add(target)


def conv_part(frames, causal_weight, plan, first_tap, slots):
    clips, held, height, columns, channels = frames.shape
    padded = jnp.pad(frames, ((0, 0), (0, 0), (1, 1), (1, 1), (0, 0)))
    taps = jnp.concatenate(
        [padded[:, :, :, kw : kw + columns] for kw in range(3)], axis=-1
    )
    places = height * columns
    dots = sum(count for _, _, count in plan) * 3
    blocks = len(plan) * 3
    return pl.pallas_call(
        functools.partial(conv_part_kernel, plan, first_tap),
        in_specs=[
            pl.BlockSpec(memory_space=pltpu.VMEM),
            pl.BlockSpec(memory_space=pl.ANY),
        ],
        out_specs=pl.BlockSpec(memory_space=pltpu.VMEM),
        out_shape=jax.ShapeDtypeStruct((clips, slots, places, channels), jnp.float32),
        scratch_shapes=[
            pltpu.VMEM((blocks, 3, channels, channels), causal_weight.dtype),
            pltpu.SemaphoreType.DMA((blocks,)),
        ],
        compiler_params=pltpu.CompilerParams(vmem_limit_bytes=48 * 1024 * 1024),
        cost_estimate=pl.CostEstimate(
            flops=2 * clips * places * dots * 3 * channels * channels,
            transcendentals=0,
            bytes_accessed=blocks * 3 * channels * channels * 2
            + taps.size * 2
            + clips * slots * places * channels * 4,
        ),
    )(taps, causal_weight)


def conv_plans(slots):
    own, carried = {}, {}
    for kt in range(3):
        for slot in range(slots):
            source = slot + kt
            if source >= 2:
                own.setdefault(kt, []).append((source - 2, slot))
            else:
                carried.setdefault(kt, []).append((source, slot))
    return own, carried


def plan_of(table):
    taps = sorted(table)
    assert taps == list(range(taps[0], taps[-1] + 1))
    runs = []
    for kt in taps:
        pairs = sorted(table[kt], key=lambda pair: pair[1])
        frame, slot = pairs[0]
        assert pairs == [(frame + k, slot + k) for k in range(len(pairs))]
        runs.append((frame, slot, len(pairs)))
    return tuple(runs), taps[0]


def own_conv(own_frames, causal_weight):
    own_table, _ = conv_plans(own_frames.shape[1])
    own_plan, own_first = plan_of(own_table)
    return conv_part(own_frames, causal_weight, own_plan, own_first, own_frames.shape[1])


def carried_conv(carried_frames, causal_weight, slots):
    _, carried_table = conv_plans(slots)
    carried_plan, carried_first = plan_of(carried_table)
    return conv_part(carried_frames, causal_weight, carried_plan, carried_first, slots)


def frame_major(total, clips, height, columns):
    clips, slots, places, channels = total.shape
    return total.reshape(clips, slots, height, columns, channels)


def gathered_body(
    segment_input,
    inner_input,
    lengths,
    inner_gain,
    causal_weight,
    causal_bias,
    attention_gain,
    triple_weight,
    triple_bias,
    output_weight,
    output_bias,
):
    clip_count, frame_count, row_count, column_count, channels = segment_input.shape
    sections = lax.axis_size("tm")
    counts = lengths[:, 0]
    ahead = [(i, i + 1) for i in range(sections - 1)]
    prev_counts = lax.ppermute(counts, "tm", ahead)
    both = jnp.concatenate([inner_input, segment_input], axis=0)
    both_all = lax.all_gather(both, "rows", axis=2, tiled=True)
    inner_all = both_all[:clip_count]
    segment_all = both_all[clip_count:]
    wide = (counts > 1)[:, None, None, None]
    last_raw = jnp.where(wide, inner_all[:, frame_count - 1], inner_all[:, 0])
    prev_raw = lax.ppermute(inner_all, "tm", ahead)
    before_raw = lax.ppermute(last_raw, "tm", [(i, i + 2) for i in range(sections - 2)])
    own = activate(inner_all, inner_gain)
    own_sum = own_conv(own, causal_weight)
    own_sum, prev_raw, before_raw, prev_counts = lax.optimization_barrier(
        (own_sum, prev_raw, before_raw, prev_counts)
    )
    prev = activate(prev_raw, inner_gain)
    before = activate(before_raw, inner_gain)
    prev_wide = (prev_counts > 1)[:, None, None, None]
    carried = jnp.stack(
        [
            jnp.where(prev_wide, prev[:, frame_count - 2], before),
            jnp.where(prev_wide, prev[:, frame_count - 1], prev[:, 0]),
        ],
        axis=1,
    )
    carried_sum = carried_conv(carried, causal_weight, frame_count)
    height = inner_all.shape[2]
    convolved = frame_major(own_sum + carried_sum, clip_count, height, column_count) + causal_bias
    residual = (segment_all.astype(jnp.float32) + convolved).astype(jnp.bfloat16)
    normed = normalize(residual, attention_gain).astype(jnp.bfloat16)
    height = normed.shape[2]
    frames = clip_count * frame_count
    places = height * column_count
    flat = normed.reshape(frames * places, channels)
    packed = (
        jnp.dot(flat, triple_weight[:, channels:], preferred_element_type=jnp.float32)
        + triple_bias[channels:]
    ).reshape(frames, places, 2 * channels)
    key_vectors = packed[:, :, :channels]
    values = packed[:, :, channels:].astype(jnp.bfloat16)
    start = lax.axis_index("rows") * row_count
    mine = lax.dynamic_slice_in_dim(normed, start, row_count, axis=2)
    queries = (
        jnp.dot(
            mine.reshape(-1, channels), triple_weight[:, :channels],
            preferred_element_type=jnp.float32,
        )
        + triple_bias[:channels]
    ).reshape(frames, row_count * column_count, channels)
    scores = jnp.einsum(
        "nqc,nkc->nqk", queries, key_vectors, precision=lax.Precision.HIGHEST
    ) / math.sqrt(channels)
    row_max = jnp.max(scores, axis=-1, keepdims=True)
    exponent = jnp.exp(scores - row_max)
    weights = (exponent / jnp.sum(exponent, axis=-1, keepdims=True)).astype(jnp.bfloat16)
    attended = jnp.einsum(
        "nqk,nkc->nqc", weights, values, preferred_element_type=jnp.float32
    ).astype(jnp.bfloat16)
    projected = (
        jnp.dot(attended.reshape(-1, channels), output_weight, preferred_element_type=jnp.float32)
        + output_bias
    ).astype(jnp.bfloat16)
    projected = projected.reshape(clip_count, frame_count, row_count, column_count, channels)
    residual_mine = lax.dynamic_slice_in_dim(residual, start, row_count, axis=2)
    live_mask = (jnp.arange(frame_count, dtype=jnp.int32)[None, :] < counts[:, None]).astype(
        jnp.float32
    )
    summed = residual_mine.astype(jnp.float32) + projected.astype(jnp.float32)
    return (summed * live_mask[:, :, None, None, None]).astype(jnp.bfloat16)


GATHER_LIMIT = 1 << 22


def chosen_body(segment_input, inner_input, *rest):
    gathered = inner_input.size * inner_input.dtype.itemsize * lax.axis_size("rows")
    if gathered <= GATHER_LIMIT:
        return gathered_body(segment_input, inner_input, *rest)
    return body(segment_input, inner_input, *rest)


def solution(mesh):
    placed = (
        P("clips", "tm", "rows", None, None),
        P("clips", "tm", "rows", None, None),
        P("clips", "tm"),
        P(),
        P(),
        P(),
        P(),
        P(),
        P(),
        P(),
        P(),
    )
    return jax.shard_map(
        chosen_body,
        mesh=mesh,
        in_specs=placed,
        out_specs=P("clips", "tm", "rows", None, None),
        check_vma=False,
    )
```

```python
import functools
import math

import jax
import jax.numpy as jnp
from jax import lax
from jax.sharding import PartitionSpec as P
from jax.experimental import pallas as pl
from jax.experimental.pallas import tpu as pltpu

EPSILON = 1e-06


def prefix(part, axis, combine, identity):
    place = lax.axis_index(axis)
    gathered = jax.tree.map(lambda a: lax.all_gather(a, axis), part)
    state = jax.tree.map(lambda a, e: jnp.zeros_like(a) + jnp.asarray(e, a.dtype), part, identity)

    def one(step, state):
        return combine(
            state, jax.tree.map(lambda a: lax.dynamic_index_in_dim(a, step, 0, False), gathered)
        )

    return lax.fori_loop(0, place, one, state)


def as_sent(x):

    def short(part):
        return part.astype(jnp.bfloat16) if part.dtype == jnp.float32 else part

    return jax.tree.map(short, x)


def with_halo(cells, sides, width):
    for axis, dim in sides:
        count = lax.axis_size(axis)
        ends = count - 1
        head = lax.slice_in_dim(cells, 0, width, axis=dim)
        tail = lax.slice_in_dim(cells, cells.shape[dim] - width, cells.shape[dim], axis=dim)
        cells = jnp.concatenate(
            [
                lax.ppermute(tail, axis, [(i, (i + 1) % count) for i in range(ends)]),
                cells,
                lax.ppermute(head, axis, [((i + 1) % count, i) for i in range(ends)]),
            ],
            axis=dim,
        )
    return cells


def normalize(field, gain):
    widened = field.astype(jnp.float32)
    return widened * lax.rsqrt(jnp.mean(widened * widened, axis=-1, keepdims=True) + EPSILON) * gain


def last_two(extended, counts):
    slot_total = extended.shape[1]
    chosen = []
    for position in range(2):
        target = counts + position
        picked = jnp.zeros_like(extended[:, 0])
        for slot_index in range(slot_total):
            matches = (target == slot_index)[:, None, None, None]
            picked = jnp.where(matches, extended[:, slot_index], picked)
        chosen.append(picked)
    return jnp.stack(chosen, axis=1)


def summarize(activated, counts):
    blanks = jnp.zeros((activated.shape[0], 2) + activated.shape[2:], activated.dtype)
    summary = last_two(jnp.concatenate([blanks, activated], axis=1), counts)
    return (summary, jnp.minimum(counts, 2).astype(jnp.bfloat16))


def join_later(earlier, later):
    early_frames, early_count = earlier
    late_frames, late_count = later
    complete = (late_count > 1.5)[:, None, None, None, None]
    single = (late_count > 0.5)[:, None, None, None, None]
    shifted = jnp.concatenate([early_frames[:, 1:], late_frames[:, 1:]], axis=1)
    frames = jnp.where(complete, late_frames, jnp.where(single, shifted, early_frames))
    total_count = jnp.minimum(early_count + late_count, 2.0).astype(early_count.dtype)
    return (frames, total_count)


def incoming_cache(summary, counts):
    starting = (jnp.zeros_like(summary), jnp.zeros_like(counts))
    combined = prefix((summary, counts), "tm", join_later, starting)
    return combined[0]


def convolve(padded, causal_weight, causal_bias):
    clip_count, slot_total, rows_padded, column_count, channels = padded.shape
    frame_count = slot_total - 2
    row_count = rows_padded - 2
    widened = jnp.pad(padded, ((0, 0), (0, 0), (0, 0), (1, 1), (0, 0)))
    summed = jnp.zeros((clip_count * frame_count * row_count * column_count, channels), jnp.float32)
    for delta_time in range(3):
        for delta_row in range(3):
            window = widened[
                :, delta_time : delta_time + frame_count, delta_row : delta_row + row_count
            ]
            columns = jnp.concatenate(
                [window[:, :, :, delta_col : delta_col + column_count] for delta_col in range(3)],
                axis=-1,
            )
            kernel = causal_weight[delta_time, delta_row].reshape(3 * channels, channels)
            summed = summed + jnp.dot(
                columns.reshape(-1, 3 * channels), kernel, preferred_element_type=jnp.float32
            )
    return summed.reshape(clip_count, frame_count, row_count, column_count, channels) + causal_bias


def attend(normed, triple_weight, triple_bias, output_weight, output_bias):
    frame_count, places, channels = normed.shape
    packed = (
        jnp.dot(normed.reshape(-1, channels), triple_weight, preferred_element_type=jnp.float32)
        + triple_bias
    )
    packed = packed.reshape(frame_count, places, 3 * channels)
    queries = packed[:, :, :channels]
    key_vectors = packed[:, :, channels : 2 * channels]
    values = packed[:, :, 2 * channels :].astype(jnp.bfloat16)
    scores = jnp.einsum(
        "nqc,nkc->nqk", queries, key_vectors, precision=lax.Precision.HIGHEST
    ) / math.sqrt(channels)
    row_max = jnp.max(scores, axis=-1, keepdims=True)
    exponent = jnp.exp(scores - row_max)
    weights = (exponent / jnp.sum(exponent, axis=-1, keepdims=True)).astype(jnp.bfloat16)
    attended = jnp.einsum(
        "nqk,nkc->nqc", weights, values, preferred_element_type=jnp.float32
    ).astype(jnp.bfloat16)
    projected = (
        jnp.dot(attended.reshape(-1, channels), output_weight, preferred_element_type=jnp.float32)
        + output_bias
    )
    return projected.reshape(frame_count, places, channels).astype(jnp.bfloat16)


def body(
    segment_input,
    inner_input,
    lengths,
    inner_gain,
    causal_weight,
    causal_bias,
    attention_gain,
    triple_weight,
    triple_bias,
    output_weight,
    output_bias,
):
    clip_count, frame_count, row_count, column_count, channels = segment_input.shape
    activated = jax.nn.silu(normalize(inner_input, inner_gain)).astype(jnp.bfloat16)
    counts = lengths[:, 0]
    live_mask = (jnp.arange(frame_count, dtype=jnp.int32)[None, :] < counts[:, None]).astype(
        jnp.float32
    )
    carried = incoming_cache(*summarize(activated, counts))
    extended = jnp.concatenate([carried, activated], axis=1)
    padded = with_halo(as_sent(extended), (("rows", 2),), 1).astype(extended.dtype)
    convolved = convolve(padded, causal_weight, causal_bias)
    residual = (segment_input.astype(jnp.float32) + convolved).astype(jnp.bfloat16)
    residual = lax.optimization_barrier(residual)
    normed = normalize(residual, attention_gain).astype(jnp.bfloat16)
    row_devices = lax.axis_size("rows")
    per_device = clip_count * frame_count // row_devices
    grouped = normed.reshape(row_devices, per_device, row_count, column_count, channels)
    portion = lax.all_to_all(grouped, "rows", split_axis=0, concat_axis=2, tiled=True)
    owned = portion.shape[1]
    height = portion.shape[2]
    flat = portion.reshape(owned, height * column_count, channels)
    result = attend(flat, triple_weight, triple_bias, output_weight, output_bias)
    result = result.reshape(1, owned, height, column_count, channels)
    projected = lax.all_to_all(result, "rows", split_axis=2, concat_axis=0, tiled=True)
    projected = projected.reshape(clip_count, frame_count, row_count, column_count, channels)
    projected = lax.optimization_barrier(projected)
    summed = residual.astype(jnp.float32) + projected.astype(jnp.float32)
    return (summed * live_mask[:, :, None, None, None]).astype(jnp.bfloat16)


def activate(field, gain):
    return jax.nn.silu(normalize(field, gain)).astype(jnp.bfloat16)


def conv_part_kernel(plan, first_tap, x_ref, w_hbm, o_ref, w_vmem, sems):
    clips, held, rows, columns, width = x_ref.shape
    height = rows - 2
    places = height * columns
    channels = w_vmem.shape[-1]
    copies = []
    for index in range(len(plan)):
        for kh in range(3):
            slot_index = index * 3 + kh
            copy = pltpu.make_async_copy(
                w_hbm.at[first_tap + index, kh], w_vmem.at[slot_index], sems.at[slot_index]
            )
            copy.start()
            copies.append(copy)
    written = set()
    for index, (frame, slot, count) in enumerate(plan):
        for kh in range(3):
            slot_index = index * 3 + kh
            copies[slot_index].wait()
            weight = w_vmem[slot_index].reshape(width, channels)
            lhs = x_ref[:, frame : frame + count, kh : kh + height, :, :]
            lhs = lhs.reshape(clips * count * places, width)
            term = jnp.dot(lhs, weight, preferred_element_type=jnp.float32)
            term = term.reshape(clips, count, places, channels)
            for part in range(count):
                target = slot + part
                if target in written:
                    o_ref[:, target] += term[:, part]
                else:
                    o_ref[:, target] = term[:, part]
                    written.add(target)


def conv_part(frames, causal_weight, plan, first_tap, slots):
    clips, held, height, columns, channels = frames.shape
    padded = jnp.pad(frames, ((0, 0), (0, 0), (1, 1), (1, 1), (0, 0)))
    taps = jnp.concatenate(
        [padded[:, :, :, kw : kw + columns] for kw in range(3)], axis=-1
    )
    places = height * columns
    dots = sum(count for _, _, count in plan) * 3
    blocks = len(plan) * 3
    return pl.pallas_call(
        functools.partial(conv_part_kernel, plan, first_tap),
        in_specs=[
            pl.BlockSpec(memory_space=pltpu.VMEM),
            pl.BlockSpec(memory_space=pl.ANY),
        ],
        out_specs=pl.BlockSpec(memory_space=pltpu.VMEM),
        out_shape=jax.ShapeDtypeStruct((clips, slots, places, channels), jnp.float32),
        scratch_shapes=[
            pltpu.VMEM((blocks, 3, channels, channels), causal_weight.dtype),
            pltpu.SemaphoreType.DMA((blocks,)),
        ],
        compiler_params=pltpu.CompilerParams(vmem_limit_bytes=48 * 1024 * 1024),
        cost_estimate=pl.CostEstimate(
            flops=2 * clips * places * dots * 3 * channels * channels,
            transcendentals=0,
            bytes_accessed=blocks * 3 * channels * channels * 2
            + taps.size * 2
            + clips * slots * places * channels * 4,
        ),
    )(taps, causal_weight)


def own_conv(own_frames, causal_weight):
    slots = own_frames.shape[1]
    return conv_part(own_frames, causal_weight, ((0, 0, slots),), 2, slots)


def carried_conv(carried_frames, causal_weight, slots):
    plan = ((0, 0, slots), (1, 0, slots))
    return conv_part(carried_frames, causal_weight, plan, 0, slots)


def frame_major(total, clips, height, columns):
    clips, slots, places, channels = total.shape
    return total.reshape(clips, slots, height, columns, channels)


def gathered_body(
    segment_input,
    inner_input,
    lengths,
    inner_gain,
    causal_weight,
    causal_bias,
    attention_gain,
    triple_weight,
    triple_bias,
    output_weight,
    output_bias,
):
    clip_count, frame_count, row_count, column_count, channels = segment_input.shape
    sections = lax.axis_size("tm")
    counts = lengths[:, 0]
    ahead = [(i, i + 1) for i in range(sections - 1)]
    prev_counts = lax.ppermute(counts, "tm", ahead)
    both = jnp.concatenate([inner_input, segment_input], axis=0)
    both_all = lax.all_gather(both, "rows", axis=2, tiled=True)
    inner_all = both_all[:clip_count]
    segment_all = both_all[clip_count:]
    wide = (counts > 1)[:, None, None, None]
    last_raw = jnp.where(wide, inner_all[:, frame_count - 1], inner_all[:, 0])
    prev_raw = lax.ppermute(inner_all, "tm", ahead)
    before_raw = lax.ppermute(last_raw, "tm", [(i, i + 2) for i in range(sections - 2)])
    own = activate(inner_all, inner_gain)
    own_sum = own_conv(own, causal_weight)
    own_sum, prev_raw, before_raw, prev_counts = lax.optimization_barrier(
        (own_sum, prev_raw, before_raw, prev_counts)
    )
    prev = activate(prev_raw, inner_gain)
    before = activate(before_raw, inner_gain)
    prev_wide = (prev_counts > 1)[:, None, None, None]
    carried = jnp.stack(
        [
            jnp.where(prev_wide, prev[:, frame_count - 2], before),
            jnp.where(prev_wide, prev[:, frame_count - 1], prev[:, 0]),
        ],
        axis=1,
    )
    carried = jnp.concatenate([carried, own[:, : frame_count - 1]], axis=1)
    carried_sum = carried_conv(carried, causal_weight, frame_count)
    height = inner_all.shape[2]
    convolved = frame_major(own_sum + carried_sum, clip_count, height, column_count) + causal_bias
    residual = (segment_all.astype(jnp.float32) + convolved).astype(jnp.bfloat16)
    normed = normalize(residual, attention_gain).astype(jnp.bfloat16)
    height = normed.shape[2]
    frames = clip_count * frame_count
    places = height * column_count
    flat = normed.reshape(frames * places, channels)
    packed = (
        jnp.dot(flat, triple_weight[:, channels:], preferred_element_type=jnp.float32)
        + triple_bias[channels:]
    ).reshape(frames, places, 2 * channels)
    key_vectors = packed[:, :, :channels]
    values = packed[:, :, channels:].astype(jnp.bfloat16)
    start = lax.axis_index("rows") * row_count
    mine = lax.dynamic_slice_in_dim(normed, start, row_count, axis=2)
    queries = (
        jnp.dot(
            mine.reshape(-1, channels), triple_weight[:, :channels],
            preferred_element_type=jnp.float32,
        )
        + triple_bias[:channels]
    ).reshape(frames, row_count * column_count, channels)
    scores = jnp.einsum(
        "nqc,nkc->nqk", queries, key_vectors, precision=lax.Precision.HIGHEST
    ) / math.sqrt(channels)
    row_max = jnp.max(scores, axis=-1, keepdims=True)
    exponent = jnp.exp(scores - row_max)
    weights = (exponent / jnp.sum(exponent, axis=-1, keepdims=True)).astype(jnp.bfloat16)
    attended = jnp.einsum(
        "nqk,nkc->nqc", weights, values, preferred_element_type=jnp.float32
    ).astype(jnp.bfloat16)
    projected = (
        jnp.dot(attended.reshape(-1, channels), output_weight, preferred_element_type=jnp.float32)
        + output_bias
    ).astype(jnp.bfloat16)
    projected = projected.reshape(clip_count, frame_count, row_count, column_count, channels)
    residual_mine = lax.dynamic_slice_in_dim(residual, start, row_count, axis=2)
    live_mask = (jnp.arange(frame_count, dtype=jnp.int32)[None, :] < counts[:, None]).astype(
        jnp.float32
    )
    summed = residual_mine.astype(jnp.float32) + projected.astype(jnp.float32)
    return (summed * live_mask[:, :, None, None, None]).astype(jnp.bfloat16)


GATHER_LIMIT = 1 << 22


def chosen_body(segment_input, inner_input, *rest):
    gathered = inner_input.size * inner_input.dtype.itemsize * lax.axis_size("rows")
    if gathered <= GATHER_LIMIT:
        return gathered_body(segment_input, inner_input, *rest)
    return body(segment_input, inner_input, *rest)


def solution(mesh):
    placed = (
        P("clips", "tm", "rows", None, None),
        P("clips", "tm", "rows", None, None),
        P("clips", "tm"),
        P(),
        P(),
        P(),
        P(),
        P(),
        P(),
        P(),
        P(),
    )
    return jax.shard_map(
        chosen_body,
        mesh=mesh,
        in_specs=placed,
        out_specs=P("clips", "tm", "rows", None, None),
        check_vma=False,
    )
```

```python
import functools
import math

import jax
import jax.numpy as jnp
from jax import lax
from jax.sharding import PartitionSpec as P
from jax.experimental import pallas as pl
from jax.experimental.pallas import tpu as pltpu

EPSILON = 1e-06


def prefix(part, axis, combine, identity):
    place = lax.axis_index(axis)
    gathered = jax.tree.map(lambda a: lax.all_gather(a, axis), part)
    state = jax.tree.map(lambda a, e: jnp.zeros_like(a) + jnp.asarray(e, a.dtype), part, identity)

    def one(step, state):
        return combine(
            state, jax.tree.map(lambda a: lax.dynamic_index_in_dim(a, step, 0, False), gathered)
        )

    return lax.fori_loop(0, place, one, state)


def as_sent(x):

    def short(part):
        return part.astype(jnp.bfloat16) if part.dtype == jnp.float32 else part

    return jax.tree.map(short, x)


def with_halo(cells, sides, width):
    for axis, dim in sides:
        count = lax.axis_size(axis)
        ends = count - 1
        head = lax.slice_in_dim(cells, 0, width, axis=dim)
        tail = lax.slice_in_dim(cells, cells.shape[dim] - width, cells.shape[dim], axis=dim)
        cells = jnp.concatenate(
            [
                lax.ppermute(tail, axis, [(i, (i + 1) % count) for i in range(ends)]),
                cells,
                lax.ppermute(head, axis, [((i + 1) % count, i) for i in range(ends)]),
            ],
            axis=dim,
        )
    return cells


def normalize(field, gain):
    widened = field.astype(jnp.float32)
    return widened * lax.rsqrt(jnp.mean(widened * widened, axis=-1, keepdims=True) + EPSILON) * gain


def last_two(extended, counts):
    slot_total = extended.shape[1]
    chosen = []
    for position in range(2):
        target = counts + position
        picked = jnp.zeros_like(extended[:, 0])
        for slot_index in range(slot_total):
            matches = (target == slot_index)[:, None, None, None]
            picked = jnp.where(matches, extended[:, slot_index], picked)
        chosen.append(picked)
    return jnp.stack(chosen, axis=1)


def summarize(activated, counts):
    blanks = jnp.zeros((activated.shape[0], 2) + activated.shape[2:], activated.dtype)
    summary = last_two(jnp.concatenate([blanks, activated], axis=1), counts)
    return (summary, jnp.minimum(counts, 2).astype(jnp.bfloat16))


def join_later(earlier, later):
    early_frames, early_count = earlier
    late_frames, late_count = later
    complete = (late_count > 1.5)[:, None, None, None, None]
    single = (late_count > 0.5)[:, None, None, None, None]
    shifted = jnp.concatenate([early_frames[:, 1:], late_frames[:, 1:]], axis=1)
    frames = jnp.where(complete, late_frames, jnp.where(single, shifted, early_frames))
    total_count = jnp.minimum(early_count + late_count, 2.0).astype(early_count.dtype)
    return (frames, total_count)


def incoming_cache(summary, counts):
    starting = (jnp.zeros_like(summary), jnp.zeros_like(counts))
    combined = prefix((summary, counts), "tm", join_later, starting)
    return combined[0]


def convolve(padded, causal_weight, causal_bias):
    clip_count, slot_total, rows_padded, column_count, channels = padded.shape
    frame_count = slot_total - 2
    row_count = rows_padded - 2
    widened = jnp.pad(padded, ((0, 0), (0, 0), (0, 0), (1, 1), (0, 0)))
    summed = jnp.zeros((clip_count * frame_count * row_count * column_count, channels), jnp.float32)
    for delta_time in range(3):
        for delta_row in range(3):
            window = widened[
                :, delta_time : delta_time + frame_count, delta_row : delta_row + row_count
            ]
            columns = jnp.concatenate(
                [window[:, :, :, delta_col : delta_col + column_count] for delta_col in range(3)],
                axis=-1,
            )
            kernel = causal_weight[delta_time, delta_row].reshape(3 * channels, channels)
            summed = summed + jnp.dot(
                columns.reshape(-1, 3 * channels), kernel, preferred_element_type=jnp.float32
            )
    return summed.reshape(clip_count, frame_count, row_count, column_count, channels) + causal_bias


def attend(normed, triple_weight, triple_bias, output_weight, output_bias):
    frame_count, places, channels = normed.shape
    packed = (
        jnp.dot(normed.reshape(-1, channels), triple_weight, preferred_element_type=jnp.float32)
        + triple_bias
    )
    packed = packed.reshape(frame_count, places, 3 * channels)
    queries = packed[:, :, :channels]
    key_vectors = packed[:, :, channels : 2 * channels]
    values = packed[:, :, 2 * channels :].astype(jnp.bfloat16)
    scores = jnp.einsum(
        "nqc,nkc->nqk", queries, key_vectors, precision=lax.Precision.HIGHEST
    ) / math.sqrt(channels)
    row_max = jnp.max(scores, axis=-1, keepdims=True)
    exponent = jnp.exp(scores - row_max)
    weights = (exponent / jnp.sum(exponent, axis=-1, keepdims=True)).astype(jnp.bfloat16)
    attended = jnp.einsum(
        "nqk,nkc->nqc", weights, values, preferred_element_type=jnp.float32
    ).astype(jnp.bfloat16)
    projected = (
        jnp.dot(attended.reshape(-1, channels), output_weight, preferred_element_type=jnp.float32)
        + output_bias
    )
    return projected.reshape(frame_count, places, channels).astype(jnp.bfloat16)


def body(
    segment_input,
    inner_input,
    lengths,
    inner_gain,
    causal_weight,
    causal_bias,
    attention_gain,
    triple_weight,
    triple_bias,
    output_weight,
    output_bias,
):
    clip_count, frame_count, row_count, column_count, channels = segment_input.shape
    activated = jax.nn.silu(normalize(inner_input, inner_gain)).astype(jnp.bfloat16)
    counts = lengths[:, 0]
    live_mask = (jnp.arange(frame_count, dtype=jnp.int32)[None, :] < counts[:, None]).astype(
        jnp.float32
    )
    carried = incoming_cache(*summarize(activated, counts))
    extended = jnp.concatenate([carried, activated], axis=1)
    padded = with_halo(as_sent(extended), (("rows", 2),), 1).astype(extended.dtype)
    convolved = convolve(padded, causal_weight, causal_bias)
    residual = (segment_input.astype(jnp.float32) + convolved).astype(jnp.bfloat16)
    residual = lax.optimization_barrier(residual)
    normed = normalize(residual, attention_gain).astype(jnp.bfloat16)
    row_devices = lax.axis_size("rows")
    per_device = clip_count * frame_count // row_devices
    grouped = normed.reshape(row_devices, per_device, row_count, column_count, channels)
    portion = lax.all_to_all(grouped, "rows", split_axis=0, concat_axis=2, tiled=True)
    owned = portion.shape[1]
    height = portion.shape[2]
    flat = portion.reshape(owned, height * column_count, channels)
    result = attend(flat, triple_weight, triple_bias, output_weight, output_bias)
    result = result.reshape(1, owned, height, column_count, channels)
    projected = lax.all_to_all(result, "rows", split_axis=2, concat_axis=0, tiled=True)
    projected = projected.reshape(clip_count, frame_count, row_count, column_count, channels)
    projected = lax.optimization_barrier(projected)
    summed = residual.astype(jnp.float32) + projected.astype(jnp.float32)
    return (summed * live_mask[:, :, None, None, None]).astype(jnp.bfloat16)


def activate(field, gain):
    return jax.nn.silu(normalize(field, gain)).astype(jnp.bfloat16)


def conv_part_kernel(plan, first_tap, x_ref, w_hbm, o_ref, w_vmem, sems):
    clips, held, rows, columns, width = x_ref.shape
    height = rows - 2
    places = height * columns
    channels = w_vmem.shape[-1]
    copies = []
    for index in range(len(plan)):
        for kh in range(3):
            slot_index = index * 3 + kh
            copy = pltpu.make_async_copy(
                w_hbm.at[first_tap + index, kh], w_vmem.at[slot_index], sems.at[slot_index]
            )
            copy.start()
            copies.append(copy)
    written = set()
    for index, (frame, slot, count) in enumerate(plan):
        for kh in range(3):
            slot_index = index * 3 + kh
            copies[slot_index].wait()
            weight = w_vmem[slot_index].reshape(width, channels)
            lhs = x_ref[:, frame : frame + count, kh : kh + height, :, :]
            lhs = lhs.reshape(clips * count * places, width)
            term = jnp.dot(lhs, weight, preferred_element_type=jnp.float32)
            term = term.reshape(clips, count, places, channels)
            for part in range(count):
                target = slot + part
                if target in written:
                    o_ref[:, target] += term[:, part]
                else:
                    o_ref[:, target] = term[:, part]
                    written.add(target)


def conv_part(frames, causal_weight, plan, first_tap, slots):
    clips, held, height, columns, channels = frames.shape
    padded = jnp.pad(frames, ((0, 0), (0, 0), (1, 1), (1, 1), (0, 0)))
    taps = jnp.concatenate(
        [padded[:, :, :, kw : kw + columns] for kw in range(3)], axis=-1
    )
    places = height * columns
    dots = sum(count for _, _, count in plan) * 3
    blocks = len(plan) * 3
    return pl.pallas_call(
        functools.partial(conv_part_kernel, plan, first_tap),
        in_specs=[
            pl.BlockSpec(memory_space=pltpu.VMEM),
            pl.BlockSpec(memory_space=pl.ANY),
        ],
        out_specs=pl.BlockSpec(memory_space=pltpu.VMEM),
        out_shape=jax.ShapeDtypeStruct((clips, slots, places, channels), jnp.float32),
        scratch_shapes=[
            pltpu.VMEM((blocks, 3, channels, channels), causal_weight.dtype),
            pltpu.SemaphoreType.DMA((blocks,)),
        ],
        compiler_params=pltpu.CompilerParams(vmem_limit_bytes=48 * 1024 * 1024),
        cost_estimate=pl.CostEstimate(
            flops=2 * clips * places * dots * 3 * channels * channels,
            transcendentals=0,
            bytes_accessed=blocks * 3 * channels * channels * 2
            + taps.size * 2
            + clips * slots * places * channels * 4,
        ),
    )(taps, causal_weight)


def conv_plans(slots):
    own, carried = {}, {}
    for kt in range(3):
        for slot in range(slots):
            source = slot + kt
            if source >= 2:
                own.setdefault(kt, []).append((source - 2, slot))
            else:
                carried.setdefault(kt, []).append((source, slot))
    return own, carried


def plan_of(table):
    taps = sorted(table)
    assert taps == list(range(taps[0], taps[-1] + 1))
    runs = []
    for kt in taps:
        pairs = sorted(table[kt], key=lambda pair: pair[1])
        frame, slot = pairs[0]
        assert pairs == [(frame + k, slot + k) for k in range(len(pairs))]
        runs.append((frame, slot, len(pairs)))
    return tuple(runs), taps[0]


def own_conv(own_frames, causal_weight):
    own_table, _ = conv_plans(own_frames.shape[1])
    own_plan, own_first = plan_of(own_table)
    return conv_part(own_frames, causal_weight, own_plan, own_first, own_frames.shape[1])


def carried_conv(carried_frames, causal_weight, slots):
    _, carried_table = conv_plans(slots)
    carried_plan, carried_first = plan_of(carried_table)
    return conv_part(carried_frames, causal_weight, carried_plan, carried_first, slots)


def frame_major(total, clips, height, columns):
    clips, slots, places, channels = total.shape
    return total.reshape(clips, slots, height, columns, channels)


def gathered_body(
    segment_input,
    inner_input,
    lengths,
    inner_gain,
    causal_weight,
    causal_bias,
    attention_gain,
    triple_weight,
    triple_bias,
    output_weight,
    output_bias,
):
    clip_count, frame_count, row_count, column_count, channels = segment_input.shape
    sections = lax.axis_size("tm")
    counts = lengths[:, 0]
    ahead = [(i, i + 1) for i in range(sections - 1)]
    row_devices = lax.axis_size("rows")
    row_place = lax.axis_index("rows")
    segment_own = segment_input.reshape(clip_count, frame_count, row_count * column_count, channels)
    received = [segment_own] + [
        lax.ppermute(
            segment_own, "rows", [(i, (i + shift) % row_devices) for i in range(row_devices)]
        )
        for shift in range(1, row_devices)
    ]
    inner_all = lax.all_gather(inner_input, "rows", axis=2, tiled=True)
    by_shift = jnp.stack(received)
    order = (row_place - jnp.arange(row_devices)) % row_devices
    segment_all = jnp.take(by_shift, order, axis=0)
    segment_all = jnp.moveaxis(segment_all, 0, 2).reshape(
        clip_count, frame_count, row_devices * row_count, column_count, channels
    )
    wide = (counts > 1)[:, None, None, None]
    last_raw = jnp.where(wide, inner_all[:, frame_count - 1], inner_all[:, 0])
    height = inner_all.shape[2]
    marks = jnp.broadcast_to(
        counts.astype(inner_all.dtype)[:, None, None, None, None],
        (clip_count, frame_count, height, column_count, 128),
    )
    sent = lax.ppermute(jnp.concatenate([inner_all, marks], axis=-1), "tm", ahead)
    prev_raw = sent[..., :channels]
    prev_counts = sent[:, 0, 0, 0, channels]
    before_raw = lax.ppermute(last_raw, "tm", [(i, i + 2) for i in range(sections - 2)])
    own = activate(inner_all, inner_gain)
    own_sum = own_conv(own, causal_weight)
    own_sum, prev_raw, before_raw, prev_counts = lax.optimization_barrier(
        (own_sum, prev_raw, before_raw, prev_counts)
    )
    prev = activate(prev_raw, inner_gain)
    before = activate(before_raw, inner_gain)
    prev_wide = (prev_counts > 1)[:, None, None, None]
    carried = jnp.stack(
        [
            jnp.where(prev_wide, prev[:, frame_count - 2], before),
            jnp.where(prev_wide, prev[:, frame_count - 1], prev[:, 0]),
        ],
        axis=1,
    )
    carried_sum = carried_conv(carried, causal_weight, frame_count)
    convolved = frame_major(own_sum + carried_sum, clip_count, height, column_count) + causal_bias
    residual = (segment_all.astype(jnp.float32) + convolved).astype(jnp.bfloat16)
    normed = normalize(residual, attention_gain).astype(jnp.bfloat16)
    height = normed.shape[2]
    frames = clip_count * frame_count
    places = height * column_count
    flat = normed.reshape(frames * places, channels)
    packed = (
        jnp.dot(flat, triple_weight[:, channels:], preferred_element_type=jnp.float32)
        + triple_bias[channels:]
    ).reshape(frames, places, 2 * channels)
    key_vectors = packed[:, :, :channels]
    values = packed[:, :, channels:].astype(jnp.bfloat16)
    start = lax.axis_index("rows") * row_count
    mine = lax.dynamic_slice_in_dim(normed, start, row_count, axis=2)
    queries = (
        jnp.dot(
            mine.reshape(-1, channels), triple_weight[:, :channels],
            preferred_element_type=jnp.float32,
        )
        + triple_bias[:channels]
    ).reshape(frames, row_count * column_count, channels)
    scores = jnp.einsum(
        "nqc,nkc->nqk", queries, key_vectors, precision=lax.Precision.HIGHEST
    ) / math.sqrt(channels)
    row_max = jnp.max(scores, axis=-1, keepdims=True)
    exponent = jnp.exp(scores - row_max)
    weights = (exponent / jnp.sum(exponent, axis=-1, keepdims=True)).astype(jnp.bfloat16)
    attended = jnp.einsum(
        "nqk,nkc->nqc", weights, values, preferred_element_type=jnp.float32
    ).astype(jnp.bfloat16)
    projected = (
        jnp.dot(attended.reshape(-1, channels), output_weight, preferred_element_type=jnp.float32)
        + output_bias
    ).astype(jnp.bfloat16)
    projected = projected.reshape(clip_count, frame_count, row_count, column_count, channels)
    residual_mine = lax.dynamic_slice_in_dim(residual, start, row_count, axis=2)
    live_mask = (jnp.arange(frame_count, dtype=jnp.int32)[None, :] < counts[:, None]).astype(
        jnp.float32
    )
    summed = residual_mine.astype(jnp.float32) + projected.astype(jnp.float32)
    return (summed * live_mask[:, :, None, None, None]).astype(jnp.bfloat16)


GATHER_LIMIT = 1 << 22


def chosen_body(segment_input, inner_input, *rest):
    gathered = inner_input.size * inner_input.dtype.itemsize * lax.axis_size("rows")
    if gathered <= GATHER_LIMIT:
        return gathered_body(segment_input, inner_input, *rest)
    return body(segment_input, inner_input, *rest)


def solution(mesh):
    placed = (
        P("clips", "tm", "rows", None, None),
        P("clips", "tm", "rows", None, None),
        P("clips", "tm"),
        P(),
        P(),
        P(),
        P(),
        P(),
        P(),
        P(),
        P(),
    )
    return jax.shard_map(
        chosen_body,
        mesh=mesh,
        in_specs=placed,
        out_specs=P("clips", "tm", "rows", None, None),
        check_vma=False,
    )
```

```python
import functools
import math

import jax
import jax.numpy as jnp
from jax import lax
from jax.sharding import PartitionSpec as P
from jax.experimental import pallas as pl
from jax.experimental.pallas import tpu as pltpu

EPSILON = 1e-06


def prefix(part, axis, combine, identity):
    place = lax.axis_index(axis)
    gathered = jax.tree.map(lambda a: lax.all_gather(a, axis), part)
    state = jax.tree.map(lambda a, e: jnp.zeros_like(a) + jnp.asarray(e, a.dtype), part, identity)

    def one(step, state):
        return combine(
            state, jax.tree.map(lambda a: lax.dynamic_index_in_dim(a, step, 0, False), gathered)
        )

    return lax.fori_loop(0, place, one, state)


def as_sent(x):

    def short(part):
        return part.astype(jnp.bfloat16) if part.dtype == jnp.float32 else part

    return jax.tree.map(short, x)


def with_halo(cells, sides, width):
    for axis, dim in sides:
        count = lax.axis_size(axis)
        ends = count - 1
        head = lax.slice_in_dim(cells, 0, width, axis=dim)
        tail = lax.slice_in_dim(cells, cells.shape[dim] - width, cells.shape[dim], axis=dim)
        cells = jnp.concatenate(
            [
                lax.ppermute(tail, axis, [(i, (i + 1) % count) for i in range(ends)]),
                cells,
                lax.ppermute(head, axis, [((i + 1) % count, i) for i in range(ends)]),
            ],
            axis=dim,
        )
    return cells


def normalize(field, gain):
    widened = field.astype(jnp.float32)
    return widened * lax.rsqrt(jnp.mean(widened * widened, axis=-1, keepdims=True) + EPSILON) * gain


def last_two(extended, counts):
    slot_total = extended.shape[1]
    chosen = []
    for position in range(2):
        target = counts + position
        picked = jnp.zeros_like(extended[:, 0])
        for slot_index in range(slot_total):
            matches = (target == slot_index)[:, None, None, None]
            picked = jnp.where(matches, extended[:, slot_index], picked)
        chosen.append(picked)
    return jnp.stack(chosen, axis=1)


def summarize(activated, counts):
    blanks = jnp.zeros((activated.shape[0], 2) + activated.shape[2:], activated.dtype)
    summary = last_two(jnp.concatenate([blanks, activated], axis=1), counts)
    return (summary, jnp.minimum(counts, 2).astype(jnp.bfloat16))


def join_later(earlier, later):
    early_frames, early_count = earlier
    late_frames, late_count = later
    complete = (late_count > 1.5)[:, None, None, None, None]
    single = (late_count > 0.5)[:, None, None, None, None]
    shifted = jnp.concatenate([early_frames[:, 1:], late_frames[:, 1:]], axis=1)
    frames = jnp.where(complete, late_frames, jnp.where(single, shifted, early_frames))
    total_count = jnp.minimum(early_count + late_count, 2.0).astype(early_count.dtype)
    return (frames, total_count)


def incoming_cache(summary, counts):
    starting = (jnp.zeros_like(summary), jnp.zeros_like(counts))
    combined = prefix((summary, counts), "tm", join_later, starting)
    return combined[0]


def convolve(padded, causal_weight, causal_bias):
    clip_count, slot_total, rows_padded, column_count, channels = padded.shape
    frame_count = slot_total - 2
    row_count = rows_padded - 2
    widened = jnp.pad(padded, ((0, 0), (0, 0), (0, 0), (1, 1), (0, 0)))
    summed = jnp.zeros((clip_count * frame_count * row_count * column_count, channels), jnp.float32)
    for delta_time in range(3):
        for delta_row in range(3):
            window = widened[
                :, delta_time : delta_time + frame_count, delta_row : delta_row + row_count
            ]
            columns = jnp.concatenate(
                [window[:, :, :, delta_col : delta_col + column_count] for delta_col in range(3)],
                axis=-1,
            )
            kernel = causal_weight[delta_time, delta_row].reshape(3 * channels, channels)
            summed = summed + jnp.dot(
                columns.reshape(-1, 3 * channels), kernel, preferred_element_type=jnp.float32
            )
    return summed.reshape(clip_count, frame_count, row_count, column_count, channels) + causal_bias


def attend(normed, triple_weight, triple_bias, output_weight, output_bias):
    frame_count, places, channels = normed.shape
    packed = (
        jnp.dot(normed.reshape(-1, channels), triple_weight, preferred_element_type=jnp.float32)
        + triple_bias
    )
    packed = packed.reshape(frame_count, places, 3 * channels)
    queries = packed[:, :, :channels]
    key_vectors = packed[:, :, channels : 2 * channels]
    values = packed[:, :, 2 * channels :].astype(jnp.bfloat16)
    scores = jnp.einsum(
        "nqc,nkc->nqk", queries, key_vectors, precision=lax.Precision.HIGHEST
    ) / math.sqrt(channels)
    row_max = jnp.max(scores, axis=-1, keepdims=True)
    exponent = jnp.exp(scores - row_max)
    weights = (exponent / jnp.sum(exponent, axis=-1, keepdims=True)).astype(jnp.bfloat16)
    attended = jnp.einsum(
        "nqk,nkc->nqc", weights, values, preferred_element_type=jnp.float32
    ).astype(jnp.bfloat16)
    projected = (
        jnp.dot(attended.reshape(-1, channels), output_weight, preferred_element_type=jnp.float32)
        + output_bias
    )
    return projected.reshape(frame_count, places, channels).astype(jnp.bfloat16)


def body(
    segment_input,
    inner_input,
    lengths,
    inner_gain,
    causal_weight,
    causal_bias,
    attention_gain,
    triple_weight,
    triple_bias,
    output_weight,
    output_bias,
):
    clip_count, frame_count, row_count, column_count, channels = segment_input.shape
    activated = jax.nn.silu(normalize(inner_input, inner_gain)).astype(jnp.bfloat16)
    counts = lengths[:, 0]
    live_mask = (jnp.arange(frame_count, dtype=jnp.int32)[None, :] < counts[:, None]).astype(
        jnp.float32
    )
    carried = incoming_cache(*summarize(activated, counts))
    extended = jnp.concatenate([carried, activated], axis=1)
    padded = with_halo(as_sent(extended), (("rows", 2),), 1).astype(extended.dtype)
    convolved = convolve(padded, causal_weight, causal_bias)
    residual = (segment_input.astype(jnp.float32) + convolved).astype(jnp.bfloat16)
    residual = lax.optimization_barrier(residual)
    normed = normalize(residual, attention_gain).astype(jnp.bfloat16)
    row_devices = lax.axis_size("rows")
    per_device = clip_count * frame_count // row_devices
    grouped = normed.reshape(row_devices, per_device, row_count, column_count, channels)
    portion = lax.all_to_all(grouped, "rows", split_axis=0, concat_axis=2, tiled=True)
    owned = portion.shape[1]
    height = portion.shape[2]
    flat = portion.reshape(owned, height * column_count, channels)
    result = attend(flat, triple_weight, triple_bias, output_weight, output_bias)
    result = result.reshape(1, owned, height, column_count, channels)
    projected = lax.all_to_all(result, "rows", split_axis=2, concat_axis=0, tiled=True)
    projected = projected.reshape(clip_count, frame_count, row_count, column_count, channels)
    projected = lax.optimization_barrier(projected)
    summed = residual.astype(jnp.float32) + projected.astype(jnp.float32)
    return (summed * live_mask[:, :, None, None, None]).astype(jnp.bfloat16)


def activate(field, gain):
    return jax.nn.silu(normalize(field, gain)).astype(jnp.bfloat16)


def conv_part_kernel(plan, first_tap, x_ref, w_hbm, o_ref, w_vmem, sems):
    clips, held, rows, columns, width = x_ref.shape
    height = rows - 2
    places = height * columns
    channels = w_vmem.shape[-1]
    copies = []
    for index in range(len(plan)):
        for kh in range(3):
            slot_index = index * 3 + kh
            copy = pltpu.make_async_copy(
                w_hbm.at[first_tap + index, kh], w_vmem.at[slot_index], sems.at[slot_index]
            )
            copy.start()
            copies.append(copy)
    written = set()
    for index, (frame, slot, count) in enumerate(plan):
        for kh in range(3):
            slot_index = index * 3 + kh
            copies[slot_index].wait()
            weight = w_vmem[slot_index].reshape(width, channels)
            lhs = x_ref[:, frame : frame + count, kh : kh + height, :, :]
            lhs = lhs.reshape(clips * count * places, width)
            term = jnp.dot(lhs, weight, preferred_element_type=jnp.float32)
            term = term.reshape(clips, count, places, channels)
            for part in range(count):
                target = slot + part
                if target in written:
                    o_ref[:, target] += term[:, part]
                else:
                    o_ref[:, target] = term[:, part]
                    written.add(target)


def conv_part(frames, causal_weight, plan, first_tap, slots):
    clips, held, height, columns, channels = frames.shape
    padded = jnp.pad(frames, ((0, 0), (0, 0), (1, 1), (1, 1), (0, 0)))
    taps = jnp.concatenate(
        [padded[:, :, :, kw : kw + columns] for kw in range(3)], axis=-1
    )
    places = height * columns
    dots = sum(count for _, _, count in plan) * 3
    blocks = len(plan) * 3
    return pl.pallas_call(
        functools.partial(conv_part_kernel, plan, first_tap),
        in_specs=[
            pl.BlockSpec(memory_space=pltpu.VMEM),
            pl.BlockSpec(memory_space=pl.ANY),
        ],
        out_specs=pl.BlockSpec(memory_space=pltpu.VMEM),
        out_shape=jax.ShapeDtypeStruct((clips, slots, places, channels), jnp.float32),
        scratch_shapes=[
            pltpu.VMEM((blocks, 3, channels, channels), causal_weight.dtype),
            pltpu.SemaphoreType.DMA((blocks,)),
        ],
        compiler_params=pltpu.CompilerParams(vmem_limit_bytes=48 * 1024 * 1024),
        cost_estimate=pl.CostEstimate(
            flops=2 * clips * places * dots * 3 * channels * channels,
            transcendentals=0,
            bytes_accessed=blocks * 3 * channels * channels * 2
            + taps.size * 2
            + clips * slots * places * channels * 4,
        ),
    )(taps, causal_weight)


def conv_plans(slots):
    own, carried = {}, {}
    for kt in range(3):
        for slot in range(slots):
            source = slot + kt
            if source >= 2:
                own.setdefault(kt, []).append((source - 2, slot))
            else:
                carried.setdefault(kt, []).append((source, slot))
    return own, carried


def plan_of(table):
    taps = sorted(table)
    assert taps == list(range(taps[0], taps[-1] + 1))
    runs = []
    for kt in taps:
        pairs = sorted(table[kt], key=lambda pair: pair[1])
        frame, slot = pairs[0]
        assert pairs == [(frame + k, slot + k) for k in range(len(pairs))]
        runs.append((frame, slot, len(pairs)))
    return tuple(runs), taps[0]


def own_conv(own_frames, causal_weight):
    own_table, _ = conv_plans(own_frames.shape[1])
    own_plan, own_first = plan_of(own_table)
    return conv_part(own_frames, causal_weight, own_plan, own_first, own_frames.shape[1])


def carried_conv(carried_frames, causal_weight, slots):
    _, carried_table = conv_plans(slots)
    carried_plan, carried_first = plan_of(carried_table)
    return conv_part(carried_frames, causal_weight, carried_plan, carried_first, slots)


def frame_major(total, clips, height, columns):
    clips, slots, places, channels = total.shape
    return total.reshape(clips, slots, height, columns, channels)


def gathered_body(
    segment_input,
    inner_input,
    lengths,
    inner_gain,
    causal_weight,
    causal_bias,
    attention_gain,
    triple_weight,
    triple_bias,
    output_weight,
    output_bias,
):
    clip_count, frame_count, row_count, column_count, channels = segment_input.shape
    sections = lax.axis_size("tm")
    counts = lengths[:, 0]
    ahead = [(i, i + 1) for i in range(sections - 1)]
    prev_counts = lax.ppermute(counts, "tm", ahead)
    both = jnp.concatenate([inner_input, segment_input], axis=0)
    both_all = lax.all_gather(both, "rows", axis=2, tiled=True)
    inner_all = both_all[:clip_count]
    segment_all = both_all[clip_count:]
    wide = (counts > 1)[:, None, None, None]
    own = activate(inner_all, inner_gain)
    last = jnp.where(wide, own[:, frame_count - 1], own[:, 0])
    prev = lax.ppermute(own, "tm", ahead)
    before = lax.ppermute(last, "tm", [(i, i + 2) for i in range(sections - 2)])
    own_sum = own_conv(own, causal_weight)
    own_sum, prev, before, prev_counts = lax.optimization_barrier(
        (own_sum, prev, before, prev_counts)
    )
    prev_wide = (prev_counts > 1)[:, None, None, None]
    carried = jnp.stack(
        [
            jnp.where(prev_wide, prev[:, frame_count - 2], before),
            jnp.where(prev_wide, prev[:, frame_count - 1], prev[:, 0]),
        ],
        axis=1,
    )
    carried_sum = carried_conv(carried, causal_weight, frame_count)
    height = inner_all.shape[2]
    convolved = frame_major(own_sum + carried_sum, clip_count, height, column_count) + causal_bias
    residual = (segment_all.astype(jnp.float32) + convolved).astype(jnp.bfloat16)
    normed = normalize(residual, attention_gain).astype(jnp.bfloat16)
    height = normed.shape[2]
    frames = clip_count * frame_count
    places = height * column_count
    flat = normed.reshape(frames * places, channels)
    packed = (
        jnp.dot(flat, triple_weight[:, channels:], preferred_element_type=jnp.float32)
        + triple_bias[channels:]
    ).reshape(frames, places, 2 * channels)
    key_vectors = packed[:, :, :channels]
    values = packed[:, :, channels:].astype(jnp.bfloat16)
    start = lax.axis_index("rows") * row_count
    mine = lax.dynamic_slice_in_dim(normed, start, row_count, axis=2)
    queries = (
        jnp.dot(
            mine.reshape(-1, channels), triple_weight[:, :channels],
            preferred_element_type=jnp.float32,
        )
        + triple_bias[:channels]
    ).reshape(frames, row_count * column_count, channels)
    scores = jnp.einsum(
        "nqc,nkc->nqk", queries, key_vectors, precision=lax.Precision.HIGHEST
    ) / math.sqrt(channels)
    row_max = jnp.max(scores, axis=-1, keepdims=True)
    exponent = jnp.exp(scores - row_max)
    weights = (exponent / jnp.sum(exponent, axis=-1, keepdims=True)).astype(jnp.bfloat16)
    attended = jnp.einsum(
        "nqk,nkc->nqc", weights, values, preferred_element_type=jnp.float32
    ).astype(jnp.bfloat16)
    projected = (
        jnp.dot(attended.reshape(-1, channels), output_weight, preferred_element_type=jnp.float32)
        + output_bias
    ).astype(jnp.bfloat16)
    projected = projected.reshape(clip_count, frame_count, row_count, column_count, channels)
    residual_mine = lax.dynamic_slice_in_dim(residual, start, row_count, axis=2)
    live_mask = (jnp.arange(frame_count, dtype=jnp.int32)[None, :] < counts[:, None]).astype(
        jnp.float32
    )
    summed = residual_mine.astype(jnp.float32) + projected.astype(jnp.float32)
    return (summed * live_mask[:, :, None, None, None]).astype(jnp.bfloat16)


GATHER_LIMIT = 1 << 22


def chosen_body(segment_input, inner_input, *rest):
    gathered = inner_input.size * inner_input.dtype.itemsize * lax.axis_size("rows")
    if gathered <= GATHER_LIMIT:
        return gathered_body(segment_input, inner_input, *rest)
    return body(segment_input, inner_input, *rest)


def solution(mesh):
    placed = (
        P("clips", "tm", "rows", None, None),
        P("clips", "tm", "rows", None, None),
        P("clips", "tm"),
        P(),
        P(),
        P(),
        P(),
        P(),
        P(),
        P(),
        P(),
    )
    return jax.shard_map(
        chosen_body,
        mesh=mesh,
        in_specs=placed,
        out_specs=P("clips", "tm", "rows", None, None),
        check_vma=False,
    )
```

```python
import functools
import math

import jax
import jax.numpy as jnp
from jax import lax
from jax.sharding import PartitionSpec as P
from jax.experimental import pallas as pl
from jax.experimental.pallas import tpu as pltpu

EPSILON = 1e-06


def prefix(part, axis, combine, identity):
    place = lax.axis_index(axis)
    gathered = jax.tree.map(lambda a: lax.all_gather(a, axis), part)
    state = jax.tree.map(lambda a, e: jnp.zeros_like(a) + jnp.asarray(e, a.dtype), part, identity)

    def one(step, state):
        return combine(
            state, jax.tree.map(lambda a: lax.dynamic_index_in_dim(a, step, 0, False), gathered)
        )

    return lax.fori_loop(0, place, one, state)


def as_sent(x):

    def short(part):
        return part.astype(jnp.bfloat16) if part.dtype == jnp.float32 else part

    return jax.tree.map(short, x)


def with_halo(cells, sides, width):
    for axis, dim in sides:
        count = lax.axis_size(axis)
        ends = count - 1
        head = lax.slice_in_dim(cells, 0, width, axis=dim)
        tail = lax.slice_in_dim(cells, cells.shape[dim] - width, cells.shape[dim], axis=dim)
        cells = jnp.concatenate(
            [
                lax.ppermute(tail, axis, [(i, (i + 1) % count) for i in range(ends)]),
                cells,
                lax.ppermute(head, axis, [((i + 1) % count, i) for i in range(ends)]),
            ],
            axis=dim,
        )
    return cells


def normalize(field, gain):
    widened = field.astype(jnp.float32)
    return widened * lax.rsqrt(jnp.mean(widened * widened, axis=-1, keepdims=True) + EPSILON) * gain


def last_two(extended, counts):
    slot_total = extended.shape[1]
    chosen = []
    for position in range(2):
        target = counts + position
        picked = jnp.zeros_like(extended[:, 0])
        for slot_index in range(slot_total):
            matches = (target == slot_index)[:, None, None, None]
            picked = jnp.where(matches, extended[:, slot_index], picked)
        chosen.append(picked)
    return jnp.stack(chosen, axis=1)


def summarize(activated, counts):
    blanks = jnp.zeros((activated.shape[0], 2) + activated.shape[2:], activated.dtype)
    summary = last_two(jnp.concatenate([blanks, activated], axis=1), counts)
    return (summary, jnp.minimum(counts, 2).astype(jnp.bfloat16))


def join_later(earlier, later):
    early_frames, early_count = earlier
    late_frames, late_count = later
    complete = (late_count > 1.5)[:, None, None, None, None]
    single = (late_count > 0.5)[:, None, None, None, None]
    shifted = jnp.concatenate([early_frames[:, 1:], late_frames[:, 1:]], axis=1)
    frames = jnp.where(complete, late_frames, jnp.where(single, shifted, early_frames))
    total_count = jnp.minimum(early_count + late_count, 2.0).astype(early_count.dtype)
    return (frames, total_count)


def incoming_cache(summary, counts):
    starting = (jnp.zeros_like(summary), jnp.zeros_like(counts))
    combined = prefix((summary, counts), "tm", join_later, starting)
    return combined[0]


def convolve(padded, causal_weight, causal_bias):
    clip_count, slot_total, rows_padded, column_count, channels = padded.shape
    frame_count = slot_total - 2
    row_count = rows_padded - 2
    widened = jnp.pad(padded, ((0, 0), (0, 0), (0, 0), (1, 1), (0, 0)))
    summed = jnp.zeros((clip_count * frame_count * row_count * column_count, channels), jnp.float32)
    for delta_time in range(3):
        for delta_row in range(3):
            window = widened[
                :, delta_time : delta_time + frame_count, delta_row : delta_row + row_count
            ]
            columns = jnp.concatenate(
                [window[:, :, :, delta_col : delta_col + column_count] for delta_col in range(3)],
                axis=-1,
            )
            kernel = causal_weight[delta_time, delta_row].reshape(3 * channels, channels)
            summed = summed + jnp.dot(
                columns.reshape(-1, 3 * channels), kernel, preferred_element_type=jnp.float32
            )
    return summed.reshape(clip_count, frame_count, row_count, column_count, channels) + causal_bias


def attend(normed, triple_weight, triple_bias, output_weight, output_bias):
    frame_count, places, channels = normed.shape
    packed = (
        jnp.dot(normed.reshape(-1, channels), triple_weight, preferred_element_type=jnp.float32)
        + triple_bias
    )
    packed = packed.reshape(frame_count, places, 3 * channels)
    queries = packed[:, :, :channels]
    key_vectors = packed[:, :, channels : 2 * channels]
    values = packed[:, :, 2 * channels :].astype(jnp.bfloat16)
    scores = jnp.einsum(
        "nqc,nkc->nqk", queries, key_vectors, precision=lax.Precision.HIGHEST
    ) / math.sqrt(channels)
    row_max = jnp.max(scores, axis=-1, keepdims=True)
    exponent = jnp.exp(scores - row_max)
    weights = (exponent / jnp.sum(exponent, axis=-1, keepdims=True)).astype(jnp.bfloat16)
    attended = jnp.einsum(
        "nqk,nkc->nqc", weights, values, preferred_element_type=jnp.float32
    ).astype(jnp.bfloat16)
    projected = (
        jnp.dot(attended.reshape(-1, channels), output_weight, preferred_element_type=jnp.float32)
        + output_bias
    )
    return projected.reshape(frame_count, places, channels).astype(jnp.bfloat16)


def body(
    segment_input,
    inner_input,
    lengths,
    inner_gain,
    causal_weight,
    causal_bias,
    attention_gain,
    triple_weight,
    triple_bias,
    output_weight,
    output_bias,
):
    clip_count, frame_count, row_count, column_count, channels = segment_input.shape
    activated = jax.nn.silu(normalize(inner_input, inner_gain)).astype(jnp.bfloat16)
    counts = lengths[:, 0]
    live_mask = (jnp.arange(frame_count, dtype=jnp.int32)[None, :] < counts[:, None]).astype(
        jnp.float32
    )
    carried = incoming_cache(*summarize(activated, counts))
    extended = jnp.concatenate([carried, activated], axis=1)
    padded = with_halo(as_sent(extended), (("rows", 2),), 1).astype(extended.dtype)
    convolved = convolve(padded, causal_weight, causal_bias)
    residual = (segment_input.astype(jnp.float32) + convolved).astype(jnp.bfloat16)
    residual = lax.optimization_barrier(residual)
    normed = normalize(residual, attention_gain).astype(jnp.bfloat16)
    row_devices = lax.axis_size("rows")
    per_device = clip_count * frame_count // row_devices
    grouped = normed.reshape(row_devices, per_device, row_count, column_count, channels)
    portion = lax.all_to_all(grouped, "rows", split_axis=0, concat_axis=2, tiled=True)
    owned = portion.shape[1]
    height = portion.shape[2]
    flat = portion.reshape(owned, height * column_count, channels)
    result = attend(flat, triple_weight, triple_bias, output_weight, output_bias)
    result = result.reshape(1, owned, height, column_count, channels)
    projected = lax.all_to_all(result, "rows", split_axis=2, concat_axis=0, tiled=True)
    projected = projected.reshape(clip_count, frame_count, row_count, column_count, channels)
    projected = lax.optimization_barrier(projected)
    summed = residual.astype(jnp.float32) + projected.astype(jnp.float32)
    return (summed * live_mask[:, :, None, None, None]).astype(jnp.bfloat16)


def activate(field, gain):
    return jax.nn.silu(normalize(field, gain)).astype(jnp.bfloat16)


def conv_part_kernel(plan, first_tap, x_ref, w_hbm, o_ref, w_vmem, sems):
    clips, held, rows, columns, width = x_ref.shape
    height = rows - 2
    places = height * columns
    channels = w_vmem.shape[-1]
    copies = []
    for index in range(len(plan)):
        for kh in range(3):
            slot_index = index * 3 + kh
            copy = pltpu.make_async_copy(
                w_hbm.at[first_tap + index, kh], w_vmem.at[slot_index], sems.at[slot_index]
            )
            copy.start()
            copies.append(copy)
    written = set()
    for index, (frame, slot, count) in enumerate(plan):
        for kh in range(3):
            slot_index = index * 3 + kh
            copies[slot_index].wait()
            weight = w_vmem[slot_index].reshape(width, channels)
            lhs = x_ref[:, frame : frame + count, kh : kh + height, :, :]
            lhs = lhs.reshape(clips * count * places, width)
            term = jnp.dot(lhs, weight, preferred_element_type=jnp.float32)
            term = term.reshape(clips, count, places, channels)
            for part in range(count):
                target = slot + part
                if target in written:
                    o_ref[:, target] += term[:, part]
                else:
                    o_ref[:, target] = term[:, part]
                    written.add(target)


def conv_part(frames, causal_weight, plan, first_tap, slots):
    clips, held, height, columns, channels = frames.shape
    padded = jnp.pad(frames, ((0, 0), (0, 0), (1, 1), (1, 1), (0, 0)))
    taps = jnp.concatenate(
        [padded[:, :, :, kw : kw + columns] for kw in range(3)], axis=-1
    )
    places = height * columns
    dots = sum(count for _, _, count in plan) * 3
    blocks = len(plan) * 3
    return pl.pallas_call(
        functools.partial(conv_part_kernel, plan, first_tap),
        in_specs=[
            pl.BlockSpec(memory_space=pltpu.VMEM),
            pl.BlockSpec(memory_space=pl.ANY),
        ],
        out_specs=pl.BlockSpec(memory_space=pltpu.VMEM),
        out_shape=jax.ShapeDtypeStruct((clips, slots, places, channels), jnp.float32),
        scratch_shapes=[
            pltpu.VMEM((blocks, 3, channels, channels), causal_weight.dtype),
            pltpu.SemaphoreType.DMA((blocks,)),
        ],
        compiler_params=pltpu.CompilerParams(vmem_limit_bytes=12 * 1024 * 1024),
        cost_estimate=pl.CostEstimate(
            flops=2 * clips * places * dots * 3 * channels * channels,
            transcendentals=0,
            bytes_accessed=blocks * 3 * channels * channels * 2
            + taps.size * 2
            + clips * slots * places * channels * 4,
        ),
    )(taps, causal_weight)


def conv_plans(slots):
    own, carried = {}, {}
    for kt in range(3):
        for slot in range(slots):
            source = slot + kt
            if source >= 2:
                own.setdefault(kt, []).append((source - 2, slot))
            else:
                carried.setdefault(kt, []).append((source, slot))
    return own, carried


def plan_of(table):
    taps = sorted(table)
    assert taps == list(range(taps[0], taps[-1] + 1))
    runs = []
    for kt in taps:
        pairs = sorted(table[kt], key=lambda pair: pair[1])
        frame, slot = pairs[0]
        assert pairs == [(frame + k, slot + k) for k in range(len(pairs))]
        runs.append((frame, slot, len(pairs)))
    return tuple(runs), taps[0]


def own_conv(own_frames, causal_weight):
    own_table, _ = conv_plans(own_frames.shape[1])
    own_plan, own_first = plan_of(own_table)
    return conv_part(own_frames, causal_weight, own_plan, own_first, own_frames.shape[1])


def carried_conv(carried_frames, causal_weight, slots):
    _, carried_table = conv_plans(slots)
    carried_plan, carried_first = plan_of(carried_table)
    return conv_part(carried_frames, causal_weight, carried_plan, carried_first, slots)


def frame_major(total, clips, height, columns):
    clips, slots, places, channels = total.shape
    return total.reshape(clips, slots, height, columns, channels)


def gathered_body(
    segment_input,
    inner_input,
    lengths,
    inner_gain,
    causal_weight,
    causal_bias,
    attention_gain,
    triple_weight,
    triple_bias,
    output_weight,
    output_bias,
):
    clip_count, frame_count, row_count, column_count, channels = segment_input.shape
    sections = lax.axis_size("tm")
    counts = lengths[:, 0]
    ahead = [(i, i + 1) for i in range(sections - 1)]
    prev_counts = lax.ppermute(counts, "tm", ahead)
    both = jnp.concatenate([inner_input, segment_input], axis=0)
    both_all = lax.all_gather(both, "rows", axis=2, tiled=True)
    inner_all = both_all[:clip_count]
    segment_all = both_all[clip_count:]
    wide = (counts > 1)[:, None, None, None]
    last_raw = jnp.where(wide, inner_all[:, frame_count - 1], inner_all[:, 0])
    prev_raw = lax.ppermute(inner_all, "tm", ahead)
    before_raw = lax.ppermute(last_raw, "tm", [(i, i + 2) for i in range(sections - 2)])
    own = activate(inner_all, inner_gain)
    own_sum = own_conv(own, causal_weight)
    own_sum, prev_raw, before_raw, prev_counts = lax.optimization_barrier(
        (own_sum, prev_raw, before_raw, prev_counts)
    )
    prev = activate(prev_raw, inner_gain)
    before = activate(before_raw, inner_gain)
    prev_wide = (prev_counts > 1)[:, None, None, None]
    carried = jnp.stack(
        [
            jnp.where(prev_wide, prev[:, frame_count - 2], before),
            jnp.where(prev_wide, prev[:, frame_count - 1], prev[:, 0]),
        ],
        axis=1,
    )
    carried_sum = carried_conv(carried, causal_weight, frame_count)
    height = inner_all.shape[2]
    convolved = frame_major(own_sum + carried_sum, clip_count, height, column_count) + causal_bias
    residual = (segment_all.astype(jnp.float32) + convolved).astype(jnp.bfloat16)
    normed = normalize(residual, attention_gain).astype(jnp.bfloat16)
    height = normed.shape[2]
    frames = clip_count * frame_count
    places = height * column_count
    flat = normed.reshape(frames * places, channels)
    packed = (
        jnp.dot(flat, triple_weight[:, channels:], preferred_element_type=jnp.float32)
        + triple_bias[channels:]
    ).reshape(frames, places, 2 * channels)
    key_vectors = packed[:, :, :channels]
    values = packed[:, :, channels:].astype(jnp.bfloat16)
    start = lax.axis_index("rows") * row_count
    mine = lax.dynamic_slice_in_dim(normed, start, row_count, axis=2)
    queries = (
        jnp.dot(
            mine.reshape(-1, channels), triple_weight[:, :channels],
            preferred_element_type=jnp.float32,
        )
        + triple_bias[:channels]
    ).reshape(frames, row_count * column_count, channels)
    scores = jnp.einsum(
        "nqc,nkc->nqk", queries, key_vectors, precision=lax.Precision.HIGHEST
    ) / math.sqrt(channels)
    row_max = jnp.max(scores, axis=-1, keepdims=True)
    exponent = jnp.exp(scores - row_max)
    weights = (exponent / jnp.sum(exponent, axis=-1, keepdims=True)).astype(jnp.bfloat16)
    attended = jnp.einsum(
        "nqk,nkc->nqc", weights, values, preferred_element_type=jnp.float32
    ).astype(jnp.bfloat16)
    projected = (
        jnp.dot(attended.reshape(-1, channels), output_weight, preferred_element_type=jnp.float32)
        + output_bias
    ).astype(jnp.bfloat16)
    projected = projected.reshape(clip_count, frame_count, row_count, column_count, channels)
    residual_mine = lax.dynamic_slice_in_dim(residual, start, row_count, axis=2)
    live_mask = (jnp.arange(frame_count, dtype=jnp.int32)[None, :] < counts[:, None]).astype(
        jnp.float32
    )
    summed = residual_mine.astype(jnp.float32) + projected.astype(jnp.float32)
    return (summed * live_mask[:, :, None, None, None]).astype(jnp.bfloat16)


GATHER_LIMIT = 1 << 22


def chosen_body(segment_input, inner_input, *rest):
    gathered = inner_input.size * inner_input.dtype.itemsize * lax.axis_size("rows")
    if gathered <= GATHER_LIMIT:
        return gathered_body(segment_input, inner_input, *rest)
    return body(segment_input, inner_input, *rest)


def solution(mesh):
    placed = (
        P("clips", "tm", "rows", None, None),
        P("clips", "tm", "rows", None, None),
        P("clips", "tm"),
        P(),
        P(),
        P(),
        P(),
        P(),
        P(),
        P(),
        P(),
    )
    return jax.shard_map(
        chosen_body,
        mesh=mesh,
        in_specs=placed,
        out_specs=P("clips", "tm", "rows", None, None),
        check_vma=False,
    )
```

```python
import functools
import math

import jax
import jax.numpy as jnp
from jax import lax
from jax.sharding import PartitionSpec as P
from jax.experimental import pallas as pl
from jax.experimental.pallas import tpu as pltpu

EPSILON = 1e-06


def prefix(part, axis, combine, identity):
    place = lax.axis_index(axis)
    gathered = jax.tree.map(lambda a: lax.all_gather(a, axis), part)
    state = jax.tree.map(lambda a, e: jnp.zeros_like(a) + jnp.asarray(e, a.dtype), part, identity)

    def one(step, state):
        return combine(
            state, jax.tree.map(lambda a: lax.dynamic_index_in_dim(a, step, 0, False), gathered)
        )

    return lax.fori_loop(0, place, one, state)


def as_sent(x):

    def short(part):
        return part.astype(jnp.bfloat16) if part.dtype == jnp.float32 else part

    return jax.tree.map(short, x)


def with_halo(cells, sides, width):
    for axis, dim in sides:
        count = lax.axis_size(axis)
        ends = count - 1
        head = lax.slice_in_dim(cells, 0, width, axis=dim)
        tail = lax.slice_in_dim(cells, cells.shape[dim] - width, cells.shape[dim], axis=dim)
        cells = jnp.concatenate(
            [
                lax.ppermute(tail, axis, [(i, (i + 1) % count) for i in range(ends)]),
                cells,
                lax.ppermute(head, axis, [((i + 1) % count, i) for i in range(ends)]),
            ],
            axis=dim,
        )
    return cells


def normalize(field, gain):
    widened = field.astype(jnp.float32)
    return widened * lax.rsqrt(jnp.mean(widened * widened, axis=-1, keepdims=True) + EPSILON) * gain


def last_two(extended, counts):
    slot_total = extended.shape[1]
    chosen = []
    for position in range(2):
        target = counts + position
        picked = jnp.zeros_like(extended[:, 0])
        for slot_index in range(slot_total):
            matches = (target == slot_index)[:, None, None, None]
            picked = jnp.where(matches, extended[:, slot_index], picked)
        chosen.append(picked)
    return jnp.stack(chosen, axis=1)


def summarize(activated, counts):
    blanks = jnp.zeros((activated.shape[0], 2) + activated.shape[2:], activated.dtype)
    summary = last_two(jnp.concatenate([blanks, activated], axis=1), counts)
    return (summary, jnp.minimum(counts, 2).astype(jnp.bfloat16))


def join_later(earlier, later):
    early_frames, early_count = earlier
    late_frames, late_count = later
    complete = (late_count > 1.5)[:, None, None, None, None]
    single = (late_count > 0.5)[:, None, None, None, None]
    shifted = jnp.concatenate([early_frames[:, 1:], late_frames[:, 1:]], axis=1)
    frames = jnp.where(complete, late_frames, jnp.where(single, shifted, early_frames))
    total_count = jnp.minimum(early_count + late_count, 2.0).astype(early_count.dtype)
    return (frames, total_count)


def incoming_cache(summary, counts):
    starting = (jnp.zeros_like(summary), jnp.zeros_like(counts))
    combined = prefix((summary, counts), "tm", join_later, starting)
    return combined[0]


def convolve(padded, causal_weight, causal_bias):
    clip_count, slot_total, rows_padded, column_count, channels = padded.shape
    frame_count = slot_total - 2
    row_count = rows_padded - 2
    widened = jnp.pad(padded, ((0, 0), (0, 0), (0, 0), (1, 1), (0, 0)))
    summed = jnp.zeros((clip_count * frame_count * row_count * column_count, channels), jnp.float32)
    for delta_time in range(3):
        for delta_row in range(3):
            window = widened[
                :, delta_time : delta_time + frame_count, delta_row : delta_row + row_count
            ]
            columns = jnp.concatenate(
                [window[:, :, :, delta_col : delta_col + column_count] for delta_col in range(3)],
                axis=-1,
            )
            kernel = causal_weight[delta_time, delta_row].reshape(3 * channels, channels)
            summed = summed + jnp.dot(
                columns.reshape(-1, 3 * channels), kernel, preferred_element_type=jnp.float32
            )
    return summed.reshape(clip_count, frame_count, row_count, column_count, channels) + causal_bias


def attend(normed, triple_weight, triple_bias, output_weight, output_bias):
    frame_count, places, channels = normed.shape
    packed = (
        jnp.dot(normed.reshape(-1, channels), triple_weight, preferred_element_type=jnp.float32)
        + triple_bias
    )
    packed = packed.reshape(frame_count, places, 3 * channels)
    queries = packed[:, :, :channels]
    key_vectors = packed[:, :, channels : 2 * channels]
    values = packed[:, :, 2 * channels :].astype(jnp.bfloat16)
    scores = jnp.einsum(
        "nqc,nkc->nqk", queries, key_vectors, precision=lax.Precision.HIGHEST
    ) / math.sqrt(channels)
    row_max = jnp.max(scores, axis=-1, keepdims=True)
    exponent = jnp.exp(scores - row_max)
    weights = (exponent / jnp.sum(exponent, axis=-1, keepdims=True)).astype(jnp.bfloat16)
    attended = jnp.einsum(
        "nqk,nkc->nqc", weights, values, preferred_element_type=jnp.float32
    ).astype(jnp.bfloat16)
    projected = (
        jnp.dot(attended.reshape(-1, channels), output_weight, preferred_element_type=jnp.float32)
        + output_bias
    )
    return projected.reshape(frame_count, places, channels).astype(jnp.bfloat16)


def body(
    segment_input,
    inner_input,
    lengths,
    inner_gain,
    causal_weight,
    causal_bias,
    attention_gain,
    triple_weight,
    triple_bias,
    output_weight,
    output_bias,
):
    clip_count, frame_count, row_count, column_count, channels = segment_input.shape
    activated = jax.nn.silu(normalize(inner_input, inner_gain)).astype(jnp.bfloat16)
    counts = lengths[:, 0]
    live_mask = (jnp.arange(frame_count, dtype=jnp.int32)[None, :] < counts[:, None]).astype(
        jnp.float32
    )
    carried = incoming_cache(*summarize(activated, counts))
    extended = jnp.concatenate([carried, activated], axis=1)
    padded = with_halo(as_sent(extended), (("rows", 2),), 1).astype(extended.dtype)
    convolved = convolve(padded, causal_weight, causal_bias)
    residual = (segment_input.astype(jnp.float32) + convolved).astype(jnp.bfloat16)
    residual = lax.optimization_barrier(residual)
    normed = normalize(residual, attention_gain).astype(jnp.bfloat16)
    row_devices = lax.axis_size("rows")
    per_device = clip_count * frame_count // row_devices
    grouped = normed.reshape(row_devices, per_device, row_count, column_count, channels)
    portion = lax.all_to_all(grouped, "rows", split_axis=0, concat_axis=2, tiled=True)
    owned = portion.shape[1]
    height = portion.shape[2]
    flat = portion.reshape(owned, height * column_count, channels)
    result = attend(flat, triple_weight, triple_bias, output_weight, output_bias)
    result = result.reshape(1, owned, height, column_count, channels)
    projected = lax.all_to_all(result, "rows", split_axis=2, concat_axis=0, tiled=True)
    projected = projected.reshape(clip_count, frame_count, row_count, column_count, channels)
    projected = lax.optimization_barrier(projected)
    summed = residual.astype(jnp.float32) + projected.astype(jnp.float32)
    return (summed * live_mask[:, :, None, None, None]).astype(jnp.bfloat16)


def activate(field, gain):
    return jax.nn.silu(normalize(field, gain)).astype(jnp.bfloat16)


def conv_part_kernel(plan, first_tap, x_ref, w_hbm, o_ref, w_vmem, sems):
    clips, held, rows, columns, width = x_ref.shape
    height = rows - 2
    places = height * columns
    channels = w_vmem.shape[-1]
    copies = []
    for index in range(len(plan)):
        for kh in range(3):
            slot_index = index * 3 + kh
            copy = pltpu.make_async_copy(
                w_hbm.at[first_tap + index, kh], w_vmem.at[slot_index], sems.at[slot_index]
            )
            copy.start()
            copies.append(copy)
    written = set()
    for index, (frame, slot, count) in enumerate(plan):
        for kh in range(3):
            slot_index = index * 3 + kh
            copies[slot_index].wait()
            weight = w_vmem[slot_index].reshape(width, channels)
            lhs = x_ref[:, frame : frame + count, kh : kh + height, :, :]
            lhs = lhs.reshape(clips * count * places, width)
            term = jnp.dot(lhs, weight, preferred_element_type=jnp.float32)
            term = term.reshape(clips, count, places, channels)
            for part in range(count):
                target = slot + part
                if target in written:
                    o_ref[:, target] += term[:, part]
                else:
                    o_ref[:, target] = term[:, part]
                    written.add(target)


def conv_part(frames, causal_weight, plan, first_tap, slots):
    clips, held, height, columns, channels = frames.shape
    padded = jnp.pad(frames, ((0, 0), (0, 0), (1, 1), (1, 1), (0, 0)))
    taps = jnp.concatenate(
        [padded[:, :, :, kw : kw + columns] for kw in range(3)], axis=-1
    )
    places = height * columns
    dots = sum(count for _, _, count in plan) * 3
    blocks = len(plan) * 3
    return pl.pallas_call(
        functools.partial(conv_part_kernel, plan, first_tap),
        in_specs=[
            pl.BlockSpec(memory_space=pltpu.VMEM),
            pl.BlockSpec(memory_space=pl.ANY),
        ],
        out_specs=pl.BlockSpec(memory_space=pltpu.VMEM),
        out_shape=jax.ShapeDtypeStruct((clips, slots, places, channels), jnp.float32),
        scratch_shapes=[
            pltpu.VMEM((blocks, 3, channels, channels), causal_weight.dtype),
            pltpu.SemaphoreType.DMA((blocks,)),
        ],
        compiler_params=pltpu.CompilerParams(vmem_limit_bytes=48 * 1024 * 1024),
        cost_estimate=pl.CostEstimate(
            flops=2 * clips * places * dots * 3 * channels * channels,
            transcendentals=0,
            bytes_accessed=blocks * 3 * channels * channels * 2
            + taps.size * 2
            + clips * slots * places * channels * 4,
        ),
    )(taps, causal_weight)


def conv_plans(slots):
    own, carried = {}, {}
    for kt in range(3):
        for slot in range(slots):
            source = slot + kt
            if source >= 2:
                own.setdefault(kt, []).append((source - 2, slot))
            else:
                carried.setdefault(kt, []).append((source, slot))
    return own, carried


def plan_of(table):
    taps = sorted(table)
    assert taps == list(range(taps[0], taps[-1] + 1))
    runs = []
    for kt in taps:
        pairs = sorted(table[kt], key=lambda pair: pair[1])
        frame, slot = pairs[0]
        assert pairs == [(frame + k, slot + k) for k in range(len(pairs))]
        runs.append((frame, slot, len(pairs)))
    return tuple(runs), taps[0]


def own_conv(own_frames, causal_weight):
    own_table, _ = conv_plans(own_frames.shape[1])
    own_plan, own_first = plan_of(own_table)
    return conv_part(own_frames, causal_weight, own_plan, own_first, own_frames.shape[1])


def carried_conv(carried_frames, causal_weight, slots):
    _, carried_table = conv_plans(slots)
    carried_plan, carried_first = plan_of(carried_table)
    return conv_part(carried_frames, causal_weight, carried_plan, carried_first, slots)


def frame_major(total, clips, height, columns):
    clips, slots, places, channels = total.shape
    return total.reshape(clips, slots, height, columns, channels)


def gathered_body(
    segment_input,
    inner_input,
    lengths,
    inner_gain,
    causal_weight,
    causal_bias,
    attention_gain,
    triple_weight,
    triple_bias,
    output_weight,
    output_bias,
):
    clip_count, frame_count, row_count, column_count, channels = segment_input.shape
    sections = lax.axis_size("tm")
    counts = lengths[:, 0]
    ahead = [(i, i + 1) for i in range(sections - 1)]
    prev_counts = lax.ppermute(counts, "tm", ahead)
    both = jnp.concatenate([inner_input, segment_input], axis=0)
    prev_counts, both = lax.optimization_barrier((prev_counts, both))
    both_all = lax.all_gather(both, "rows", axis=2, tiled=True)
    inner_all = both_all[:clip_count]
    segment_all = both_all[clip_count:]
    wide = (counts > 1)[:, None, None, None]
    last_raw = jnp.where(wide, inner_all[:, frame_count - 1], inner_all[:, 0])
    prev_raw = lax.ppermute(inner_all, "tm", ahead)
    before_raw = lax.ppermute(last_raw, "tm", [(i, i + 2) for i in range(sections - 2)])
    own = activate(inner_all, inner_gain)
    own_sum = own_conv(own, causal_weight)
    own_sum, prev_raw, before_raw, prev_counts = lax.optimization_barrier(
        (own_sum, prev_raw, before_raw, prev_counts)
    )
    prev = activate(prev_raw, inner_gain)
    before = activate(before_raw, inner_gain)
    prev_wide = (prev_counts > 1)[:, None, None, None]
    carried = jnp.stack(
        [
            jnp.where(prev_wide, prev[:, frame_count - 2], before),
            jnp.where(prev_wide, prev[:, frame_count - 1], prev[:, 0]),
        ],
        axis=1,
    )
    carried_sum = carried_conv(carried, causal_weight, frame_count)
    height = inner_all.shape[2]
    convolved = frame_major(own_sum + carried_sum, clip_count, height, column_count) + causal_bias
    residual = (segment_all.astype(jnp.float32) + convolved).astype(jnp.bfloat16)
    normed = normalize(residual, attention_gain).astype(jnp.bfloat16)
    height = normed.shape[2]
    frames = clip_count * frame_count
    places = height * column_count
    flat = normed.reshape(frames * places, channels)
    packed = (
        jnp.dot(flat, triple_weight[:, channels:], preferred_element_type=jnp.float32)
        + triple_bias[channels:]
    ).reshape(frames, places, 2 * channels)
    key_vectors = packed[:, :, :channels]
    values = packed[:, :, channels:].astype(jnp.bfloat16)
    start = lax.axis_index("rows") * row_count
    mine = lax.dynamic_slice_in_dim(normed, start, row_count, axis=2)
    queries = (
        jnp.dot(
            mine.reshape(-1, channels), triple_weight[:, :channels],
            preferred_element_type=jnp.float32,
        )
        + triple_bias[:channels]
    ).reshape(frames, row_count * column_count, channels)
    scores = jnp.einsum(
        "nqc,nkc->nqk", queries, key_vectors, precision=lax.Precision.HIGHEST
    ) / math.sqrt(channels)
    row_max = jnp.max(scores, axis=-1, keepdims=True)
    exponent = jnp.exp(scores - row_max)
    weights = (exponent / jnp.sum(exponent, axis=-1, keepdims=True)).astype(jnp.bfloat16)
    attended = jnp.einsum(
        "nqk,nkc->nqc", weights, values, preferred_element_type=jnp.float32
    ).astype(jnp.bfloat16)
    projected = (
        jnp.dot(attended.reshape(-1, channels), output_weight, preferred_element_type=jnp.float32)
        + output_bias
    ).astype(jnp.bfloat16)
    projected = projected.reshape(clip_count, frame_count, row_count, column_count, channels)
    residual_mine = lax.dynamic_slice_in_dim(residual, start, row_count, axis=2)
    live_mask = (jnp.arange(frame_count, dtype=jnp.int32)[None, :] < counts[:, None]).astype(
        jnp.float32
    )
    summed = residual_mine.astype(jnp.float32) + projected.astype(jnp.float32)
    return (summed * live_mask[:, :, None, None, None]).astype(jnp.bfloat16)


GATHER_LIMIT = 1 << 22


def chosen_body(segment_input, inner_input, *rest):
    gathered = inner_input.size * inner_input.dtype.itemsize * lax.axis_size("rows")
    if gathered <= GATHER_LIMIT:
        return gathered_body(segment_input, inner_input, *rest)
    return body(segment_input, inner_input, *rest)


def solution(mesh):
    placed = (
        P("clips", "tm", "rows", None, None),
        P("clips", "tm", "rows", None, None),
        P("clips", "tm"),
        P(),
        P(),
        P(),
        P(),
        P(),
        P(),
        P(),
        P(),
    )
    return jax.shard_map(
        chosen_body,
        mesh=mesh,
        in_specs=placed,
        out_specs=P("clips", "tm", "rows", None, None),
        check_vma=False,
    )
```

```python
import functools
import math

import jax
import jax.numpy as jnp
from jax import lax
from jax.sharding import PartitionSpec as P
from jax.experimental import pallas as pl
from jax.experimental.pallas import tpu as pltpu

EPSILON = 1e-06


def prefix(part, axis, combine, identity):
    place = lax.axis_index(axis)
    gathered = jax.tree.map(lambda a: lax.all_gather(a, axis), part)
    state = jax.tree.map(lambda a, e: jnp.zeros_like(a) + jnp.asarray(e, a.dtype), part, identity)

    def one(step, state):
        return combine(
            state, jax.tree.map(lambda a: lax.dynamic_index_in_dim(a, step, 0, False), gathered)
        )

    return lax.fori_loop(0, place, one, state)


def as_sent(x):

    def short(part):
        return part.astype(jnp.bfloat16) if part.dtype == jnp.float32 else part

    return jax.tree.map(short, x)


def with_halo(cells, sides, width):
    for axis, dim in sides:
        count = lax.axis_size(axis)
        ends = count - 1
        head = lax.slice_in_dim(cells, 0, width, axis=dim)
        tail = lax.slice_in_dim(cells, cells.shape[dim] - width, cells.shape[dim], axis=dim)
        cells = jnp.concatenate(
            [
                lax.ppermute(tail, axis, [(i, (i + 1) % count) for i in range(ends)]),
                cells,
                lax.ppermute(head, axis, [((i + 1) % count, i) for i in range(ends)]),
            ],
            axis=dim,
        )
    return cells


def normalize(field, gain):
    widened = field.astype(jnp.float32)
    return widened * lax.rsqrt(jnp.mean(widened * widened, axis=-1, keepdims=True) + EPSILON) * gain


def last_two(extended, counts):
    slot_total = extended.shape[1]
    chosen = []
    for position in range(2):
        target = counts + position
        picked = jnp.zeros_like(extended[:, 0])
        for slot_index in range(slot_total):
            matches = (target == slot_index)[:, None, None, None]
            picked = jnp.where(matches, extended[:, slot_index], picked)
        chosen.append(picked)
    return jnp.stack(chosen, axis=1)


def summarize(activated, counts):
    blanks = jnp.zeros((activated.shape[0], 2) + activated.shape[2:], activated.dtype)
    summary = last_two(jnp.concatenate([blanks, activated], axis=1), counts)
    return (summary, jnp.minimum(counts, 2).astype(jnp.bfloat16))


def join_later(earlier, later):
    early_frames, early_count = earlier
    late_frames, late_count = later
    complete = (late_count > 1.5)[:, None, None, None, None]
    single = (late_count > 0.5)[:, None, None, None, None]
    shifted = jnp.concatenate([early_frames[:, 1:], late_frames[:, 1:]], axis=1)
    frames = jnp.where(complete, late_frames, jnp.where(single, shifted, early_frames))
    total_count = jnp.minimum(early_count + late_count, 2.0).astype(early_count.dtype)
    return (frames, total_count)


def incoming_cache(summary, counts):
    starting = (jnp.zeros_like(summary), jnp.zeros_like(counts))
    combined = prefix((summary, counts), "tm", join_later, starting)
    return combined[0]


def convolve(padded, causal_weight, causal_bias):
    clip_count, slot_total, rows_padded, column_count, channels = padded.shape
    frame_count = slot_total - 2
    row_count = rows_padded - 2
    widened = jnp.pad(padded, ((0, 0), (0, 0), (0, 0), (1, 1), (0, 0)))
    summed = jnp.zeros((clip_count * frame_count * row_count * column_count, channels), jnp.float32)
    for delta_time in range(3):
        for delta_row in range(3):
            window = widened[
                :, delta_time : delta_time + frame_count, delta_row : delta_row + row_count
            ]
            columns = jnp.concatenate(
                [window[:, :, :, delta_col : delta_col + column_count] for delta_col in range(3)],
                axis=-1,
            )
            kernel = causal_weight[delta_time, delta_row].reshape(3 * channels, channels)
            summed = summed + jnp.dot(
                columns.reshape(-1, 3 * channels), kernel, preferred_element_type=jnp.float32
            )
    return summed.reshape(clip_count, frame_count, row_count, column_count, channels) + causal_bias


def attend(normed, triple_weight, triple_bias, output_weight, output_bias):
    frame_count, places, channels = normed.shape
    packed = (
        jnp.dot(normed.reshape(-1, channels), triple_weight, preferred_element_type=jnp.float32)
        + triple_bias
    )
    packed = packed.reshape(frame_count, places, 3 * channels)
    queries = packed[:, :, :channels]
    key_vectors = packed[:, :, channels : 2 * channels]
    values = packed[:, :, 2 * channels :].astype(jnp.bfloat16)
    scores = jnp.einsum(
        "nqc,nkc->nqk", queries, key_vectors, precision=lax.Precision.HIGHEST
    ) / math.sqrt(channels)
    row_max = jnp.max(scores, axis=-1, keepdims=True)
    exponent = jnp.exp(scores - row_max)
    weights = (exponent / jnp.sum(exponent, axis=-1, keepdims=True)).astype(jnp.bfloat16)
    attended = jnp.einsum(
        "nqk,nkc->nqc", weights, values, preferred_element_type=jnp.float32
    ).astype(jnp.bfloat16)
    projected = (
        jnp.dot(attended.reshape(-1, channels), output_weight, preferred_element_type=jnp.float32)
        + output_bias
    )
    return projected.reshape(frame_count, places, channels).astype(jnp.bfloat16)


def body(
    segment_input,
    inner_input,
    lengths,
    inner_gain,
    causal_weight,
    causal_bias,
    attention_gain,
    triple_weight,
    triple_bias,
    output_weight,
    output_bias,
):
    clip_count, frame_count, row_count, column_count, channels = segment_input.shape
    activated = jax.nn.silu(normalize(inner_input, inner_gain)).astype(jnp.bfloat16)
    counts = lengths[:, 0]
    live_mask = (jnp.arange(frame_count, dtype=jnp.int32)[None, :] < counts[:, None]).astype(
        jnp.float32
    )
    carried = incoming_cache(*summarize(activated, counts))
    extended = jnp.concatenate([carried, activated], axis=1)
    padded = with_halo(as_sent(extended), (("rows", 2),), 1).astype(extended.dtype)
    convolved = convolve(padded, causal_weight, causal_bias)
    residual = (segment_input.astype(jnp.float32) + convolved).astype(jnp.bfloat16)
    residual = lax.optimization_barrier(residual)
    normed = normalize(residual, attention_gain).astype(jnp.bfloat16)
    row_devices = lax.axis_size("rows")
    per_device = clip_count * frame_count // row_devices
    grouped = normed.reshape(row_devices, per_device, row_count, column_count, channels)
    portion = lax.all_to_all(grouped, "rows", split_axis=0, concat_axis=2, tiled=True)
    owned = portion.shape[1]
    height = portion.shape[2]
    flat = portion.reshape(owned, height * column_count, channels)
    result = attend(flat, triple_weight, triple_bias, output_weight, output_bias)
    result = result.reshape(1, owned, height, column_count, channels)
    projected = lax.all_to_all(result, "rows", split_axis=2, concat_axis=0, tiled=True)
    projected = projected.reshape(clip_count, frame_count, row_count, column_count, channels)
    projected = lax.optimization_barrier(projected)
    summed = residual.astype(jnp.float32) + projected.astype(jnp.float32)
    return (summed * live_mask[:, :, None, None, None]).astype(jnp.bfloat16)


def activate(field, gain):
    return jax.nn.silu(normalize(field, gain)).astype(jnp.bfloat16)


def conv_part_kernel(plan, first_tap, x_ref, w_hbm, o_ref, w_vmem, sems):
    clips, held, rows, columns, width = x_ref.shape
    height = rows - 2
    places = height * columns
    channels = w_vmem.shape[-1]
    copies = []
    for index in range(len(plan)):
        for kh in range(3):
            slot_index = index * 3 + kh
            copy = pltpu.make_async_copy(
                w_hbm.at[first_tap + index, kh], w_vmem.at[slot_index], sems.at[slot_index]
            )
            copy.start()
            copies.append(copy)
    written = set()
    for index, (frame, slot, count) in enumerate(plan):
        for kh in range(3):
            slot_index = index * 3 + kh
            copies[slot_index].wait()
            weight = w_vmem[slot_index].reshape(width, channels)
            lhs = x_ref[:, frame : frame + count, kh : kh + height, :, :]
            lhs = lhs.reshape(clips * count * places, width)
            term = jnp.dot(lhs, weight, preferred_element_type=jnp.float32)
            term = term.reshape(clips, count, places, channels)
            for part in range(count):
                target = slot + part
                if target in written:
                    o_ref[:, target] += term[:, part]
                else:
                    o_ref[:, target] = term[:, part]
                    written.add(target)


def conv_part(frames, causal_weight, plan, first_tap, slots):
    clips, held, height, columns, channels = frames.shape
    padded = jnp.pad(frames, ((0, 0), (0, 0), (1, 1), (1, 1), (0, 0)))
    taps = jnp.concatenate(
        [padded[:, :, :, kw : kw + columns] for kw in range(3)], axis=-1
    )
    places = height * columns
    dots = sum(count for _, _, count in plan) * 3
    blocks = len(plan) * 3
    return pl.pallas_call(
        functools.partial(conv_part_kernel, plan, first_tap),
        in_specs=[
            pl.BlockSpec(memory_space=pltpu.VMEM),
            pl.BlockSpec(memory_space=pl.ANY),
        ],
        out_specs=pl.BlockSpec(memory_space=pltpu.VMEM),
        out_shape=jax.ShapeDtypeStruct((clips, slots, places, channels), jnp.float32),
        scratch_shapes=[
            pltpu.VMEM((blocks, 3, channels, channels), causal_weight.dtype),
            pltpu.SemaphoreType.DMA((blocks,)),
        ],
        compiler_params=pltpu.CompilerParams(vmem_limit_bytes=48 * 1024 * 1024),
        cost_estimate=pl.CostEstimate(
            flops=2 * clips * places * dots * 3 * channels * channels,
            transcendentals=0,
            bytes_accessed=blocks * 3 * channels * channels * 2
            + taps.size * 2
            + clips * slots * places * channels * 4,
        ),
    )(taps, causal_weight)


def conv_plans(slots):
    own, carried = {}, {}
    for kt in range(3):
        for slot in range(slots):
            source = slot + kt
            if source >= 2:
                own.setdefault(kt, []).append((source - 2, slot))
            else:
                carried.setdefault(kt, []).append((source, slot))
    return own, carried


def plan_of(table):
    taps = sorted(table)
    assert taps == list(range(taps[0], taps[-1] + 1))
    runs = []
    for kt in taps:
        pairs = sorted(table[kt], key=lambda pair: pair[1])
        frame, slot = pairs[0]
        assert pairs == [(frame + k, slot + k) for k in range(len(pairs))]
        runs.append((frame, slot, len(pairs)))
    return tuple(runs), taps[0]


def own_conv(own_frames, causal_weight):
    own_table, _ = conv_plans(own_frames.shape[1])
    own_plan, own_first = plan_of(own_table)
    return conv_part(own_frames, causal_weight, own_plan, own_first, own_frames.shape[1])


def carried_conv(carried_frames, causal_weight, slots):
    _, carried_table = conv_plans(slots)
    carried_plan, carried_first = plan_of(carried_table)
    return conv_part(carried_frames, causal_weight, carried_plan, carried_first, slots)


def frame_major(total, clips, height, columns):
    clips, slots, places, channels = total.shape
    return total.reshape(clips, slots, height, columns, channels)


def gathered_body(
    segment_input,
    inner_input,
    lengths,
    inner_gain,
    causal_weight,
    causal_bias,
    attention_gain,
    triple_weight,
    triple_bias,
    output_weight,
    output_bias,
):
    clip_count, frame_count, row_count, column_count, channels = segment_input.shape
    sections = lax.axis_size("tm")
    counts = lengths[:, 0]
    ahead = [(i, i + 1) for i in range(sections - 1)]
    prev_counts = lax.ppermute(counts, "tm", ahead)
    both = jnp.concatenate([inner_input, segment_input], axis=0)
    both_all = lax.all_gather(both, "rows", axis=2, tiled=True)
    inner_all = both_all[:clip_count]
    segment_all = both_all[clip_count:]
    wide = (counts > 1)[:, None, None, None]
    last_raw = jnp.where(wide, inner_all[:, frame_count - 1], inner_all[:, 0])
    prev_raw = lax.ppermute(inner_all, "tm", ahead)
    own = activate(inner_all, inner_gain)
    own_sum = own_conv(own, causal_weight)
    own_sum, last_raw = lax.optimization_barrier((own_sum, last_raw))
    before_raw = lax.ppermute(last_raw, "tm", [(i, i + 2) for i in range(sections - 2)])
    own_sum, prev_raw, before_raw, prev_counts = lax.optimization_barrier(
        (own_sum, prev_raw, before_raw, prev_counts)
    )
    prev = activate(prev_raw, inner_gain)
    before = activate(before_raw, inner_gain)
    prev_wide = (prev_counts > 1)[:, None, None, None]
    carried = jnp.stack(
        [
            jnp.where(prev_wide, prev[:, frame_count - 2], before),
            jnp.where(prev_wide, prev[:, frame_count - 1], prev[:, 0]),
        ],
        axis=1,
    )
    carried_sum = carried_conv(carried, causal_weight, frame_count)
    height = inner_all.shape[2]
    convolved = frame_major(own_sum + carried_sum, clip_count, height, column_count) + causal_bias
    residual = (segment_all.astype(jnp.float32) + convolved).astype(jnp.bfloat16)
    normed = normalize(residual, attention_gain).astype(jnp.bfloat16)
    height = normed.shape[2]
    frames = clip_count * frame_count
    places = height * column_count
    flat = normed.reshape(frames * places, channels)
    packed = (
        jnp.dot(flat, triple_weight[:, channels:], preferred_element_type=jnp.float32)
        + triple_bias[channels:]
    ).reshape(frames, places, 2 * channels)
    key_vectors = packed[:, :, :channels]
    values = packed[:, :, channels:].astype(jnp.bfloat16)
    start = lax.axis_index("rows") * row_count
    mine = lax.dynamic_slice_in_dim(normed, start, row_count, axis=2)
    queries = (
        jnp.dot(
            mine.reshape(-1, channels), triple_weight[:, :channels],
            preferred_element_type=jnp.float32,
        )
        + triple_bias[:channels]
    ).reshape(frames, row_count * column_count, channels)
    scores = jnp.einsum(
        "nqc,nkc->nqk", queries, key_vectors, precision=lax.Precision.HIGHEST
    ) / math.sqrt(channels)
    row_max = jnp.max(scores, axis=-1, keepdims=True)
    exponent = jnp.exp(scores - row_max)
    weights = (exponent / jnp.sum(exponent, axis=-1, keepdims=True)).astype(jnp.bfloat16)
    attended = jnp.einsum(
        "nqk,nkc->nqc", weights, values, preferred_element_type=jnp.float32
    ).astype(jnp.bfloat16)
    projected = (
        jnp.dot(attended.reshape(-1, channels), output_weight, preferred_element_type=jnp.float32)
        + output_bias
    ).astype(jnp.bfloat16)
    projected = projected.reshape(clip_count, frame_count, row_count, column_count, channels)
    residual_mine = lax.dynamic_slice_in_dim(residual, start, row_count, axis=2)
    live_mask = (jnp.arange(frame_count, dtype=jnp.int32)[None, :] < counts[:, None]).astype(
        jnp.float32
    )
    summed = residual_mine.astype(jnp.float32) + projected.astype(jnp.float32)
    return (summed * live_mask[:, :, None, None, None]).astype(jnp.bfloat16)


GATHER_LIMIT = 1 << 22


def chosen_body(segment_input, inner_input, *rest):
    gathered = inner_input.size * inner_input.dtype.itemsize * lax.axis_size("rows")
    if gathered <= GATHER_LIMIT:
        return gathered_body(segment_input, inner_input, *rest)
    return body(segment_input, inner_input, *rest)


def solution(mesh):
    placed = (
        P("clips", "tm", "rows", None, None),
        P("clips", "tm", "rows", None, None),
        P("clips", "tm"),
        P(),
        P(),
        P(),
        P(),
        P(),
        P(),
        P(),
        P(),
    )
    return jax.shard_map(
        chosen_body,
        mesh=mesh,
        in_specs=placed,
        out_specs=P("clips", "tm", "rows", None, None),
        check_vma=False,
    )
```

```python
import functools
import math

import jax
import jax.numpy as jnp
from jax import lax
from jax.sharding import PartitionSpec as P
from jax.experimental import pallas as pl
from jax.experimental.pallas import tpu as pltpu

EPSILON = 1e-06


def prefix(part, axis, combine, identity):
    place = lax.axis_index(axis)
    gathered = jax.tree.map(lambda a: lax.all_gather(a, axis), part)
    state = jax.tree.map(lambda a, e: jnp.zeros_like(a) + jnp.asarray(e, a.dtype), part, identity)

    def one(step, state):
        return combine(
            state, jax.tree.map(lambda a: lax.dynamic_index_in_dim(a, step, 0, False), gathered)
        )

    return lax.fori_loop(0, place, one, state)


def as_sent(x):

    def short(part):
        return part.astype(jnp.bfloat16) if part.dtype == jnp.float32 else part

    return jax.tree.map(short, x)


def with_halo(cells, sides, width):
    for axis, dim in sides:
        count = lax.axis_size(axis)
        ends = count - 1
        head = lax.slice_in_dim(cells, 0, width, axis=dim)
        tail = lax.slice_in_dim(cells, cells.shape[dim] - width, cells.shape[dim], axis=dim)
        cells = jnp.concatenate(
            [
                lax.ppermute(tail, axis, [(i, (i + 1) % count) for i in range(ends)]),
                cells,
                lax.ppermute(head, axis, [((i + 1) % count, i) for i in range(ends)]),
            ],
            axis=dim,
        )
    return cells


def normalize(field, gain):
    widened = field.astype(jnp.float32)
    return widened * lax.rsqrt(jnp.mean(widened * widened, axis=-1, keepdims=True) + EPSILON) * gain


def last_two(extended, counts):
    slot_total = extended.shape[1]
    chosen = []
    for position in range(2):
        target = counts + position
        picked = jnp.zeros_like(extended[:, 0])
        for slot_index in range(slot_total):
            matches = (target == slot_index)[:, None, None, None]
            picked = jnp.where(matches, extended[:, slot_index], picked)
        chosen.append(picked)
    return jnp.stack(chosen, axis=1)


def summarize(activated, counts):
    blanks = jnp.zeros((activated.shape[0], 2) + activated.shape[2:], activated.dtype)
    summary = last_two(jnp.concatenate([blanks, activated], axis=1), counts)
    return (summary, jnp.minimum(counts, 2).astype(jnp.bfloat16))


def join_later(earlier, later):
    early_frames, early_count = earlier
    late_frames, late_count = later
    complete = (late_count > 1.5)[:, None, None, None, None]
    single = (late_count > 0.5)[:, None, None, None, None]
    shifted = jnp.concatenate([early_frames[:, 1:], late_frames[:, 1:]], axis=1)
    frames = jnp.where(complete, late_frames, jnp.where(single, shifted, early_frames))
    total_count = jnp.minimum(early_count + late_count, 2.0).astype(early_count.dtype)
    return (frames, total_count)


def incoming_cache(summary, counts):
    starting = (jnp.zeros_like(summary), jnp.zeros_like(counts))
    combined = prefix((summary, counts), "tm", join_later, starting)
    return combined[0]


def convolve(padded, causal_weight, causal_bias):
    clip_count, slot_total, rows_padded, column_count, channels = padded.shape
    frame_count = slot_total - 2
    row_count = rows_padded - 2
    widened = jnp.pad(padded, ((0, 0), (0, 0), (0, 0), (1, 1), (0, 0)))
    summed = jnp.zeros((clip_count * frame_count * row_count * column_count, channels), jnp.float32)
    for delta_time in range(3):
        for delta_row in range(3):
            window = widened[
                :, delta_time : delta_time + frame_count, delta_row : delta_row + row_count
            ]
            columns = jnp.concatenate(
                [window[:, :, :, delta_col : delta_col + column_count] for delta_col in range(3)],
                axis=-1,
            )
            kernel = causal_weight[delta_time, delta_row].reshape(3 * channels, channels)
            summed = summed + jnp.dot(
                columns.reshape(-1, 3 * channels), kernel, preferred_element_type=jnp.float32
            )
    return summed.reshape(clip_count, frame_count, row_count, column_count, channels) + causal_bias


def attend(normed, triple_weight, triple_bias, output_weight, output_bias):
    frame_count, places, channels = normed.shape
    packed = (
        jnp.dot(normed.reshape(-1, channels), triple_weight, preferred_element_type=jnp.float32)
        + triple_bias
    )
    packed = packed.reshape(frame_count, places, 3 * channels)
    queries = packed[:, :, :channels]
    key_vectors = packed[:, :, channels : 2 * channels]
    values = packed[:, :, 2 * channels :].astype(jnp.bfloat16)
    scores = jnp.einsum(
        "nqc,nkc->nqk", queries, key_vectors, precision=lax.Precision.HIGHEST
    ) / math.sqrt(channels)
    row_max = jnp.max(scores, axis=-1, keepdims=True)
    exponent = jnp.exp(scores - row_max)
    weights = (exponent / jnp.sum(exponent, axis=-1, keepdims=True)).astype(jnp.bfloat16)
    attended = jnp.einsum(
        "nqk,nkc->nqc", weights, values, preferred_element_type=jnp.float32
    ).astype(jnp.bfloat16)
    projected = (
        jnp.dot(attended.reshape(-1, channels), output_weight, preferred_element_type=jnp.float32)
        + output_bias
    )
    return projected.reshape(frame_count, places, channels).astype(jnp.bfloat16)


def body(
    segment_input,
    inner_input,
    lengths,
    inner_gain,
    causal_weight,
    causal_bias,
    attention_gain,
    triple_weight,
    triple_bias,
    output_weight,
    output_bias,
):
    clip_count, frame_count, row_count, column_count, channels = segment_input.shape
    activated = jax.nn.silu(normalize(inner_input, inner_gain)).astype(jnp.bfloat16)
    counts = lengths[:, 0]
    live_mask = (jnp.arange(frame_count, dtype=jnp.int32)[None, :] < counts[:, None]).astype(
        jnp.float32
    )
    carried = incoming_cache(*summarize(activated, counts))
    extended = jnp.concatenate([carried, activated], axis=1)
    padded = with_halo(as_sent(extended), (("rows", 2),), 1).astype(extended.dtype)
    convolved = convolve(padded, causal_weight, causal_bias)
    residual = (segment_input.astype(jnp.float32) + convolved).astype(jnp.bfloat16)
    residual = lax.optimization_barrier(residual)
    normed = normalize(residual, attention_gain).astype(jnp.bfloat16)
    row_devices = lax.axis_size("rows")
    per_device = clip_count * frame_count // row_devices
    grouped = normed.reshape(row_devices, per_device, row_count, column_count, channels)
    portion = lax.all_to_all(grouped, "rows", split_axis=0, concat_axis=2, tiled=True)
    owned = portion.shape[1]
    height = portion.shape[2]
    flat = portion.reshape(owned, height * column_count, channels)
    result = attend(flat, triple_weight, triple_bias, output_weight, output_bias)
    result = result.reshape(1, owned, height, column_count, channels)
    projected = lax.all_to_all(result, "rows", split_axis=2, concat_axis=0, tiled=True)
    projected = projected.reshape(clip_count, frame_count, row_count, column_count, channels)
    projected = lax.optimization_barrier(projected)
    summed = residual.astype(jnp.float32) + projected.astype(jnp.float32)
    return (summed * live_mask[:, :, None, None, None]).astype(jnp.bfloat16)


def activate(field, gain):
    return jax.nn.silu(normalize(field, gain)).astype(jnp.bfloat16)


def conv_part_kernel(plan, first_tap, x_ref, w_hbm, o_ref, w_vmem, sems):
    clips, held, rows, columns, width = x_ref.shape
    height = rows - 2
    places = height * columns
    channels = w_vmem.shape[-1]
    copies = []
    for index in range(len(plan)):
        for kh in range(3):
            slot_index = index * 3 + kh
            copy = pltpu.make_async_copy(
                w_hbm.at[first_tap + index, kh], w_vmem.at[slot_index], sems.at[slot_index]
            )
            copy.start()
            copies.append(copy)
    written = set()
    for index, (frame, slot, count) in enumerate(plan):
        for kh in range(3):
            slot_index = index * 3 + kh
            copies[slot_index].wait()
            weight = w_vmem[slot_index].reshape(width, channels)
            lhs = x_ref[:, frame : frame + count, kh : kh + height, :, :]
            lhs = lhs.reshape(clips * count * places, width)
            term = jnp.dot(lhs, weight, preferred_element_type=jnp.float32)
            term = term.reshape(clips, count, places, channels)
            for part in range(count):
                target = slot + part
                if target in written:
                    o_ref[:, target] += term[:, part]
                else:
                    o_ref[:, target] = term[:, part]
                    written.add(target)


def conv_part(frames, causal_weight, plan, first_tap, slots):
    clips, held, height, columns, channels = frames.shape
    padded = jnp.pad(frames, ((0, 0), (0, 0), (1, 1), (1, 1), (0, 0)))
    taps = jnp.concatenate(
        [padded[:, :, :, kw : kw + columns] for kw in range(3)], axis=-1
    )
    places = height * columns
    dots = sum(count for _, _, count in plan) * 3
    blocks = len(plan) * 3
    return pl.pallas_call(
        functools.partial(conv_part_kernel, plan, first_tap),
        in_specs=[
            pl.BlockSpec(memory_space=pltpu.VMEM),
            pl.BlockSpec(memory_space=pl.ANY),
        ],
        out_specs=pl.BlockSpec(memory_space=pltpu.VMEM),
        out_shape=jax.ShapeDtypeStruct((clips, slots, places, channels), jnp.float32),
        scratch_shapes=[
            pltpu.VMEM((blocks, 3, channels, channels), causal_weight.dtype),
            pltpu.SemaphoreType.DMA((blocks,)),
        ],
        compiler_params=pltpu.CompilerParams(vmem_limit_bytes=48 * 1024 * 1024),
        cost_estimate=pl.CostEstimate(
            flops=2 * clips * places * dots * 3 * channels * channels,
            transcendentals=0,
            bytes_accessed=blocks * 3 * channels * channels * 2
            + taps.size * 2
            + clips * slots * places * channels * 4,
        ),
    )(taps, causal_weight)


def conv_plans(slots):
    own, carried = {}, {}
    for kt in range(3):
        for slot in range(slots):
            source = slot + kt
            if source >= 2:
                own.setdefault(kt, []).append((source - 2, slot))
            else:
                carried.setdefault(kt, []).append((source, slot))
    return own, carried


def plan_of(table):
    taps = sorted(table)
    assert taps == list(range(taps[0], taps[-1] + 1))
    runs = []
    for kt in taps:
        pairs = sorted(table[kt], key=lambda pair: pair[1])
        frame, slot = pairs[0]
        assert pairs == [(frame + k, slot + k) for k in range(len(pairs))]
        runs.append((frame, slot, len(pairs)))
    return tuple(runs), taps[0]


def own_conv(own_frames, causal_weight):
    own_table, _ = conv_plans(own_frames.shape[1])
    own_plan, own_first = plan_of(own_table)
    return conv_part(own_frames, causal_weight, own_plan, own_first, own_frames.shape[1])


def carried_conv(carried_frames, causal_weight, slots):
    _, carried_table = conv_plans(slots)
    carried_plan, carried_first = plan_of(carried_table)
    return conv_part(carried_frames, causal_weight, carried_plan, carried_first, slots)


def frame_major(total, clips, height, columns):
    clips, slots, places, channels = total.shape
    return total.reshape(clips, slots, height, columns, channels)


def gathered_body(
    segment_input,
    inner_input,
    lengths,
    inner_gain,
    causal_weight,
    causal_bias,
    attention_gain,
    triple_weight,
    triple_bias,
    output_weight,
    output_bias,
):
    clip_count, frame_count, row_count, column_count, channels = segment_input.shape
    sections = lax.axis_size("tm")
    counts = lengths[:, 0]
    ahead = [(i, i + 1) for i in range(sections - 1)]
    prev_counts = lax.ppermute(counts, "tm", ahead)
    both = jnp.concatenate([inner_input, segment_input], axis=0)
    both_all = lax.all_gather(both, "rows", axis=3, tiled=True)
    both_all = both_all.reshape(2 * clip_count, frame_count, -1, column_count, channels)
    inner_all = both_all[:clip_count]
    segment_all = both_all[clip_count:]
    wide = (counts > 1)[:, None, None, None]
    last_raw = jnp.where(wide, inner_all[:, frame_count - 1], inner_all[:, 0])
    prev_raw = lax.ppermute(inner_all, "tm", ahead)
    before_raw = lax.ppermute(last_raw, "tm", [(i, i + 2) for i in range(sections - 2)])
    own = activate(inner_all, inner_gain)
    own_sum = own_conv(own, causal_weight)
    own_sum, prev_raw, before_raw, prev_counts = lax.optimization_barrier(
        (own_sum, prev_raw, before_raw, prev_counts)
    )
    prev = activate(prev_raw, inner_gain)
    before = activate(before_raw, inner_gain)
    prev_wide = (prev_counts > 1)[:, None, None, None]
    carried = jnp.stack(
        [
            jnp.where(prev_wide, prev[:, frame_count - 2], before),
            jnp.where(prev_wide, prev[:, frame_count - 1], prev[:, 0]),
        ],
        axis=1,
    )
    carried_sum = carried_conv(carried, causal_weight, frame_count)
    height = inner_all.shape[2]
    convolved = frame_major(own_sum + carried_sum, clip_count, height, column_count) + causal_bias
    residual = (segment_all.astype(jnp.float32) + convolved).astype(jnp.bfloat16)
    normed = normalize(residual, attention_gain).astype(jnp.bfloat16)
    height = normed.shape[2]
    frames = clip_count * frame_count
    places = height * column_count
    flat = normed.reshape(frames * places, channels)
    packed = (
        jnp.dot(flat, triple_weight[:, channels:], preferred_element_type=jnp.float32)
        + triple_bias[channels:]
    ).reshape(frames, places, 2 * channels)
    key_vectors = packed[:, :, :channels]
    values = packed[:, :, channels:].astype(jnp.bfloat16)
    start = lax.axis_index("rows") * row_count
    mine = lax.dynamic_slice_in_dim(normed, start, row_count, axis=2)
    queries = (
        jnp.dot(
            mine.reshape(-1, channels), triple_weight[:, :channels],
            preferred_element_type=jnp.float32,
        )
        + triple_bias[:channels]
    ).reshape(frames, row_count * column_count, channels)
    scores = jnp.einsum(
        "nqc,nkc->nqk", queries, key_vectors, precision=lax.Precision.HIGHEST
    ) / math.sqrt(channels)
    row_max = jnp.max(scores, axis=-1, keepdims=True)
    exponent = jnp.exp(scores - row_max)
    weights = (exponent / jnp.sum(exponent, axis=-1, keepdims=True)).astype(jnp.bfloat16)
    attended = jnp.einsum(
        "nqk,nkc->nqc", weights, values, preferred_element_type=jnp.float32
    ).astype(jnp.bfloat16)
    projected = (
        jnp.dot(attended.reshape(-1, channels), output_weight, preferred_element_type=jnp.float32)
        + output_bias
    ).astype(jnp.bfloat16)
    projected = projected.reshape(clip_count, frame_count, row_count, column_count, channels)
    residual_mine = lax.dynamic_slice_in_dim(residual, start, row_count, axis=2)
    live_mask = (jnp.arange(frame_count, dtype=jnp.int32)[None, :] < counts[:, None]).astype(
        jnp.float32
    )
    summed = residual_mine.astype(jnp.float32) + projected.astype(jnp.float32)
    return (summed * live_mask[:, :, None, None, None]).astype(jnp.bfloat16)


GATHER_LIMIT = 1 << 22


def chosen_body(segment_input, inner_input, *rest):
    gathered = inner_input.size * inner_input.dtype.itemsize * lax.axis_size("rows")
    if gathered <= GATHER_LIMIT:
        return gathered_body(segment_input, inner_input, *rest)
    return body(segment_input, inner_input, *rest)


def solution(mesh):
    placed = (
        P("clips", "tm", "rows", None, None),
        P("clips", "tm", "rows", None, None),
        P("clips", "tm"),
        P(),
        P(),
        P(),
        P(),
        P(),
        P(),
        P(),
        P(),
    )
    return jax.shard_map(
        chosen_body,
        mesh=mesh,
        in_specs=placed,
        out_specs=P("clips", "tm", "rows", None, None),
        check_vma=False,
    )
```

```python
import functools
import math

import jax
import jax.numpy as jnp
from jax import lax
from jax.sharding import PartitionSpec as P
from jax.experimental import pallas as pl
from jax.experimental.pallas import tpu as pltpu

EPSILON = 1e-06


def prefix(part, axis, combine, identity):
    place = lax.axis_index(axis)
    gathered = jax.tree.map(lambda a: lax.all_gather(a, axis), part)
    state = jax.tree.map(lambda a, e: jnp.zeros_like(a) + jnp.asarray(e, a.dtype), part, identity)

    def one(step, state):
        return combine(
            state, jax.tree.map(lambda a: lax.dynamic_index_in_dim(a, step, 0, False), gathered)
        )

    return lax.fori_loop(0, place, one, state)


def as_sent(x):

    def short(part):
        return part.astype(jnp.bfloat16) if part.dtype == jnp.float32 else part

    return jax.tree.map(short, x)


def with_halo(cells, sides, width):
    for axis, dim in sides:
        count = lax.axis_size(axis)
        ends = count - 1
        head = lax.slice_in_dim(cells, 0, width, axis=dim)
        tail = lax.slice_in_dim(cells, cells.shape[dim] - width, cells.shape[dim], axis=dim)
        cells = jnp.concatenate(
            [
                lax.ppermute(tail, axis, [(i, (i + 1) % count) for i in range(ends)]),
                cells,
                lax.ppermute(head, axis, [((i + 1) % count, i) for i in range(ends)]),
            ],
            axis=dim,
        )
    return cells


def normalize(field, gain):
    widened = field.astype(jnp.float32)
    return widened * lax.rsqrt(jnp.mean(widened * widened, axis=-1, keepdims=True) + EPSILON) * gain


def last_two(extended, counts):
    slot_total = extended.shape[1]
    chosen = []
    for position in range(2):
        target = counts + position
        picked = jnp.zeros_like(extended[:, 0])
        for slot_index in range(slot_total):
            matches = (target == slot_index)[:, None, None, None]
            picked = jnp.where(matches, extended[:, slot_index], picked)
        chosen.append(picked)
    return jnp.stack(chosen, axis=1)


def summarize(activated, counts):
    blanks = jnp.zeros((activated.shape[0], 2) + activated.shape[2:], activated.dtype)
    summary = last_two(jnp.concatenate([blanks, activated], axis=1), counts)
    return (summary, jnp.minimum(counts, 2).astype(jnp.bfloat16))


def join_later(earlier, later):
    early_frames, early_count = earlier
    late_frames, late_count = later
    complete = (late_count > 1.5)[:, None, None, None, None]
    single = (late_count > 0.5)[:, None, None, None, None]
    shifted = jnp.concatenate([early_frames[:, 1:], late_frames[:, 1:]], axis=1)
    frames = jnp.where(complete, late_frames, jnp.where(single, shifted, early_frames))
    total_count = jnp.minimum(early_count + late_count, 2.0).astype(early_count.dtype)
    return (frames, total_count)


def incoming_cache(summary, counts):
    starting = (jnp.zeros_like(summary), jnp.zeros_like(counts))
    combined = prefix((summary, counts), "tm", join_later, starting)
    return combined[0]


def convolve(padded, causal_weight, causal_bias):
    clip_count, slot_total, rows_padded, column_count, channels = padded.shape
    frame_count = slot_total - 2
    row_count = rows_padded - 2
    widened = jnp.pad(padded, ((0, 0), (0, 0), (0, 0), (1, 1), (0, 0)))
    summed = jnp.zeros((clip_count * frame_count * row_count * column_count, channels), jnp.float32)
    for delta_time in range(3):
        for delta_row in range(3):
            window = widened[
                :, delta_time : delta_time + frame_count, delta_row : delta_row + row_count
            ]
            columns = jnp.concatenate(
                [window[:, :, :, delta_col : delta_col + column_count] for delta_col in range(3)],
                axis=-1,
            )
            kernel = causal_weight[delta_time, delta_row].reshape(3 * channels, channels)
            summed = summed + jnp.dot(
                columns.reshape(-1, 3 * channels), kernel, preferred_element_type=jnp.float32
            )
    return summed.reshape(clip_count, frame_count, row_count, column_count, channels) + causal_bias


def attend(normed, triple_weight, triple_bias, output_weight, output_bias):
    frame_count, places, channels = normed.shape
    packed = (
        jnp.dot(normed.reshape(-1, channels), triple_weight, preferred_element_type=jnp.float32)
        + triple_bias
    )
    packed = packed.reshape(frame_count, places, 3 * channels)
    queries = packed[:, :, :channels]
    key_vectors = packed[:, :, channels : 2 * channels]
    values = packed[:, :, 2 * channels :].astype(jnp.bfloat16)
    scores = jnp.einsum(
        "nqc,nkc->nqk", queries, key_vectors, precision=lax.Precision.HIGHEST
    ) / math.sqrt(channels)
    row_max = jnp.max(scores, axis=-1, keepdims=True)
    exponent = jnp.exp(scores - row_max)
    weights = (exponent / jnp.sum(exponent, axis=-1, keepdims=True)).astype(jnp.bfloat16)
    attended = jnp.einsum(
        "nqk,nkc->nqc", weights, values, preferred_element_type=jnp.float32
    ).astype(jnp.bfloat16)
    projected = (
        jnp.dot(attended.reshape(-1, channels), output_weight, preferred_element_type=jnp.float32)
        + output_bias
    )
    return projected.reshape(frame_count, places, channels).astype(jnp.bfloat16)


def body(
    segment_input,
    inner_input,
    lengths,
    inner_gain,
    causal_weight,
    causal_bias,
    attention_gain,
    triple_weight,
    triple_bias,
    output_weight,
    output_bias,
):
    clip_count, frame_count, row_count, column_count, channels = segment_input.shape
    activated = jax.nn.silu(normalize(inner_input, inner_gain)).astype(jnp.bfloat16)
    counts = lengths[:, 0]
    live_mask = (jnp.arange(frame_count, dtype=jnp.int32)[None, :] < counts[:, None]).astype(
        jnp.float32
    )
    carried = incoming_cache(*summarize(activated, counts))
    extended = jnp.concatenate([carried, activated], axis=1)
    padded = with_halo(as_sent(extended), (("rows", 2),), 1).astype(extended.dtype)
    convolved = convolve(padded, causal_weight, causal_bias)
    residual = (segment_input.astype(jnp.float32) + convolved).astype(jnp.bfloat16)
    residual = lax.optimization_barrier(residual)
    normed = normalize(residual, attention_gain).astype(jnp.bfloat16)
    row_devices = lax.axis_size("rows")
    per_device = clip_count * frame_count // row_devices
    grouped = normed.reshape(row_devices, per_device, row_count, column_count, channels)
    portion = lax.all_to_all(grouped, "rows", split_axis=0, concat_axis=2, tiled=True)
    owned = portion.shape[1]
    height = portion.shape[2]
    flat = portion.reshape(owned, height * column_count, channels)
    result = attend(flat, triple_weight, triple_bias, output_weight, output_bias)
    result = result.reshape(1, owned, height, column_count, channels)
    projected = lax.all_to_all(result, "rows", split_axis=2, concat_axis=0, tiled=True)
    projected = projected.reshape(clip_count, frame_count, row_count, column_count, channels)
    projected = lax.optimization_barrier(projected)
    summed = residual.astype(jnp.float32) + projected.astype(jnp.float32)
    return (summed * live_mask[:, :, None, None, None]).astype(jnp.bfloat16)


def activate(field, gain):
    return jax.nn.silu(normalize(field, gain)).astype(jnp.bfloat16)


def conv_part_kernel(plan, first_tap, x_ref, w_hbm, o_ref, w_vmem, sems):
    clips, held, rows, columns, width = x_ref.shape
    height = rows - 2
    places = height * columns
    channels = w_vmem.shape[-1]
    copies = []
    for index in range(len(plan)):
        for kh in range(3):
            slot_index = index * 3 + kh
            copy = pltpu.make_async_copy(
                w_hbm.at[first_tap + index, kh], w_vmem.at[slot_index], sems.at[slot_index]
            )
            copy.start()
            copies.append(copy)
    written = set()
    for index, (frame, slot, count) in enumerate(plan):
        for kh in range(3):
            slot_index = index * 3 + kh
            copies[slot_index].wait()
            weight = w_vmem[slot_index].reshape(width, channels)
            lhs = x_ref[:, frame : frame + count, kh : kh + height, :, :]
            lhs = lhs.reshape(clips * count * places, width)
            term = jnp.dot(lhs, weight, preferred_element_type=jnp.float32)
            term = term.reshape(clips, count, places, channels)
            for part in range(count):
                target = slot + part
                if target in written:
                    o_ref[:, target] += term[:, part]
                else:
                    o_ref[:, target] = term[:, part]
                    written.add(target)


def conv_part(frames, causal_weight, plan, first_tap, slots):
    clips, held, height, columns, channels = frames.shape
    padded = jnp.pad(frames, ((0, 0), (0, 0), (1, 1), (1, 1), (0, 0)))
    taps = jnp.concatenate(
        [padded[:, :, :, kw : kw + columns] for kw in range(3)], axis=-1
    )
    places = height * columns
    dots = sum(count for _, _, count in plan) * 3
    blocks = len(plan) * 3
    return pl.pallas_call(
        functools.partial(conv_part_kernel, plan, first_tap),
        in_specs=[
            pl.BlockSpec(memory_space=pltpu.VMEM),
            pl.BlockSpec(memory_space=pl.ANY),
        ],
        out_specs=pl.BlockSpec(memory_space=pltpu.VMEM),
        out_shape=jax.ShapeDtypeStruct((clips, slots, places, channels), jnp.float32),
        scratch_shapes=[
            pltpu.VMEM((blocks, 3, channels, channels), causal_weight.dtype),
            pltpu.SemaphoreType.DMA((blocks,)),
        ],
        compiler_params=pltpu.CompilerParams(vmem_limit_bytes=48 * 1024 * 1024),
        cost_estimate=pl.CostEstimate(
            flops=2 * clips * places * dots * 3 * channels * channels,
            transcendentals=0,
            bytes_accessed=blocks * 3 * channels * channels * 2
            + taps.size * 2
            + clips * slots * places * channels * 4,
        ),
    )(taps, causal_weight)


def conv_plans(slots):
    own, carried = {}, {}
    for kt in range(3):
        for slot in range(slots):
            source = slot + kt
            if source >= 2:
                own.setdefault(kt, []).append((source - 2, slot))
            else:
                carried.setdefault(kt, []).append((source, slot))
    return own, carried


def plan_of(table):
    taps = sorted(table)
    assert taps == list(range(taps[0], taps[-1] + 1))
    runs = []
    for kt in taps:
        pairs = sorted(table[kt], key=lambda pair: pair[1])
        frame, slot = pairs[0]
        assert pairs == [(frame + k, slot + k) for k in range(len(pairs))]
        runs.append((frame, slot, len(pairs)))
    return tuple(runs), taps[0]


def own_conv(own_frames, causal_weight):
    own_table, _ = conv_plans(own_frames.shape[1])
    own_plan, own_first = plan_of(own_table)
    return conv_part(own_frames, causal_weight, own_plan, own_first, own_frames.shape[1])


def carried_conv(carried_frames, causal_weight, slots):
    _, carried_table = conv_plans(slots)
    carried_plan, carried_first = plan_of(carried_table)
    return conv_part(carried_frames, causal_weight, carried_plan, carried_first, slots)


def frame_major(total, clips, height, columns):
    clips, slots, places, channels = total.shape
    return total.reshape(clips, slots, height, columns, channels)


def attend_kernel(res_ref, mine_ref, mask_ref, gain_ref, wkv_ref, bkv_ref, wq_ref, bq_ref,
                  wo_ref, bo_ref, o_ref):
    frames, places, channels = res_ref.shape
    gain = gain_ref[...]
    for n in range(frames):
        wide = res_ref[n].astype(jnp.float32)
        scale = lax.rsqrt(jnp.mean(wide * wide, axis=-1, keepdims=True) + EPSILON)
        normed = (wide * scale * gain).astype(jnp.bfloat16)
        packed = (
            jnp.dot(normed, wkv_ref[...], preferred_element_type=jnp.float32) + bkv_ref[...]
        )
        key_vectors = packed[:, :channels]
        values = packed[:, channels:].astype(jnp.bfloat16)
        own = mine_ref[n].astype(jnp.float32)
        own_scale = lax.rsqrt(jnp.mean(own * own, axis=-1, keepdims=True) + EPSILON)
        own_normed = (own * own_scale * gain).astype(jnp.bfloat16)
        queries = (
            jnp.dot(own_normed, wq_ref[...], preferred_element_type=jnp.float32) + bq_ref[...]
        )
        scores = lax.dot_general(
            queries, key_vectors, (((1,), (1,)), ((), ())),
            precision=lax.Precision.HIGHEST, preferred_element_type=jnp.float32,
        ) / math.sqrt(channels)
        row_max = jnp.max(scores, axis=-1, keepdims=True)
        exponent = jnp.exp(scores - row_max)
        weights = (exponent / jnp.sum(exponent, axis=-1, keepdims=True)).astype(jnp.bfloat16)
        attended = jnp.dot(weights, values, preferred_element_type=jnp.float32).astype(
            jnp.bfloat16
        )
        projected = (
            jnp.dot(attended, wo_ref[...], preferred_element_type=jnp.float32) + bo_ref[...]
        ).astype(jnp.bfloat16)
        summed = own + projected.astype(jnp.float32)
        o_ref[n] = (summed * mask_ref[n]).astype(o_ref.dtype)


def attend_local(residual, mine, mask, attention_gain, triple_weight, triple_bias,
                 output_weight, output_bias):
    frames, places, channels = residual.shape
    own_places = mine.shape[1]
    vmem = pl.BlockSpec(memory_space=pltpu.VMEM)
    return pl.pallas_call(
        attend_kernel,
        in_specs=[vmem] * 10,
        out_specs=vmem,
        out_shape=jax.ShapeDtypeStruct((frames, own_places, channels), jnp.bfloat16),
        cost_estimate=pl.CostEstimate(
            flops=2 * frames * (places * channels * 2 * channels + 4 * own_places * channels * channels
                                + 8 * own_places * places * channels),
            transcendentals=frames * own_places * places,
            bytes_accessed=triple_weight.size * 2 + output_weight.size * 2 + residual.size * 2,
        ),
    )(
        residual,
        mine,
        mask,
        attention_gain.reshape(1, channels),
        triple_weight[:, channels:],
        triple_bias[channels:].reshape(1, 2 * channels),
        triple_weight[:, :channels],
        triple_bias[:channels].reshape(1, channels),
        output_weight,
        output_bias.reshape(1, channels),
    )


def gathered_body(
    segment_input,
    inner_input,
    lengths,
    inner_gain,
    causal_weight,
    causal_bias,
    attention_gain,
    triple_weight,
    triple_bias,
    output_weight,
    output_bias,
):
    clip_count, frame_count, row_count, column_count, channels = segment_input.shape
    sections = lax.axis_size("tm")
    counts = lengths[:, 0]
    ahead = [(i, i + 1) for i in range(sections - 1)]
    prev_counts = lax.ppermute(counts, "tm", ahead)
    both = jnp.concatenate([inner_input, segment_input], axis=0)
    both_all = lax.all_gather(both, "rows", axis=2, tiled=True)
    inner_all = both_all[:clip_count]
    segment_all = both_all[clip_count:]
    wide = (counts > 1)[:, None, None, None]
    last_raw = jnp.where(wide, inner_all[:, frame_count - 1], inner_all[:, 0])
    prev_raw = lax.ppermute(inner_all, "tm", ahead)
    before_raw = lax.ppermute(last_raw, "tm", [(i, i + 2) for i in range(sections - 2)])
    own = activate(inner_all, inner_gain)
    own_sum = own_conv(own, causal_weight)
    own_sum, prev_raw, before_raw, prev_counts = lax.optimization_barrier(
        (own_sum, prev_raw, before_raw, prev_counts)
    )
    prev = activate(prev_raw, inner_gain)
    before = activate(before_raw, inner_gain)
    prev_wide = (prev_counts > 1)[:, None, None, None]
    carried = jnp.stack(
        [
            jnp.where(prev_wide, prev[:, frame_count - 2], before),
            jnp.where(prev_wide, prev[:, frame_count - 1], prev[:, 0]),
        ],
        axis=1,
    )
    carried_sum = carried_conv(carried, causal_weight, frame_count)
    height = inner_all.shape[2]
    convolved = frame_major(own_sum + carried_sum, clip_count, height, column_count) + causal_bias
    residual = (segment_all.astype(jnp.float32) + convolved).astype(jnp.bfloat16)
    height = residual.shape[2]
    frames = clip_count * frame_count
    start = lax.axis_index("rows") * row_count
    mine = lax.dynamic_slice_in_dim(residual, start, row_count, axis=2)
    live_mask = (jnp.arange(frame_count, dtype=jnp.int32)[None, :] < counts[:, None]).astype(
        jnp.float32
    )
    result = attend_local(
        residual.reshape(frames, height * column_count, channels),
        mine.reshape(frames, row_count * column_count, channels),
        live_mask.reshape(frames, 1, 1),
        attention_gain,
        triple_weight,
        triple_bias,
        output_weight,
        output_bias,
    )
    return result.reshape(clip_count, frame_count, row_count, column_count, channels)


GATHER_LIMIT = 1 << 22


def chosen_body(segment_input, inner_input, *rest):
    gathered = inner_input.size * inner_input.dtype.itemsize * lax.axis_size("rows")
    if gathered <= GATHER_LIMIT:
        return gathered_body(segment_input, inner_input, *rest)
    return body(segment_input, inner_input, *rest)


def solution(mesh):
    placed = (
        P("clips", "tm", "rows", None, None),
        P("clips", "tm", "rows", None, None),
        P("clips", "tm"),
        P(),
        P(),
        P(),
        P(),
        P(),
        P(),
        P(),
        P(),
    )
    return jax.shard_map(
        chosen_body,
        mesh=mesh,
        in_specs=placed,
        out_specs=P("clips", "tm", "rows", None, None),
        check_vma=False,
    )
```

```python
import functools
import math

import jax
import jax.numpy as jnp
from jax import lax
from jax.sharding import PartitionSpec as P
from jax.experimental import pallas as pl
from jax.experimental.pallas import tpu as pltpu

EPSILON = 1e-06


def prefix(part, axis, combine, identity):
    place = lax.axis_index(axis)
    gathered = jax.tree.map(lambda a: lax.all_gather(a, axis), part)
    state = jax.tree.map(lambda a, e: jnp.zeros_like(a) + jnp.asarray(e, a.dtype), part, identity)

    def one(step, state):
        return combine(
            state, jax.tree.map(lambda a: lax.dynamic_index_in_dim(a, step, 0, False), gathered)
        )

    return lax.fori_loop(0, place, one, state)


def as_sent(x):

    def short(part):
        return part.astype(jnp.bfloat16) if part.dtype == jnp.float32 else part

    return jax.tree.map(short, x)


def with_halo(cells, sides, width):
    for axis, dim in sides:
        count = lax.axis_size(axis)
        ends = count - 1
        head = lax.slice_in_dim(cells, 0, width, axis=dim)
        tail = lax.slice_in_dim(cells, cells.shape[dim] - width, cells.shape[dim], axis=dim)
        cells = jnp.concatenate(
            [
                lax.ppermute(tail, axis, [(i, (i + 1) % count) for i in range(ends)]),
                cells,
                lax.ppermute(head, axis, [((i + 1) % count, i) for i in range(ends)]),
            ],
            axis=dim,
        )
    return cells


def normalize(field, gain):
    widened = field.astype(jnp.float32)
    return widened * lax.rsqrt(jnp.mean(widened * widened, axis=-1, keepdims=True) + EPSILON) * gain


def last_two(extended, counts):
    slot_total = extended.shape[1]
    chosen = []
    for position in range(2):
        target = counts + position
        picked = jnp.zeros_like(extended[:, 0])
        for slot_index in range(slot_total):
            matches = (target == slot_index)[:, None, None, None]
            picked = jnp.where(matches, extended[:, slot_index], picked)
        chosen.append(picked)
    return jnp.stack(chosen, axis=1)


def summarize(activated, counts):
    blanks = jnp.zeros((activated.shape[0], 2) + activated.shape[2:], activated.dtype)
    summary = last_two(jnp.concatenate([blanks, activated], axis=1), counts)
    return (summary, jnp.minimum(counts, 2).astype(jnp.bfloat16))


def join_later(earlier, later):
    early_frames, early_count = earlier
    late_frames, late_count = later
    complete = (late_count > 1.5)[:, None, None, None, None]
    single = (late_count > 0.5)[:, None, None, None, None]
    shifted = jnp.concatenate([early_frames[:, 1:], late_frames[:, 1:]], axis=1)
    frames = jnp.where(complete, late_frames, jnp.where(single, shifted, early_frames))
    total_count = jnp.minimum(early_count + late_count, 2.0).astype(early_count.dtype)
    return (frames, total_count)


def incoming_cache(summary, counts):
    starting = (jnp.zeros_like(summary), jnp.zeros_like(counts))
    combined = prefix((summary, counts), "tm", join_later, starting)
    return combined[0]


def convolve(padded, causal_weight, causal_bias):
    clip_count, slot_total, rows_padded, column_count, channels = padded.shape
    frame_count = slot_total - 2
    row_count = rows_padded - 2
    widened = jnp.pad(padded, ((0, 0), (0, 0), (0, 0), (1, 1), (0, 0)))
    summed = jnp.zeros((clip_count * frame_count * row_count * column_count, channels), jnp.float32)
    for delta_time in range(3):
        for delta_row in range(3):
            window = widened[
                :, delta_time : delta_time + frame_count, delta_row : delta_row + row_count
            ]
            columns = jnp.concatenate(
                [window[:, :, :, delta_col : delta_col + column_count] for delta_col in range(3)],
                axis=-1,
            )
            kernel = causal_weight[delta_time, delta_row].reshape(3 * channels, channels)
            summed = summed + jnp.dot(
                columns.reshape(-1, 3 * channels), kernel, preferred_element_type=jnp.float32
            )
    return summed.reshape(clip_count, frame_count, row_count, column_count, channels) + causal_bias


def attend(normed, triple_weight, triple_bias, output_weight, output_bias):
    frame_count, places, channels = normed.shape
    packed = (
        jnp.dot(normed.reshape(-1, channels), triple_weight, preferred_element_type=jnp.float32)
        + triple_bias
    )
    packed = packed.reshape(frame_count, places, 3 * channels)
    queries = packed[:, :, :channels]
    key_vectors = packed[:, :, channels : 2 * channels]
    values = packed[:, :, 2 * channels :].astype(jnp.bfloat16)
    scores = jnp.einsum(
        "nqc,nkc->nqk", queries, key_vectors, precision=lax.Precision.HIGHEST
    ) / math.sqrt(channels)
    row_max = jnp.max(scores, axis=-1, keepdims=True)
    exponent = jnp.exp(scores - row_max)
    weights = (exponent / jnp.sum(exponent, axis=-1, keepdims=True)).astype(jnp.bfloat16)
    attended = jnp.einsum(
        "nqk,nkc->nqc", weights, values, preferred_element_type=jnp.float32
    ).astype(jnp.bfloat16)
    projected = (
        jnp.dot(attended.reshape(-1, channels), output_weight, preferred_element_type=jnp.float32)
        + output_bias
    )
    return projected.reshape(frame_count, places, channels).astype(jnp.bfloat16)


def body(
    segment_input,
    inner_input,
    lengths,
    inner_gain,
    causal_weight,
    causal_bias,
    attention_gain,
    triple_weight,
    triple_bias,
    output_weight,
    output_bias,
):
    clip_count, frame_count, row_count, column_count, channels = segment_input.shape
    activated = jax.nn.silu(normalize(inner_input, inner_gain)).astype(jnp.bfloat16)
    counts = lengths[:, 0]
    live_mask = (jnp.arange(frame_count, dtype=jnp.int32)[None, :] < counts[:, None]).astype(
        jnp.float32
    )
    carried = incoming_cache(*summarize(activated, counts))
    extended = jnp.concatenate([carried, activated], axis=1)
    padded = with_halo(as_sent(extended), (("rows", 2),), 1).astype(extended.dtype)
    convolved = convolve(padded, causal_weight, causal_bias)
    residual = (segment_input.astype(jnp.float32) + convolved).astype(jnp.bfloat16)
    residual = lax.optimization_barrier(residual)
    normed = normalize(residual, attention_gain).astype(jnp.bfloat16)
    row_devices = lax.axis_size("rows")
    per_device = clip_count * frame_count // row_devices
    grouped = normed.reshape(row_devices, per_device, row_count, column_count, channels)
    portion = lax.all_to_all(grouped, "rows", split_axis=0, concat_axis=2, tiled=True)
    owned = portion.shape[1]
    height = portion.shape[2]
    flat = portion.reshape(owned, height * column_count, channels)
    result = attend(flat, triple_weight, triple_bias, output_weight, output_bias)
    result = result.reshape(1, owned, height, column_count, channels)
    projected = lax.all_to_all(result, "rows", split_axis=2, concat_axis=0, tiled=True)
    projected = projected.reshape(clip_count, frame_count, row_count, column_count, channels)
    projected = lax.optimization_barrier(projected)
    summed = residual.astype(jnp.float32) + projected.astype(jnp.float32)
    return (summed * live_mask[:, :, None, None, None]).astype(jnp.bfloat16)


def activate(field, gain):
    return jax.nn.silu(normalize(field, gain)).astype(jnp.bfloat16)


def conv_part_kernel(plan, first_tap, x_ref, w_hbm, o_ref, w_vmem, sems):
    clips, held, rows, columns, width = x_ref.shape
    height = rows - 2
    places = height * columns
    channels = w_vmem.shape[-1]
    copies = []
    for index in range(len(plan)):
        for kh in range(3):
            slot_index = index * 3 + kh
            copy = pltpu.make_async_copy(
                w_hbm.at[first_tap + index, kh], w_vmem.at[slot_index], sems.at[slot_index]
            )
            copy.start()
            copies.append(copy)
    written = set()
    for index, (frame, slot, count) in enumerate(plan):
        for kh in (1, 0, 2):
            slot_index = index * 3 + kh
            copies[slot_index].wait()
            low = 1 if kh == 0 else 0
            high = height - 1 if kh == 2 else height
            if high <= low:
                continue
            weight = w_vmem[slot_index].reshape(width, channels)
            lhs = x_ref[:, frame : frame + count, low + kh : high + kh, :, :]
            lhs = lhs.reshape(clips * count * (high - low) * columns, width)
            term = jnp.dot(lhs, weight, preferred_element_type=jnp.float32)
            term = term.reshape(clips, count, (high - low) * columns, channels)
            rows_here = slice(low * columns, high * columns)
            for part in range(count):
                target = slot + part
                if target in written:
                    o_ref[:, target, rows_here] += term[:, part]
                else:
                    o_ref[:, target] = term[:, part]
                    written.add(target)


def conv_part(frames, causal_weight, plan, first_tap, slots):
    clips, held, height, columns, channels = frames.shape
    padded = jnp.pad(frames, ((0, 0), (0, 0), (1, 1), (1, 1), (0, 0)))
    taps = jnp.concatenate(
        [padded[:, :, :, kw : kw + columns] for kw in range(3)], axis=-1
    )
    places = height * columns
    dots = sum(count for _, _, count in plan) * 3
    blocks = len(plan) * 3
    return pl.pallas_call(
        functools.partial(conv_part_kernel, plan, first_tap),
        in_specs=[
            pl.BlockSpec(memory_space=pltpu.VMEM),
            pl.BlockSpec(memory_space=pl.ANY),
        ],
        out_specs=pl.BlockSpec(memory_space=pltpu.VMEM),
        out_shape=jax.ShapeDtypeStruct((clips, slots, places, channels), jnp.float32),
        scratch_shapes=[
            pltpu.VMEM((blocks, 3, channels, channels), causal_weight.dtype),
            pltpu.SemaphoreType.DMA((blocks,)),
        ],
        compiler_params=pltpu.CompilerParams(vmem_limit_bytes=48 * 1024 * 1024),
        cost_estimate=pl.CostEstimate(
            flops=2 * clips * places * dots * 3 * channels * channels,
            transcendentals=0,
            bytes_accessed=blocks * 3 * channels * channels * 2
            + taps.size * 2
            + clips * slots * places * channels * 4,
        ),
    )(taps, causal_weight)


def conv_plans(slots):
    own, carried = {}, {}
    for kt in range(3):
        for slot in range(slots):
            source = slot + kt
            if source >= 2:
                own.setdefault(kt, []).append((source - 2, slot))
            else:
                carried.setdefault(kt, []).append((source, slot))
    return own, carried


def plan_of(table):
    taps = sorted(table)
    assert taps == list(range(taps[0], taps[-1] + 1))
    runs = []
    for kt in taps:
        pairs = sorted(table[kt], key=lambda pair: pair[1])
        frame, slot = pairs[0]
        assert pairs == [(frame + k, slot + k) for k in range(len(pairs))]
        runs.append((frame, slot, len(pairs)))
    return tuple(runs), taps[0]


def own_conv(own_frames, causal_weight):
    own_table, _ = conv_plans(own_frames.shape[1])
    own_plan, own_first = plan_of(own_table)
    return conv_part(own_frames, causal_weight, own_plan, own_first, own_frames.shape[1])


def carried_conv(carried_frames, causal_weight, slots):
    _, carried_table = conv_plans(slots)
    carried_plan, carried_first = plan_of(carried_table)
    return conv_part(carried_frames, causal_weight, carried_plan, carried_first, slots)


def frame_major(total, clips, height, columns):
    clips, slots, places, channels = total.shape
    return total.reshape(clips, slots, height, columns, channels)


def gathered_body(
    segment_input,
    inner_input,
    lengths,
    inner_gain,
    causal_weight,
    causal_bias,
    attention_gain,
    triple_weight,
    triple_bias,
    output_weight,
    output_bias,
):
    clip_count, frame_count, row_count, column_count, channels = segment_input.shape
    sections = lax.axis_size("tm")
    counts = lengths[:, 0]
    ahead = [(i, i + 1) for i in range(sections - 1)]
    prev_counts = lax.ppermute(counts, "tm", ahead)
    both = jnp.concatenate([inner_input, segment_input], axis=0)
    both_all = lax.all_gather(both, "rows", axis=2, tiled=True)
    inner_all = both_all[:clip_count]
    segment_all = both_all[clip_count:]
    wide = (counts > 1)[:, None, None, None]
    last_raw = jnp.where(wide, inner_all[:, frame_count - 1], inner_all[:, 0])
    prev_raw = lax.ppermute(inner_all, "tm", ahead)
    before_raw = lax.ppermute(last_raw, "tm", [(i, i + 2) for i in range(sections - 2)])
    own = activate(inner_all, inner_gain)
    own_sum = own_conv(own, causal_weight)
    own_sum, prev_raw, before_raw, prev_counts = lax.optimization_barrier(
        (own_sum, prev_raw, before_raw, prev_counts)
    )
    prev = activate(prev_raw, inner_gain)
    before = activate(before_raw, inner_gain)
    prev_wide = (prev_counts > 1)[:, None, None, None]
    carried = jnp.stack(
        [
            jnp.where(prev_wide, prev[:, frame_count - 2], before),
            jnp.where(prev_wide, prev[:, frame_count - 1], prev[:, 0]),
        ],
        axis=1,
    )
    carried_sum = carried_conv(carried, causal_weight, frame_count)
    height = inner_all.shape[2]
    convolved = frame_major(own_sum + carried_sum, clip_count, height, column_count) + causal_bias
    residual = (segment_all.astype(jnp.float32) + convolved).astype(jnp.bfloat16)
    normed = normalize(residual, attention_gain).astype(jnp.bfloat16)
    height = normed.shape[2]
    frames = clip_count * frame_count
    places = height * column_count
    flat = normed.reshape(frames * places, channels)
    packed = (
        jnp.dot(flat, triple_weight[:, channels:], preferred_element_type=jnp.float32)
        + triple_bias[channels:]
    ).reshape(frames, places, 2 * channels)
    key_vectors = packed[:, :, :channels]
    values = packed[:, :, channels:].astype(jnp.bfloat16)
    start = lax.axis_index("rows") * row_count
    mine = lax.dynamic_slice_in_dim(normed, start, row_count, axis=2)
    queries = (
        jnp.dot(
            mine.reshape(-1, channels), triple_weight[:, :channels],
            preferred_element_type=jnp.float32,
        )
        + triple_bias[:channels]
    ).reshape(frames, row_count * column_count, channels)
    scores = jnp.einsum(
        "nqc,nkc->nqk", queries, key_vectors, precision=lax.Precision.HIGHEST
    ) / math.sqrt(channels)
    row_max = jnp.max(scores, axis=-1, keepdims=True)
    exponent = jnp.exp(scores - row_max)
    weights = (exponent / jnp.sum(exponent, axis=-1, keepdims=True)).astype(jnp.bfloat16)
    attended = jnp.einsum(
        "nqk,nkc->nqc", weights, values, preferred_element_type=jnp.float32
    ).astype(jnp.bfloat16)
    projected = (
        jnp.dot(attended.reshape(-1, channels), output_weight, preferred_element_type=jnp.float32)
        + output_bias
    ).astype(jnp.bfloat16)
    projected = projected.reshape(clip_count, frame_count, row_count, column_count, channels)
    residual_mine = lax.dynamic_slice_in_dim(residual, start, row_count, axis=2)
    live_mask = (jnp.arange(frame_count, dtype=jnp.int32)[None, :] < counts[:, None]).astype(
        jnp.float32
    )
    summed = residual_mine.astype(jnp.float32) + projected.astype(jnp.float32)
    return (summed * live_mask[:, :, None, None, None]).astype(jnp.bfloat16)


GATHER_LIMIT = 1 << 22


def chosen_body(segment_input, inner_input, *rest):
    gathered = inner_input.size * inner_input.dtype.itemsize * lax.axis_size("rows")
    if gathered <= GATHER_LIMIT:
        return gathered_body(segment_input, inner_input, *rest)
    return body(segment_input, inner_input, *rest)


def solution(mesh):
    placed = (
        P("clips", "tm", "rows", None, None),
        P("clips", "tm", "rows", None, None),
        P("clips", "tm"),
        P(),
        P(),
        P(),
        P(),
        P(),
        P(),
        P(),
        P(),
    )
    return jax.shard_map(
        chosen_body,
        mesh=mesh,
        in_specs=placed,
        out_specs=P("clips", "tm", "rows", None, None),
        check_vma=False,
    )
```

```python
import functools
import math

import jax
import jax.numpy as jnp
from jax import lax
from jax.sharding import PartitionSpec as P
from jax.experimental import pallas as pl
from jax.experimental.pallas import tpu as pltpu

EPSILON = 1e-06
UNUSED_MARK = -100.0


def prefix(part, axis, combine, identity):
    place = lax.axis_index(axis)
    gathered = jax.tree.map(lambda a: lax.all_gather(a, axis), part)
    state = jax.tree.map(lambda a, e: jnp.zeros_like(a) + jnp.asarray(e, a.dtype), part, identity)

    def one(step, state):
        return combine(
            state, jax.tree.map(lambda a: lax.dynamic_index_in_dim(a, step, 0, False), gathered)
        )

    return lax.fori_loop(0, place, one, state)


def as_sent(x):

    def short(part):
        return part.astype(jnp.bfloat16) if part.dtype == jnp.float32 else part

    return jax.tree.map(short, x)


def with_halo(cells, sides, width):
    for axis, dim in sides:
        count = lax.axis_size(axis)
        ends = count - 1
        head = lax.slice_in_dim(cells, 0, width, axis=dim)
        tail = lax.slice_in_dim(cells, cells.shape[dim] - width, cells.shape[dim], axis=dim)
        cells = jnp.concatenate(
            [
                lax.ppermute(tail, axis, [(i, (i + 1) % count) for i in range(ends)]),
                cells,
                lax.ppermute(head, axis, [((i + 1) % count, i) for i in range(ends)]),
            ],
            axis=dim,
        )
    return cells


def normalize(field, gain):
    widened = field.astype(jnp.float32)
    return widened * lax.rsqrt(jnp.mean(widened * widened, axis=-1, keepdims=True) + EPSILON) * gain


def last_two(extended, counts):
    slot_total = extended.shape[1]
    chosen = []
    for position in range(2):
        target = counts + position
        picked = jnp.zeros_like(extended[:, 0])
        for slot_index in range(slot_total):
            matches = (target == slot_index)[:, None, None, None]
            picked = jnp.where(matches, extended[:, slot_index], picked)
        chosen.append(picked)
    return jnp.stack(chosen, axis=1)


def summarize(activated, counts):
    blanks = jnp.zeros((activated.shape[0], 2) + activated.shape[2:], activated.dtype)
    summary = last_two(jnp.concatenate([blanks, activated], axis=1), counts)
    return (summary, jnp.minimum(counts, 2).astype(jnp.bfloat16))


def join_later(earlier, later):
    early_frames, early_count = earlier
    late_frames, late_count = later
    complete = (late_count > 1.5)[:, None, None, None, None]
    single = (late_count > 0.5)[:, None, None, None, None]
    shifted = jnp.concatenate([early_frames[:, 1:], late_frames[:, 1:]], axis=1)
    frames = jnp.where(complete, late_frames, jnp.where(single, shifted, early_frames))
    total_count = jnp.minimum(early_count + late_count, 2.0).astype(early_count.dtype)
    return (frames, total_count)


def incoming_cache(summary, counts):
    starting = (jnp.zeros_like(summary), jnp.zeros_like(counts))
    combined = prefix((summary, counts), "tm", join_later, starting)
    return combined[0]


def convolve(padded, causal_weight, causal_bias):
    clip_count, slot_total, rows_padded, column_count, channels = padded.shape
    frame_count = slot_total - 2
    row_count = rows_padded - 2
    widened = jnp.pad(padded, ((0, 0), (0, 0), (0, 0), (1, 1), (0, 0)))
    summed = jnp.zeros((clip_count * frame_count * row_count * column_count, channels), jnp.float32)
    for delta_time in range(3):
        for delta_row in range(3):
            window = widened[
                :, delta_time : delta_time + frame_count, delta_row : delta_row + row_count
            ]
            columns = jnp.concatenate(
                [window[:, :, :, delta_col : delta_col + column_count] for delta_col in range(3)],
                axis=-1,
            )
            kernel = causal_weight[delta_time, delta_row].reshape(3 * channels, channels)
            summed = summed + jnp.dot(
                columns.reshape(-1, 3 * channels), kernel, preferred_element_type=jnp.float32
            )
    return summed.reshape(clip_count, frame_count, row_count, column_count, channels) + causal_bias


def attend(normed, triple_weight, triple_bias, output_weight, output_bias):
    frame_count, places, channels = normed.shape
    packed = (
        jnp.dot(normed.reshape(-1, channels), triple_weight, preferred_element_type=jnp.float32)
        + triple_bias
    )
    packed = packed.reshape(frame_count, places, 3 * channels)
    queries = packed[:, :, :channels]
    key_vectors = packed[:, :, channels : 2 * channels]
    values = packed[:, :, 2 * channels :].astype(jnp.bfloat16)
    scores = jnp.einsum(
        "nqc,nkc->nqk", queries, key_vectors, precision=lax.Precision.HIGHEST
    ) / math.sqrt(channels)
    row_max = jnp.max(scores, axis=-1, keepdims=True)
    exponent = jnp.exp(scores - row_max)
    weights = (exponent / jnp.sum(exponent, axis=-1, keepdims=True)).astype(jnp.bfloat16)
    attended = jnp.einsum(
        "nqk,nkc->nqc", weights, values, preferred_element_type=jnp.float32
    ).astype(jnp.bfloat16)
    projected = (
        jnp.dot(attended.reshape(-1, channels), output_weight, preferred_element_type=jnp.float32)
        + output_bias
    )
    return projected.reshape(frame_count, places, channels).astype(jnp.bfloat16)


def body(
    segment_input,
    inner_input,
    lengths,
    inner_gain,
    causal_weight,
    causal_bias,
    attention_gain,
    triple_weight,
    triple_bias,
    output_weight,
    output_bias,
):
    clip_count, frame_count, row_count, column_count, channels = segment_input.shape
    activated = jax.nn.silu(normalize(inner_input, inner_gain)).astype(jnp.bfloat16)
    counts = lengths[:, 0]
    live_mask = (jnp.arange(frame_count, dtype=jnp.int32)[None, :] < counts[:, None]).astype(
        jnp.float32
    )
    carried = incoming_cache(*summarize(activated, counts))
    extended = jnp.concatenate([carried, activated], axis=1)
    padded = with_halo(as_sent(extended), (("rows", 2),), 1).astype(extended.dtype)
    convolved = convolve(padded, causal_weight, causal_bias)
    residual = (segment_input.astype(jnp.float32) + convolved).astype(jnp.bfloat16)
    residual = lax.optimization_barrier(residual)
    normed = normalize(residual, attention_gain).astype(jnp.bfloat16)
    row_devices = lax.axis_size("rows")
    per_device = clip_count * frame_count // row_devices
    grouped = normed.reshape(row_devices, per_device, row_count, column_count, channels)
    portion = lax.all_to_all(grouped, "rows", split_axis=0, concat_axis=2, tiled=True)
    owned = portion.shape[1]
    height = portion.shape[2]
    flat = portion.reshape(owned, height * column_count, channels)
    result = attend(flat, triple_weight, triple_bias, output_weight, output_bias)
    result = result.reshape(1, owned, height, column_count, channels)
    projected = lax.all_to_all(result, "rows", split_axis=2, concat_axis=0, tiled=True)
    projected = projected.reshape(clip_count, frame_count, row_count, column_count, channels)
    projected = lax.optimization_barrier(projected)
    summed = residual.astype(jnp.float32) + projected.astype(jnp.float32)
    return (summed * live_mask[:, :, None, None, None]).astype(jnp.bfloat16)


def activate(field, gain):
    return jax.nn.silu(normalize(field, gain)).astype(jnp.bfloat16)


def conv_part_kernel(plan, first_tap, x_ref, w_hbm, o_ref, w_vmem, sems):
    clips, held, rows, columns, width = x_ref.shape
    height = rows - 2
    places = height * columns
    channels = w_vmem.shape[-1]
    copies = []
    for index in range(len(plan)):
        for kh in range(3):
            slot_index = index * 3 + kh
            copy = pltpu.make_async_copy(
                w_hbm.at[first_tap + index, kh], w_vmem.at[slot_index], sems.at[slot_index]
            )
            copy.start()
            copies.append(copy)
    written = set()
    for index, (frame, slot, count) in enumerate(plan):
        for kh in (1, 0, 2):
            slot_index = index * 3 + kh
            copies[slot_index].wait()
            low = 1 if kh == 0 else 0
            high = height - 1 if kh == 2 else height
            if high <= low:
                continue
            weight = w_vmem[slot_index].reshape(width, channels)
            lhs = x_ref[:, frame : frame + count, low + kh : high + kh, :, :]
            lhs = lhs.reshape(clips * count * (high - low) * columns, width)
            term = jnp.dot(lhs, weight, preferred_element_type=jnp.float32)
            term = term.reshape(clips, count, (high - low) * columns, channels)
            rows_here = slice(low * columns, high * columns)
            for part in range(count):
                target = slot + part
                if target in written:
                    o_ref[:, target, rows_here] += term[:, part]
                else:
                    o_ref[:, target] = term[:, part]
                    written.add(target)


def conv_part(frames, causal_weight, plan, first_tap, slots):
    clips, held, height, columns, channels = frames.shape
    padded = jnp.pad(frames, ((0, 0), (0, 0), (1, 1), (1, 1), (0, 0)))
    taps = jnp.concatenate(
        [padded[:, :, :, kw : kw + columns] for kw in range(3)], axis=-1
    )
    places = height * columns
    dots = sum(count for _, _, count in plan) * 3
    blocks = len(plan) * 3
    return pl.pallas_call(
        functools.partial(conv_part_kernel, plan, first_tap),
        in_specs=[
            pl.BlockSpec(memory_space=pltpu.VMEM),
            pl.BlockSpec(memory_space=pl.ANY),
        ],
        out_specs=pl.BlockSpec(memory_space=pltpu.VMEM),
        out_shape=jax.ShapeDtypeStruct((clips, slots, places, channels), jnp.float32),
        scratch_shapes=[
            pltpu.VMEM((blocks, 3, channels, channels), causal_weight.dtype),
            pltpu.SemaphoreType.DMA((blocks,)),
        ],
        compiler_params=pltpu.CompilerParams(vmem_limit_bytes=48 * 1024 * 1024),
        cost_estimate=pl.CostEstimate(
            flops=2 * clips * places * dots * 3 * channels * channels,
            transcendentals=0,
            bytes_accessed=blocks * 3 * channels * channels * 2
            + taps.size * 2
            + clips * slots * places * channels * 4,
        ),
    )(taps, causal_weight)


def conv_plans(slots):
    own, carried = {}, {}
    for kt in range(3):
        for slot in range(slots):
            source = slot + kt
            if source >= 2:
                own.setdefault(kt, []).append((source - 2, slot))
            else:
                carried.setdefault(kt, []).append((source, slot))
    return own, carried


def plan_of(table):
    taps = sorted(table)
    assert taps == list(range(taps[0], taps[-1] + 1))
    runs = []
    for kt in taps:
        pairs = sorted(table[kt], key=lambda pair: pair[1])
        frame, slot = pairs[0]
        assert pairs == [(frame + k, slot + k) for k in range(len(pairs))]
        runs.append((frame, slot, len(pairs)))
    return tuple(runs), taps[0]


def own_conv(own_frames, causal_weight):
    own_table, _ = conv_plans(own_frames.shape[1])
    own_plan, own_first = plan_of(own_table)
    return conv_part(own_frames, causal_weight, own_plan, own_first, own_frames.shape[1])


def carried_conv(carried_frames, causal_weight, slots):
    _, carried_table = conv_plans(slots)
    carried_plan, carried_first = plan_of(carried_table)
    return conv_part(carried_frames, causal_weight, carried_plan, carried_first, slots)


def frame_major(total, clips, height, columns):
    clips, slots, places, channels = total.shape
    return total.reshape(clips, slots, height, columns, channels)


def gathered_body(
    segment_input,
    inner_input,
    lengths,
    inner_gain,
    causal_weight,
    causal_bias,
    attention_gain,
    triple_weight,
    triple_bias,
    output_weight,
    output_bias,
):
    clip_count, frame_count, row_count, column_count, channels = segment_input.shape
    sections = lax.axis_size("tm")
    counts = lengths[:, 0]
    ahead = [(i, i + 1) for i in range(sections - 1)]
    both = jnp.concatenate([inner_input, segment_input], axis=0)
    both_all = lax.all_gather(both, "rows", axis=2, tiled=True)
    inner_all = both_all[:clip_count]
    segment_all = both_all[clip_count:]
    wide = (counts > 1)[:, None, None, None]
    last_raw = jnp.where(wide, inner_all[:, frame_count - 1], inner_all[:, 0])
    marked = jnp.concatenate(
        [
            inner_all[:, : frame_count - 1],
            jnp.where(wide, inner_all[:, frame_count - 1], UNUSED_MARK)[:, None],
        ],
        axis=1,
    )
    prev_raw = lax.ppermute(marked, "tm", ahead)
    before_raw = lax.ppermute(last_raw, "tm", [(i, i + 2) for i in range(sections - 2)])
    own = activate(inner_all, inner_gain)
    own_sum = own_conv(own, causal_weight)
    own_sum, prev_raw, before_raw = lax.optimization_barrier((own_sum, prev_raw, before_raw))
    prev = activate(prev_raw, inner_gain)
    before = activate(before_raw, inner_gain)
    prev_wide = (prev_raw[:, frame_count - 1, 0, 0, 0] > UNUSED_MARK / 2)[:, None, None, None]
    carried = jnp.stack(
        [
            jnp.where(prev_wide, prev[:, frame_count - 2], before),
            jnp.where(prev_wide, prev[:, frame_count - 1], prev[:, 0]),
        ],
        axis=1,
    )
    carried_sum = carried_conv(carried, causal_weight, frame_count)
    height = inner_all.shape[2]
    convolved = frame_major(own_sum + carried_sum, clip_count, height, column_count) + causal_bias
    residual = (segment_all.astype(jnp.float32) + convolved).astype(jnp.bfloat16)
    normed = normalize(residual, attention_gain).astype(jnp.bfloat16)
    height = normed.shape[2]
    frames = clip_count * frame_count
    places = height * column_count
    flat = normed.reshape(frames * places, channels)
    packed = (
        jnp.dot(flat, triple_weight[:, channels:], preferred_element_type=jnp.float32)
        + triple_bias[channels:]
    ).reshape(frames, places, 2 * channels)
    key_vectors = packed[:, :, :channels]
    values = packed[:, :, channels:].astype(jnp.bfloat16)
    start = lax.axis_index("rows") * row_count
    mine = lax.dynamic_slice_in_dim(normed, start, row_count, axis=2)
    queries = (
        jnp.dot(
            mine.reshape(-1, channels), triple_weight[:, :channels],
            preferred_element_type=jnp.float32,
        )
        + triple_bias[:channels]
    ).reshape(frames, row_count * column_count, channels)
    scores = jnp.einsum(
        "nqc,nkc->nqk", queries, key_vectors, precision=lax.Precision.HIGHEST
    ) / math.sqrt(channels)
    row_max = jnp.max(scores, axis=-1, keepdims=True)
    exponent = jnp.exp(scores - row_max)
    weights = (exponent / jnp.sum(exponent, axis=-1, keepdims=True)).astype(jnp.bfloat16)
    attended = jnp.einsum(
        "nqk,nkc->nqc", weights, values, preferred_element_type=jnp.float32
    ).astype(jnp.bfloat16)
    projected = (
        jnp.dot(attended.reshape(-1, channels), output_weight, preferred_element_type=jnp.float32)
        + output_bias
    ).astype(jnp.bfloat16)
    projected = projected.reshape(clip_count, frame_count, row_count, column_count, channels)
    residual_mine = lax.dynamic_slice_in_dim(residual, start, row_count, axis=2)
    live_mask = (jnp.arange(frame_count, dtype=jnp.int32)[None, :] < counts[:, None]).astype(
        jnp.float32
    )
    summed = residual_mine.astype(jnp.float32) + projected.astype(jnp.float32)
    return (summed * live_mask[:, :, None, None, None]).astype(jnp.bfloat16)


GATHER_LIMIT = 1 << 22


def chosen_body(segment_input, inner_input, *rest):
    gathered = inner_input.size * inner_input.dtype.itemsize * lax.axis_size("rows")
    if gathered <= GATHER_LIMIT:
        return gathered_body(segment_input, inner_input, *rest)
    return body(segment_input, inner_input, *rest)


def solution(mesh):
    placed = (
        P("clips", "tm", "rows", None, None),
        P("clips", "tm", "rows", None, None),
        P("clips", "tm"),
        P(),
        P(),
        P(),
        P(),
        P(),
        P(),
        P(),
        P(),
    )
    return jax.shard_map(
        chosen_body,
        mesh=mesh,
        in_specs=placed,
        out_specs=P("clips", "tm", "rows", None, None),
        check_vma=False,
    )
```

```python
import functools
import math

import jax
import jax.numpy as jnp
from jax import lax
from jax.sharding import PartitionSpec as P
from jax.experimental import pallas as pl
from jax.experimental.pallas import tpu as pltpu

EPSILON = 1e-06
UNUSED_MARK = -100.0


def prefix(part, axis, combine, identity):
    place = lax.axis_index(axis)
    gathered = jax.tree.map(lambda a: lax.all_gather(a, axis), part)
    state = jax.tree.map(lambda a, e: jnp.zeros_like(a) + jnp.asarray(e, a.dtype), part, identity)

    def one(step, state):
        return combine(
            state, jax.tree.map(lambda a: lax.dynamic_index_in_dim(a, step, 0, False), gathered)
        )

    return lax.fori_loop(0, place, one, state)


def as_sent(x):

    def short(part):
        return part.astype(jnp.bfloat16) if part.dtype == jnp.float32 else part

    return jax.tree.map(short, x)


def with_halo(cells, sides, width):
    for axis, dim in sides:
        count = lax.axis_size(axis)
        ends = count - 1
        head = lax.slice_in_dim(cells, 0, width, axis=dim)
        tail = lax.slice_in_dim(cells, cells.shape[dim] - width, cells.shape[dim], axis=dim)
        cells = jnp.concatenate(
            [
                lax.ppermute(tail, axis, [(i, (i + 1) % count) for i in range(ends)]),
                cells,
                lax.ppermute(head, axis, [((i + 1) % count, i) for i in range(ends)]),
            ],
            axis=dim,
        )
    return cells


def normalize(field, gain):
    widened = field.astype(jnp.float32)
    return widened * lax.rsqrt(jnp.mean(widened * widened, axis=-1, keepdims=True) + EPSILON) * gain


def last_two(extended, counts):
    slot_total = extended.shape[1]
    chosen = []
    for position in range(2):
        target = counts + position
        picked = jnp.zeros_like(extended[:, 0])
        for slot_index in range(slot_total):
            matches = (target == slot_index)[:, None, None, None]
            picked = jnp.where(matches, extended[:, slot_index], picked)
        chosen.append(picked)
    return jnp.stack(chosen, axis=1)


def summarize(activated, counts):
    blanks = jnp.zeros((activated.shape[0], 2) + activated.shape[2:], activated.dtype)
    summary = last_two(jnp.concatenate([blanks, activated], axis=1), counts)
    return (summary, jnp.minimum(counts, 2).astype(jnp.bfloat16))


def join_later(earlier, later):
    early_frames, early_count = earlier
    late_frames, late_count = later
    complete = (late_count > 1.5)[:, None, None, None, None]
    single = (late_count > 0.5)[:, None, None, None, None]
    shifted = jnp.concatenate([early_frames[:, 1:], late_frames[:, 1:]], axis=1)
    frames = jnp.where(complete, late_frames, jnp.where(single, shifted, early_frames))
    total_count = jnp.minimum(early_count + late_count, 2.0).astype(early_count.dtype)
    return (frames, total_count)


def incoming_cache(summary, counts):
    starting = (jnp.zeros_like(summary), jnp.zeros_like(counts))
    combined = prefix((summary, counts), "tm", join_later, starting)
    return combined[0]


def convolve(padded, causal_weight, causal_bias):
    clip_count, slot_total, rows_padded, column_count, channels = padded.shape
    frame_count = slot_total - 2
    row_count = rows_padded - 2
    widened = jnp.pad(padded, ((0, 0), (0, 0), (0, 0), (1, 1), (0, 0)))
    summed = jnp.zeros((clip_count * frame_count * row_count * column_count, channels), jnp.float32)
    for delta_time in range(3):
        for delta_row in range(3):
            window = widened[
                :, delta_time : delta_time + frame_count, delta_row : delta_row + row_count
            ]
            columns = jnp.concatenate(
                [window[:, :, :, delta_col : delta_col + column_count] for delta_col in range(3)],
                axis=-1,
            )
            kernel = causal_weight[delta_time, delta_row].reshape(3 * channels, channels)
            summed = summed + jnp.dot(
                columns.reshape(-1, 3 * channels), kernel, preferred_element_type=jnp.float32
            )
    return summed.reshape(clip_count, frame_count, row_count, column_count, channels) + causal_bias


def attend(normed, triple_weight, triple_bias, output_weight, output_bias):
    frame_count, places, channels = normed.shape
    packed = (
        jnp.dot(normed.reshape(-1, channels), triple_weight, preferred_element_type=jnp.float32)
        + triple_bias
    )
    packed = packed.reshape(frame_count, places, 3 * channels)
    queries = packed[:, :, :channels]
    key_vectors = packed[:, :, channels : 2 * channels]
    values = packed[:, :, 2 * channels :].astype(jnp.bfloat16)
    scores = jnp.einsum(
        "nqc,nkc->nqk", queries, key_vectors, precision=lax.Precision.HIGHEST
    ) / math.sqrt(channels)
    row_max = jnp.max(scores, axis=-1, keepdims=True)
    exponent = jnp.exp(scores - row_max)
    weights = (exponent / jnp.sum(exponent, axis=-1, keepdims=True)).astype(jnp.bfloat16)
    attended = jnp.einsum(
        "nqk,nkc->nqc", weights, values, preferred_element_type=jnp.float32
    ).astype(jnp.bfloat16)
    projected = (
        jnp.dot(attended.reshape(-1, channels), output_weight, preferred_element_type=jnp.float32)
        + output_bias
    )
    return projected.reshape(frame_count, places, channels).astype(jnp.bfloat16)


def body(
    segment_input,
    inner_input,
    lengths,
    inner_gain,
    causal_weight,
    causal_bias,
    attention_gain,
    triple_weight,
    triple_bias,
    output_weight,
    output_bias,
):
    clip_count, frame_count, row_count, column_count, channels = segment_input.shape
    activated = jax.nn.silu(normalize(inner_input, inner_gain)).astype(jnp.bfloat16)
    counts = lengths[:, 0]
    live_mask = (jnp.arange(frame_count, dtype=jnp.int32)[None, :] < counts[:, None]).astype(
        jnp.float32
    )
    carried = incoming_cache(*summarize(activated, counts))
    extended = jnp.concatenate([carried, activated], axis=1)
    padded = with_halo(as_sent(extended), (("rows", 2),), 1).astype(extended.dtype)
    convolved = convolve(padded, causal_weight, causal_bias)
    residual = (segment_input.astype(jnp.float32) + convolved).astype(jnp.bfloat16)
    residual = lax.optimization_barrier(residual)
    normed = normalize(residual, attention_gain).astype(jnp.bfloat16)
    row_devices = lax.axis_size("rows")
    per_device = clip_count * frame_count // row_devices
    grouped = normed.reshape(row_devices, per_device, row_count, column_count, channels)
    portion = lax.all_to_all(grouped, "rows", split_axis=0, concat_axis=2, tiled=True)
    owned = portion.shape[1]
    height = portion.shape[2]
    flat = portion.reshape(owned, height * column_count, channels)
    result = attend(flat, triple_weight, triple_bias, output_weight, output_bias)
    result = result.reshape(1, owned, height, column_count, channels)
    projected = lax.all_to_all(result, "rows", split_axis=2, concat_axis=0, tiled=True)
    projected = projected.reshape(clip_count, frame_count, row_count, column_count, channels)
    projected = lax.optimization_barrier(projected)
    summed = residual.astype(jnp.float32) + projected.astype(jnp.float32)
    return (summed * live_mask[:, :, None, None, None]).astype(jnp.bfloat16)


def activate(field, gain):
    return jax.nn.silu(normalize(field, gain)).astype(jnp.bfloat16)


def conv_part_kernel(plan, first_tap, x_ref, w_hbm, o_ref, w_vmem, sems):
    clips, held, rows, columns, width = x_ref.shape
    height = rows - 2
    places = height * columns
    channels = w_vmem.shape[-1]
    copies = []
    for index in range(len(plan)):
        for kh in range(3):
            slot_index = index * 3 + kh
            copy = pltpu.make_async_copy(
                w_hbm.at[first_tap + index, kh], w_vmem.at[slot_index], sems.at[slot_index]
            )
            copy.start()
            copies.append(copy)
    written = set()
    for index, (frame, slot, count) in enumerate(plan):
        for kh in (1, 0, 2):
            slot_index = index * 3 + kh
            copies[slot_index].wait()
            low = 1 if kh == 0 else 0
            high = height - 1 if kh == 2 else height
            if high <= low:
                continue
            weight = w_vmem[slot_index].reshape(width, channels)
            lhs = x_ref[:, frame : frame + count, low + kh : high + kh, :, :]
            lhs = lhs.reshape(clips * count * (high - low) * columns, width)
            term = jnp.dot(lhs, weight, preferred_element_type=jnp.float32)
            term = term.reshape(clips, count, (high - low) * columns, channels)
            rows_here = slice(low * columns, high * columns)
            for part in range(count):
                target = slot + part
                if target in written:
                    o_ref[:, target, rows_here] += term[:, part]
                else:
                    o_ref[:, target] = term[:, part]
                    written.add(target)


def conv_part(frames, causal_weight, plan, first_tap, slots):
    clips, held, height, columns, channels = frames.shape
    padded = jnp.pad(frames, ((0, 0), (0, 0), (1, 1), (1, 1), (0, 0)))
    taps = jnp.concatenate(
        [padded[:, :, :, kw : kw + columns] for kw in range(3)], axis=-1
    )
    places = height * columns
    dots = sum(count for _, _, count in plan) * 3
    blocks = len(plan) * 3
    return pl.pallas_call(
        functools.partial(conv_part_kernel, plan, first_tap),
        in_specs=[
            pl.BlockSpec(memory_space=pltpu.VMEM),
            pl.BlockSpec(memory_space=pl.ANY),
        ],
        out_specs=pl.BlockSpec(memory_space=pltpu.VMEM),
        out_shape=jax.ShapeDtypeStruct((clips, slots, places, channels), jnp.float32),
        scratch_shapes=[
            pltpu.VMEM((blocks, 3, channels, channels), causal_weight.dtype),
            pltpu.SemaphoreType.DMA((blocks,)),
        ],
        compiler_params=pltpu.CompilerParams(vmem_limit_bytes=48 * 1024 * 1024),
        cost_estimate=pl.CostEstimate(
            flops=2 * clips * places * dots * 3 * channels * channels,
            transcendentals=0,
            bytes_accessed=blocks * 3 * channels * channels * 2
            + taps.size * 2
            + clips * slots * places * channels * 4,
        ),
    )(taps, causal_weight)


def conv_plans(slots):
    own, carried = {}, {}
    for kt in range(3):
        for slot in range(slots):
            source = slot + kt
            if source >= 2:
                own.setdefault(kt, []).append((source - 2, slot))
            else:
                carried.setdefault(kt, []).append((source, slot))
    return own, carried


def plan_of(table):
    taps = sorted(table)
    assert taps == list(range(taps[0], taps[-1] + 1))
    runs = []
    for kt in taps:
        pairs = sorted(table[kt], key=lambda pair: pair[1])
        frame, slot = pairs[0]
        assert pairs == [(frame + k, slot + k) for k in range(len(pairs))]
        runs.append((frame, slot, len(pairs)))
    return tuple(runs), taps[0]


def own_conv(own_frames, causal_weight):
    own_table, _ = conv_plans(own_frames.shape[1])
    own_plan, own_first = plan_of(own_table)
    return conv_part(own_frames, causal_weight, own_plan, own_first, own_frames.shape[1])


def carried_conv(carried_frames, causal_weight, slots):
    _, carried_table = conv_plans(slots)
    carried_plan, carried_first = plan_of(carried_table)
    return conv_part(carried_frames, causal_weight, carried_plan, carried_first, slots)


def frame_major(total, clips, height, columns):
    clips, slots, places, channels = total.shape
    return total.reshape(clips, slots, height, columns, channels)


def gathered_body(
    segment_input,
    inner_input,
    lengths,
    inner_gain,
    causal_weight,
    causal_bias,
    attention_gain,
    triple_weight,
    triple_bias,
    output_weight,
    output_bias,
):
    clip_count, frame_count, row_count, column_count, channels = segment_input.shape
    sections = lax.axis_size("tm")
    counts = lengths[:, 0]
    ahead = [(i, i + 1) for i in range(sections - 1)]
    both = jnp.concatenate([inner_input, segment_input], axis=0)
    both_all = lax.all_gather(both, "rows", axis=2, tiled=True)
    inner_all = both_all[:clip_count]
    segment_all = both_all[clip_count:]
    wide = (counts > 1)[:, None, None, None]
    marked = jnp.concatenate(
        [
            inner_all[:, : frame_count - 1],
            jnp.where(wide, inner_all[:, frame_count - 1], UNUSED_MARK)[:, None],
        ],
        axis=1,
    )
    prev_raw = lax.ppermute(marked, "tm", ahead)
    before_all = lax.ppermute(marked, "tm", [(i, i + 2) for i in range(sections - 2)])
    own = activate(inner_all, inner_gain)
    own_sum = own_conv(own, causal_weight)
    own_sum, prev_raw, before_all = lax.optimization_barrier((own_sum, prev_raw, before_all))
    before_wide = (before_all[:, frame_count - 1, 0, 0, 0] > UNUSED_MARK / 2)[:, None, None, None]
    before_raw = jnp.where(before_wide, before_all[:, frame_count - 1], before_all[:, 0])
    prev = activate(prev_raw, inner_gain)
    before = activate(before_raw, inner_gain)
    prev_wide = (prev_raw[:, frame_count - 1, 0, 0, 0] > UNUSED_MARK / 2)[:, None, None, None]
    carried = jnp.stack(
        [
            jnp.where(prev_wide, prev[:, frame_count - 2], before),
            jnp.where(prev_wide, prev[:, frame_count - 1], prev[:, 0]),
        ],
        axis=1,
    )
    carried_sum = carried_conv(carried, causal_weight, frame_count)
    height = inner_all.shape[2]
    convolved = frame_major(own_sum + carried_sum, clip_count, height, column_count) + causal_bias
    residual = (segment_all.astype(jnp.float32) + convolved).astype(jnp.bfloat16)
    normed = normalize(residual, attention_gain).astype(jnp.bfloat16)
    height = normed.shape[2]
    frames = clip_count * frame_count
    places = height * column_count
    flat = normed.reshape(frames * places, channels)
    packed = (
        jnp.dot(flat, triple_weight[:, channels:], preferred_element_type=jnp.float32)
        + triple_bias[channels:]
    ).reshape(frames, places, 2 * channels)
    key_vectors = packed[:, :, :channels]
    values = packed[:, :, channels:].astype(jnp.bfloat16)
    start = lax.axis_index("rows") * row_count
    mine = lax.dynamic_slice_in_dim(normed, start, row_count, axis=2)
    queries = (
        jnp.dot(
            mine.reshape(-1, channels), triple_weight[:, :channels],
            preferred_element_type=jnp.float32,
        )
        + triple_bias[:channels]
    ).reshape(frames, row_count * column_count, channels)
    scores = jnp.einsum(
        "nqc,nkc->nqk", queries, key_vectors, precision=lax.Precision.HIGHEST
    ) / math.sqrt(channels)
    row_max = jnp.max(scores, axis=-1, keepdims=True)
    exponent = jnp.exp(scores - row_max)
    weights = (exponent / jnp.sum(exponent, axis=-1, keepdims=True)).astype(jnp.bfloat16)
    attended = jnp.einsum(
        "nqk,nkc->nqc", weights, values, preferred_element_type=jnp.float32
    ).astype(jnp.bfloat16)
    projected = (
        jnp.dot(attended.reshape(-1, channels), output_weight, preferred_element_type=jnp.float32)
        + output_bias
    ).astype(jnp.bfloat16)
    projected = projected.reshape(clip_count, frame_count, row_count, column_count, channels)
    residual_mine = lax.dynamic_slice_in_dim(residual, start, row_count, axis=2)
    live_mask = (jnp.arange(frame_count, dtype=jnp.int32)[None, :] < counts[:, None]).astype(
        jnp.float32
    )
    summed = residual_mine.astype(jnp.float32) + projected.astype(jnp.float32)
    return (summed * live_mask[:, :, None, None, None]).astype(jnp.bfloat16)


GATHER_LIMIT = 1 << 22


def chosen_body(segment_input, inner_input, *rest):
    gathered = inner_input.size * inner_input.dtype.itemsize * lax.axis_size("rows")
    if gathered <= GATHER_LIMIT:
        return gathered_body(segment_input, inner_input, *rest)
    return body(segment_input, inner_input, *rest)


def solution(mesh):
    placed = (
        P("clips", "tm", "rows", None, None),
        P("clips", "tm", "rows", None, None),
        P("clips", "tm"),
        P(),
        P(),
        P(),
        P(),
        P(),
        P(),
        P(),
        P(),
    )
    return jax.shard_map(
        chosen_body,
        mesh=mesh,
        in_specs=placed,
        out_specs=P("clips", "tm", "rows", None, None),
        check_vma=False,
    )
```

```python
import functools
import math

import jax
import jax.numpy as jnp
from jax import lax
from jax.sharding import PartitionSpec as P
from jax.experimental import pallas as pl
from jax.experimental.pallas import tpu as pltpu

EPSILON = 1e-06
UNUSED_MARK = -100.0


def prefix(part, axis, combine, identity):
    place = lax.axis_index(axis)
    gathered = jax.tree.map(lambda a: lax.all_gather(a, axis), part)
    state = jax.tree.map(lambda a, e: jnp.zeros_like(a) + jnp.asarray(e, a.dtype), part, identity)

    def one(step, state):
        return combine(
            state, jax.tree.map(lambda a: lax.dynamic_index_in_dim(a, step, 0, False), gathered)
        )

    return lax.fori_loop(0, place, one, state)


def as_sent(x):

    def short(part):
        return part.astype(jnp.bfloat16) if part.dtype == jnp.float32 else part

    return jax.tree.map(short, x)


def with_halo(cells, sides, width):
    for axis, dim in sides:
        count = lax.axis_size(axis)
        ends = count - 1
        head = lax.slice_in_dim(cells, 0, width, axis=dim)
        tail = lax.slice_in_dim(cells, cells.shape[dim] - width, cells.shape[dim], axis=dim)
        cells = jnp.concatenate(
            [
                lax.ppermute(tail, axis, [(i, (i + 1) % count) for i in range(ends)]),
                cells,
                lax.ppermute(head, axis, [((i + 1) % count, i) for i in range(ends)]),
            ],
            axis=dim,
        )
    return cells


def normalize(field, gain):
    widened = field.astype(jnp.float32)
    return widened * lax.rsqrt(jnp.mean(widened * widened, axis=-1, keepdims=True) + EPSILON) * gain


def last_two(extended, counts):
    slot_total = extended.shape[1]
    chosen = []
    for position in range(2):
        target = counts + position
        picked = jnp.zeros_like(extended[:, 0])
        for slot_index in range(slot_total):
            matches = (target == slot_index)[:, None, None, None]
            picked = jnp.where(matches, extended[:, slot_index], picked)
        chosen.append(picked)
    return jnp.stack(chosen, axis=1)


def summarize(activated, counts):
    blanks = jnp.zeros((activated.shape[0], 2) + activated.shape[2:], activated.dtype)
    summary = last_two(jnp.concatenate([blanks, activated], axis=1), counts)
    return (summary, jnp.minimum(counts, 2).astype(jnp.bfloat16))


def join_later(earlier, later):
    early_frames, early_count = earlier
    late_frames, late_count = later
    complete = (late_count > 1.5)[:, None, None, None, None]
    single = (late_count > 0.5)[:, None, None, None, None]
    shifted = jnp.concatenate([early_frames[:, 1:], late_frames[:, 1:]], axis=1)
    frames = jnp.where(complete, late_frames, jnp.where(single, shifted, early_frames))
    total_count = jnp.minimum(early_count + late_count, 2.0).astype(early_count.dtype)
    return (frames, total_count)


def incoming_cache(summary, counts):
    starting = (jnp.zeros_like(summary), jnp.zeros_like(counts))
    combined = prefix((summary, counts), "tm", join_later, starting)
    return combined[0]


def convolve(padded, causal_weight, causal_bias):
    clip_count, slot_total, rows_padded, column_count, channels = padded.shape
    frame_count = slot_total - 2
    row_count = rows_padded - 2
    widened = jnp.pad(padded, ((0, 0), (0, 0), (0, 0), (1, 1), (0, 0)))
    summed = jnp.zeros((clip_count * frame_count * row_count * column_count, channels), jnp.float32)
    for delta_time in range(3):
        for delta_row in range(3):
            window = widened[
                :, delta_time : delta_time + frame_count, delta_row : delta_row + row_count
            ]
            columns = jnp.concatenate(
                [window[:, :, :, delta_col : delta_col + column_count] for delta_col in range(3)],
                axis=-1,
            )
            kernel = causal_weight[delta_time, delta_row].reshape(3 * channels, channels)
            summed = summed + jnp.dot(
                columns.reshape(-1, 3 * channels), kernel, preferred_element_type=jnp.float32
            )
    return summed.reshape(clip_count, frame_count, row_count, column_count, channels) + causal_bias


def attend(normed, triple_weight, triple_bias, output_weight, output_bias):
    frame_count, places, channels = normed.shape
    packed = (
        jnp.dot(normed.reshape(-1, channels), triple_weight, preferred_element_type=jnp.float32)
        + triple_bias
    )
    packed = packed.reshape(frame_count, places, 3 * channels)
    queries = packed[:, :, :channels]
    key_vectors = packed[:, :, channels : 2 * channels]
    values = packed[:, :, 2 * channels :].astype(jnp.bfloat16)
    scores = jnp.einsum(
        "nqc,nkc->nqk", queries, key_vectors, precision=lax.Precision.HIGHEST
    ) / math.sqrt(channels)
    row_max = jnp.max(scores, axis=-1, keepdims=True)
    exponent = jnp.exp(scores - row_max)
    weights = (exponent / jnp.sum(exponent, axis=-1, keepdims=True)).astype(jnp.bfloat16)
    attended = jnp.einsum(
        "nqk,nkc->nqc", weights, values, preferred_element_type=jnp.float32
    ).astype(jnp.bfloat16)
    projected = (
        jnp.dot(attended.reshape(-1, channels), output_weight, preferred_element_type=jnp.float32)
        + output_bias
    )
    return projected.reshape(frame_count, places, channels).astype(jnp.bfloat16)


def body(
    segment_input,
    inner_input,
    lengths,
    inner_gain,
    causal_weight,
    causal_bias,
    attention_gain,
    triple_weight,
    triple_bias,
    output_weight,
    output_bias,
):
    clip_count, frame_count, row_count, column_count, channels = segment_input.shape
    activated = jax.nn.silu(normalize(inner_input, inner_gain)).astype(jnp.bfloat16)
    counts = lengths[:, 0]
    live_mask = (jnp.arange(frame_count, dtype=jnp.int32)[None, :] < counts[:, None]).astype(
        jnp.float32
    )
    carried = incoming_cache(*summarize(activated, counts))
    extended = jnp.concatenate([carried, activated], axis=1)
    padded = with_halo(as_sent(extended), (("rows", 2),), 1).astype(extended.dtype)
    convolved = convolve(padded, causal_weight, causal_bias)
    residual = (segment_input.astype(jnp.float32) + convolved).astype(jnp.bfloat16)
    residual = lax.optimization_barrier(residual)
    normed = normalize(residual, attention_gain).astype(jnp.bfloat16)
    row_devices = lax.axis_size("rows")
    per_device = clip_count * frame_count // row_devices
    grouped = normed.reshape(row_devices, per_device, row_count, column_count, channels)
    portion = lax.all_to_all(grouped, "rows", split_axis=0, concat_axis=2, tiled=True)
    owned = portion.shape[1]
    height = portion.shape[2]
    flat = portion.reshape(owned, height * column_count, channels)
    result = attend(flat, triple_weight, triple_bias, output_weight, output_bias)
    result = result.reshape(1, owned, height, column_count, channels)
    projected = lax.all_to_all(result, "rows", split_axis=2, concat_axis=0, tiled=True)
    projected = projected.reshape(clip_count, frame_count, row_count, column_count, channels)
    projected = lax.optimization_barrier(projected)
    summed = residual.astype(jnp.float32) + projected.astype(jnp.float32)
    return (summed * live_mask[:, :, None, None, None]).astype(jnp.bfloat16)


def activate(field, gain):
    return jax.nn.silu(normalize(field, gain)).astype(jnp.bfloat16)


def conv_part_kernel(plan, first_tap, x_ref, w_hbm, o_ref, w_vmem, sems):
    clips, held, rows, columns, width = x_ref.shape
    height = rows - 2
    places = height * columns
    channels = w_vmem.shape[-1]
    copies = []
    for index in range(len(plan)):
        for kh in range(3):
            slot_index = index * 3 + kh
            copy = pltpu.make_async_copy(
                w_hbm.at[first_tap + index, kh], w_vmem.at[slot_index], sems.at[slot_index]
            )
            copy.start()
            copies.append(copy)
    written = set()
    for index, (frame, slot, count) in enumerate(plan):
        for kh in (1, 0, 2):
            slot_index = index * 3 + kh
            copies[slot_index].wait()
            low = 1 if kh == 0 else 0
            high = height - 1 if kh == 2 else height
            if high <= low:
                continue
            weight = w_vmem[slot_index].reshape(width, channels)
            lhs = x_ref[:, frame : frame + count, low + kh : high + kh, :, :]
            lhs = lhs.reshape(clips * count * (high - low) * columns, width)
            term = jnp.dot(lhs, weight, preferred_element_type=jnp.float32)
            term = term.reshape(clips, count, (high - low) * columns, channels)
            rows_here = slice(low * columns, high * columns)
            for part in range(count):
                target = slot + part
                if target in written:
                    o_ref[:, target, rows_here] += term[:, part]
                else:
                    o_ref[:, target] = term[:, part]
                    written.add(target)


def conv_part(frames, causal_weight, plan, first_tap, slots):
    clips, held, height, columns, channels = frames.shape
    padded = jnp.pad(frames, ((0, 0), (0, 0), (1, 1), (1, 1), (0, 0)))
    taps = jnp.concatenate(
        [padded[:, :, :, kw : kw + columns] for kw in range(3)], axis=-1
    )
    places = height * columns
    dots = sum(count for _, _, count in plan) * 3
    blocks = len(plan) * 3
    return pl.pallas_call(
        functools.partial(conv_part_kernel, plan, first_tap),
        in_specs=[
            pl.BlockSpec(memory_space=pltpu.VMEM),
            pl.BlockSpec(memory_space=pl.ANY),
        ],
        out_specs=pl.BlockSpec(memory_space=pltpu.VMEM),
        out_shape=jax.ShapeDtypeStruct((clips, slots, places, channels), jnp.float32),
        scratch_shapes=[
            pltpu.VMEM((blocks, 3, channels, channels), causal_weight.dtype),
            pltpu.SemaphoreType.DMA((blocks,)),
        ],
        compiler_params=pltpu.CompilerParams(vmem_limit_bytes=48 * 1024 * 1024),
        cost_estimate=pl.CostEstimate(
            flops=2 * clips * places * dots * 3 * channels * channels,
            transcendentals=0,
            bytes_accessed=blocks * 3 * channels * channels * 2
            + taps.size * 2
            + clips * slots * places * channels * 4,
        ),
    )(taps, causal_weight)


def conv_plans(slots):
    own, carried = {}, {}
    for kt in range(3):
        for slot in range(slots):
            source = slot + kt
            if source >= 2:
                own.setdefault(kt, []).append((source - 2, slot))
            else:
                carried.setdefault(kt, []).append((source, slot))
    return own, carried


def plan_of(table):
    taps = sorted(table)
    assert taps == list(range(taps[0], taps[-1] + 1))
    runs = []
    for kt in taps:
        pairs = sorted(table[kt], key=lambda pair: pair[1])
        frame, slot = pairs[0]
        assert pairs == [(frame + k, slot + k) for k in range(len(pairs))]
        runs.append((frame, slot, len(pairs)))
    return tuple(runs), taps[0]


def own_conv(own_frames, causal_weight):
    own_table, _ = conv_plans(own_frames.shape[1])
    own_plan, own_first = plan_of(own_table)
    return conv_part(own_frames, causal_weight, own_plan, own_first, own_frames.shape[1])


def carried_conv(carried_frames, causal_weight, slots):
    _, carried_table = conv_plans(slots)
    carried_plan, carried_first = plan_of(carried_table)
    return conv_part(carried_frames, causal_weight, carried_plan, carried_first, slots)


def frame_major(total, clips, height, columns):
    clips, slots, places, channels = total.shape
    return total.reshape(clips, slots, height, columns, channels)


def gathered_body(
    segment_input,
    inner_input,
    lengths,
    inner_gain,
    causal_weight,
    causal_bias,
    attention_gain,
    triple_weight,
    triple_bias,
    output_weight,
    output_bias,
):
    clip_count, frame_count, row_count, column_count, channels = segment_input.shape
    sections = lax.axis_size("tm")
    counts = lengths[:, 0]
    ahead = [(i, i + 1) for i in range(sections - 1)]
    both = jnp.concatenate([inner_input, segment_input], axis=0)
    both_all = lax.all_gather(both, "rows", axis=2, tiled=True)
    inner_all = both_all[:clip_count]
    segment_all = both_all[clip_count:]
    wide = (counts > 1)[:, None, None, None]
    last_raw = jnp.where(wide, inner_all[:, frame_count - 1], inner_all[:, 0])
    live = jnp.arange(frame_count, dtype=jnp.int32)[None, :] < counts[:, None]
    marked = jnp.where(live[:, :, None, None, None], inner_all, UNUSED_MARK).astype(inner_all.dtype)
    prev_raw = lax.ppermute(marked, "tm", ahead)
    before_raw = lax.ppermute(last_raw, "tm", [(i, i + 2) for i in range(sections - 2)])
    own = activate(inner_all, inner_gain)
    own_sum = own_conv(own, causal_weight)
    own_sum, prev_raw, before_raw = lax.optimization_barrier((own_sum, prev_raw, before_raw))
    prev = activate(prev_raw, inner_gain)
    before = activate(before_raw, inner_gain)
    prev_wide = (prev_raw[:, frame_count - 1, 0, 0, 0] > UNUSED_MARK / 2)[:, None, None, None]
    carried = jnp.stack(
        [
            jnp.where(prev_wide, prev[:, frame_count - 2], before),
            jnp.where(prev_wide, prev[:, frame_count - 1], prev[:, 0]),
        ],
        axis=1,
    )
    carried_sum = carried_conv(carried, causal_weight, frame_count)
    height = inner_all.shape[2]
    convolved = frame_major(own_sum + carried_sum, clip_count, height, column_count) + causal_bias
    residual = (segment_all.astype(jnp.float32) + convolved).astype(jnp.bfloat16)
    normed = normalize(residual, attention_gain).astype(jnp.bfloat16)
    height = normed.shape[2]
    frames = clip_count * frame_count
    places = height * column_count
    flat = normed.reshape(frames * places, channels)
    packed = (
        jnp.dot(flat, triple_weight[:, channels:], preferred_element_type=jnp.float32)
        + triple_bias[channels:]
    ).reshape(frames, places, 2 * channels)
    key_vectors = packed[:, :, :channels]
    values = packed[:, :, channels:].astype(jnp.bfloat16)
    start = lax.axis_index("rows") * row_count
    mine = lax.dynamic_slice_in_dim(normed, start, row_count, axis=2)
    queries = (
        jnp.dot(
            mine.reshape(-1, channels), triple_weight[:, :channels],
            preferred_element_type=jnp.float32,
        )
        + triple_bias[:channels]
    ).reshape(frames, row_count * column_count, channels)
    scores = jnp.einsum(
        "nqc,nkc->nqk", queries, key_vectors, precision=lax.Precision.HIGHEST
    ) / math.sqrt(channels)
    row_max = jnp.max(scores, axis=-1, keepdims=True)
    exponent = jnp.exp(scores - row_max)
    weights = (exponent / jnp.sum(exponent, axis=-1, keepdims=True)).astype(jnp.bfloat16)
    attended = jnp.einsum(
        "nqk,nkc->nqc", weights, values, preferred_element_type=jnp.float32
    ).astype(jnp.bfloat16)
    projected = (
        jnp.dot(attended.reshape(-1, channels), output_weight, preferred_element_type=jnp.float32)
        + output_bias
    ).astype(jnp.bfloat16)
    projected = projected.reshape(clip_count, frame_count, row_count, column_count, channels)
    residual_mine = lax.dynamic_slice_in_dim(residual, start, row_count, axis=2)
    live_mask = (jnp.arange(frame_count, dtype=jnp.int32)[None, :] < counts[:, None]).astype(
        jnp.float32
    )
    summed = residual_mine.astype(jnp.float32) + projected.astype(jnp.float32)
    return (summed * live_mask[:, :, None, None, None]).astype(jnp.bfloat16)


GATHER_LIMIT = 1 << 22


def chosen_body(segment_input, inner_input, *rest):
    gathered = inner_input.size * inner_input.dtype.itemsize * lax.axis_size("rows")
    if gathered <= GATHER_LIMIT:
        return gathered_body(segment_input, inner_input, *rest)
    return body(segment_input, inner_input, *rest)


def solution(mesh):
    placed = (
        P("clips", "tm", "rows", None, None),
        P("clips", "tm", "rows", None, None),
        P("clips", "tm"),
        P(),
        P(),
        P(),
        P(),
        P(),
        P(),
        P(),
        P(),
    )
    return jax.shard_map(
        chosen_body,
        mesh=mesh,
        in_specs=placed,
        out_specs=P("clips", "tm", "rows", None, None),
        check_vma=False,
    )
```

```python
import functools
import math

import jax
import jax.numpy as jnp
from jax import lax
from jax.sharding import PartitionSpec as P
from jax.experimental import pallas as pl
from jax.experimental.pallas import tpu as pltpu

EPSILON = 1e-06
UNUSED_MARK = -100.0


def prefix(part, axis, combine, identity):
    place = lax.axis_index(axis)
    gathered = jax.tree.map(lambda a: lax.all_gather(a, axis), part)
    state = jax.tree.map(lambda a, e: jnp.zeros_like(a) + jnp.asarray(e, a.dtype), part, identity)

    def one(step, state):
        return combine(
            state, jax.tree.map(lambda a: lax.dynamic_index_in_dim(a, step, 0, False), gathered)
        )

    return lax.fori_loop(0, place, one, state)


def as_sent(x):

    def short(part):
        return part.astype(jnp.bfloat16) if part.dtype == jnp.float32 else part

    return jax.tree.map(short, x)


def with_halo(cells, sides, width):
    for axis, dim in sides:
        count = lax.axis_size(axis)
        ends = count - 1
        head = lax.slice_in_dim(cells, 0, width, axis=dim)
        tail = lax.slice_in_dim(cells, cells.shape[dim] - width, cells.shape[dim], axis=dim)
        cells = jnp.concatenate(
            [
                lax.ppermute(tail, axis, [(i, (i + 1) % count) for i in range(ends)]),
                cells,
                lax.ppermute(head, axis, [((i + 1) % count, i) for i in range(ends)]),
            ],
            axis=dim,
        )
    return cells


def normalize(field, gain):
    widened = field.astype(jnp.float32)
    return widened * lax.rsqrt(jnp.mean(widened * widened, axis=-1, keepdims=True) + EPSILON) * gain


def last_two(extended, counts):
    slot_total = extended.shape[1]
    chosen = []
    for position in range(2):
        target = counts + position
        picked = jnp.zeros_like(extended[:, 0])
        for slot_index in range(slot_total):
            matches = (target == slot_index)[:, None, None, None]
            picked = jnp.where(matches, extended[:, slot_index], picked)
        chosen.append(picked)
    return jnp.stack(chosen, axis=1)


def summarize(activated, counts):
    blanks = jnp.zeros((activated.shape[0], 2) + activated.shape[2:], activated.dtype)
    summary = last_two(jnp.concatenate([blanks, activated], axis=1), counts)
    return (summary, jnp.minimum(counts, 2).astype(jnp.bfloat16))


def join_later(earlier, later):
    early_frames, early_count = earlier
    late_frames, late_count = later
    complete = (late_count > 1.5)[:, None, None, None, None]
    single = (late_count > 0.5)[:, None, None, None, None]
    shifted = jnp.concatenate([early_frames[:, 1:], late_frames[:, 1:]], axis=1)
    frames = jnp.where(complete, late_frames, jnp.where(single, shifted, early_frames))
    total_count = jnp.minimum(early_count + late_count, 2.0).astype(early_count.dtype)
    return (frames, total_count)


def incoming_cache(summary, counts):
    starting = (jnp.zeros_like(summary), jnp.zeros_like(counts))
    combined = prefix((summary, counts), "tm", join_later, starting)
    return combined[0]


def convolve(padded, causal_weight, causal_bias):
    clip_count, slot_total, rows_padded, column_count, channels = padded.shape
    frame_count = slot_total - 2
    row_count = rows_padded - 2
    widened = jnp.pad(padded, ((0, 0), (0, 0), (0, 0), (1, 1), (0, 0)))
    summed = jnp.zeros((clip_count * frame_count * row_count * column_count, channels), jnp.float32)
    for delta_time in range(3):
        for delta_row in range(3):
            window = widened[
                :, delta_time : delta_time + frame_count, delta_row : delta_row + row_count
            ]
            columns = jnp.concatenate(
                [window[:, :, :, delta_col : delta_col + column_count] for delta_col in range(3)],
                axis=-1,
            )
            kernel = causal_weight[delta_time, delta_row].reshape(3 * channels, channels)
            summed = summed + jnp.dot(
                columns.reshape(-1, 3 * channels), kernel, preferred_element_type=jnp.float32
            )
    return summed.reshape(clip_count, frame_count, row_count, column_count, channels) + causal_bias


def attend(normed, triple_weight, triple_bias, output_weight, output_bias):
    frame_count, places, channels = normed.shape
    packed = (
        jnp.dot(normed.reshape(-1, channels), triple_weight, preferred_element_type=jnp.float32)
        + triple_bias
    )
    packed = packed.reshape(frame_count, places, 3 * channels)
    queries = packed[:, :, :channels]
    key_vectors = packed[:, :, channels : 2 * channels]
    values = packed[:, :, 2 * channels :].astype(jnp.bfloat16)
    scores = jnp.einsum(
        "nqc,nkc->nqk", queries, key_vectors, precision=lax.Precision.HIGHEST
    ) / math.sqrt(channels)
    row_max = jnp.max(scores, axis=-1, keepdims=True)
    exponent = jnp.exp(scores - row_max)
    weights = (exponent / jnp.sum(exponent, axis=-1, keepdims=True)).astype(jnp.bfloat16)
    attended = jnp.einsum(
        "nqk,nkc->nqc", weights, values, preferred_element_type=jnp.float32
    ).astype(jnp.bfloat16)
    projected = (
        jnp.dot(attended.reshape(-1, channels), output_weight, preferred_element_type=jnp.float32)
        + output_bias
    )
    return projected.reshape(frame_count, places, channels).astype(jnp.bfloat16)


def body(
    segment_input,
    inner_input,
    lengths,
    inner_gain,
    causal_weight,
    causal_bias,
    attention_gain,
    triple_weight,
    triple_bias,
    output_weight,
    output_bias,
):
    clip_count, frame_count, row_count, column_count, channels = segment_input.shape
    activated = jax.nn.silu(normalize(inner_input, inner_gain)).astype(jnp.bfloat16)
    counts = lengths[:, 0]
    live_mask = (jnp.arange(frame_count, dtype=jnp.int32)[None, :] < counts[:, None]).astype(
        jnp.float32
    )
    carried = incoming_cache(*summarize(activated, counts))
    extended = jnp.concatenate([carried, activated], axis=1)
    padded = with_halo(as_sent(extended), (("rows", 2),), 1).astype(extended.dtype)
    convolved = convolve(padded, causal_weight, causal_bias)
    residual = (segment_input.astype(jnp.float32) + convolved).astype(jnp.bfloat16)
    residual = lax.optimization_barrier(residual)
    normed = normalize(residual, attention_gain).astype(jnp.bfloat16)
    row_devices = lax.axis_size("rows")
    per_device = clip_count * frame_count // row_devices
    grouped = normed.reshape(row_devices, per_device, row_count, column_count, channels)
    portion = lax.all_to_all(grouped, "rows", split_axis=0, concat_axis=2, tiled=True)
    owned = portion.shape[1]
    height = portion.shape[2]
    flat = portion.reshape(owned, height * column_count, channels)
    result = attend(flat, triple_weight, triple_bias, output_weight, output_bias)
    result = result.reshape(1, owned, height, column_count, channels)
    projected = lax.all_to_all(result, "rows", split_axis=2, concat_axis=0, tiled=True)
    projected = projected.reshape(clip_count, frame_count, row_count, column_count, channels)
    projected = lax.optimization_barrier(projected)
    summed = residual.astype(jnp.float32) + projected.astype(jnp.float32)
    return (summed * live_mask[:, :, None, None, None]).astype(jnp.bfloat16)


def activate(field, gain):
    return jax.nn.silu(normalize(field, gain)).astype(jnp.bfloat16)


def conv_part_kernel(plan, first_tap, x_ref, w_hbm, o_ref, w_vmem, sems):
    clips, held, rows, columns, width = x_ref.shape
    height = rows - 2
    places = height * columns
    channels = w_vmem.shape[-1]
    copies = []
    for index in range(len(plan)):
        for kh in range(3):
            slot_index = index * 3 + kh
            copy = pltpu.make_async_copy(
                w_hbm.at[first_tap + index, kh], w_vmem.at[slot_index], sems.at[slot_index]
            )
            copy.start()
            copies.append(copy)
    written = set()
    for index, (frame, slot, count) in enumerate(plan):
        for kh in (1, 0, 2):
            slot_index = index * 3 + kh
            copies[slot_index].wait()
            low = 1 if kh == 0 else 0
            high = height - 1 if kh == 2 else height
            if high <= low:
                continue
            weight = w_vmem[slot_index].reshape(width, channels)
            lhs = x_ref[:, frame : frame + count, low + kh : high + kh, :, :]
            lhs = lhs.reshape(clips * count * (high - low) * columns, width)
            term = jnp.dot(lhs, weight, preferred_element_type=jnp.float32)
            term = term.reshape(clips, count, (high - low) * columns, channels)
            rows_here = slice(low * columns, high * columns)
            for part in range(count):
                target = slot + part
                if target in written:
                    o_ref[:, target, rows_here] += term[:, part]
                else:
                    o_ref[:, target] = term[:, part]
                    written.add(target)


def column_taps(frames):
    columns = frames.shape[3]
    padded = jnp.pad(frames, ((0, 0), (0, 0), (1, 1), (1, 1), (0, 0)))
    return jnp.concatenate(
        [padded[:, :, :, kw : kw + columns] for kw in range(3)], axis=-1
    )


def conv_part(frames, causal_weight, plan, first_tap, slots, taps=None):
    clips, held, height, columns, channels = frames.shape
    if taps is None:
        taps = column_taps(frames)
    places = height * columns
    dots = sum(count for _, _, count in plan) * 3
    blocks = len(plan) * 3
    return pl.pallas_call(
        functools.partial(conv_part_kernel, plan, first_tap),
        in_specs=[
            pl.BlockSpec(memory_space=pltpu.VMEM),
            pl.BlockSpec(memory_space=pl.ANY),
        ],
        out_specs=pl.BlockSpec(memory_space=pltpu.VMEM),
        out_shape=jax.ShapeDtypeStruct((clips, slots, places, channels), jnp.float32),
        scratch_shapes=[
            pltpu.VMEM((blocks, 3, channels, channels), causal_weight.dtype),
            pltpu.SemaphoreType.DMA((blocks,)),
        ],
        compiler_params=pltpu.CompilerParams(vmem_limit_bytes=48 * 1024 * 1024),
        cost_estimate=pl.CostEstimate(
            flops=2 * clips * places * dots * 3 * channels * channels,
            transcendentals=0,
            bytes_accessed=blocks * 3 * channels * channels * 2
            + taps.size * 2
            + clips * slots * places * channels * 4,
        ),
    )(taps, causal_weight)


def conv_plans(slots):
    own, carried = {}, {}
    for kt in range(3):
        for slot in range(slots):
            source = slot + kt
            if source >= 2:
                own.setdefault(kt, []).append((source - 2, slot))
            else:
                carried.setdefault(kt, []).append((source, slot))
    return own, carried


def plan_of(table):
    taps = sorted(table)
    assert taps == list(range(taps[0], taps[-1] + 1))
    runs = []
    for kt in taps:
        pairs = sorted(table[kt], key=lambda pair: pair[1])
        frame, slot = pairs[0]
        assert pairs == [(frame + k, slot + k) for k in range(len(pairs))]
        runs.append((frame, slot, len(pairs)))
    return tuple(runs), taps[0]


def own_conv(own_frames, causal_weight, taps=None):
    own_table, _ = conv_plans(own_frames.shape[1])
    own_plan, own_first = plan_of(own_table)
    return conv_part(own_frames, causal_weight, own_plan, own_first, own_frames.shape[1], taps)


def carried_conv(carried_frames, causal_weight, slots):
    _, carried_table = conv_plans(slots)
    carried_plan, carried_first = plan_of(carried_table)
    return conv_part(carried_frames, causal_weight, carried_plan, carried_first, slots)


def frame_major(total, clips, height, columns):
    clips, slots, places, channels = total.shape
    return total.reshape(clips, slots, height, columns, channels)


def gathered_body(
    segment_input,
    inner_input,
    lengths,
    inner_gain,
    causal_weight,
    causal_bias,
    attention_gain,
    triple_weight,
    triple_bias,
    output_weight,
    output_bias,
):
    clip_count, frame_count, row_count, column_count, channels = segment_input.shape
    sections = lax.axis_size("tm")
    counts = lengths[:, 0]
    ahead = [(i, i + 1) for i in range(sections - 1)]
    both = jnp.concatenate([inner_input, segment_input], axis=0)
    both_all = lax.all_gather(both, "rows", axis=2, tiled=True)
    inner_all = both_all[:clip_count]
    segment_all = both_all[clip_count:]
    wide = (counts > 1)[:, None, None, None]
    last_raw = jnp.where(wide, inner_all[:, frame_count - 1], inner_all[:, 0])
    marked = jnp.concatenate(
        [
            inner_all[:, : frame_count - 1],
            jnp.where(wide, inner_all[:, frame_count - 1], UNUSED_MARK)[:, None],
        ],
        axis=1,
    )
    prev_raw = lax.ppermute(marked, "tm", ahead)
    own = activate(inner_all, inner_gain)
    own_taps = column_taps(own)
    own_taps, last_raw = lax.optimization_barrier((own_taps, last_raw))
    before_raw = lax.ppermute(last_raw, "tm", [(i, i + 2) for i in range(sections - 2)])
    own_sum = own_conv(own, causal_weight, own_taps)
    own_sum, prev_raw, before_raw = lax.optimization_barrier((own_sum, prev_raw, before_raw))
    prev = activate(prev_raw, inner_gain)
    before = activate(before_raw, inner_gain)
    prev_wide = (prev_raw[:, frame_count - 1, 0, 0, 0] > UNUSED_MARK / 2)[:, None, None, None]
    carried = jnp.stack(
        [
            jnp.where(prev_wide, prev[:, frame_count - 2], before),
            jnp.where(prev_wide, prev[:, frame_count - 1], prev[:, 0]),
        ],
        axis=1,
    )
    carried_sum = carried_conv(carried, causal_weight, frame_count)
    height = inner_all.shape[2]
    convolved = frame_major(own_sum + carried_sum, clip_count, height, column_count) + causal_bias
    residual = (segment_all.astype(jnp.float32) + convolved).astype(jnp.bfloat16)
    normed = normalize(residual, attention_gain).astype(jnp.bfloat16)
    height = normed.shape[2]
    frames = clip_count * frame_count
    places = height * column_count
    flat = normed.reshape(frames * places, channels)
    packed = (
        jnp.dot(flat, triple_weight[:, channels:], preferred_element_type=jnp.float32)
        + triple_bias[channels:]
    ).reshape(frames, places, 2 * channels)
    key_vectors = packed[:, :, :channels]
    values = packed[:, :, channels:].astype(jnp.bfloat16)
    start = lax.axis_index("rows") * row_count
    mine = lax.dynamic_slice_in_dim(normed, start, row_count, axis=2)
    queries = (
        jnp.dot(
            mine.reshape(-1, channels), triple_weight[:, :channels],
            preferred_element_type=jnp.float32,
        )
        + triple_bias[:channels]
    ).reshape(frames, row_count * column_count, channels)
    scores = jnp.einsum(
        "nqc,nkc->nqk", queries, key_vectors, precision=lax.Precision.HIGHEST
    ) / math.sqrt(channels)
    row_max = jnp.max(scores, axis=-1, keepdims=True)
    exponent = jnp.exp(scores - row_max)
    weights = (exponent / jnp.sum(exponent, axis=-1, keepdims=True)).astype(jnp.bfloat16)
    attended = jnp.einsum(
        "nqk,nkc->nqc", weights, values, preferred_element_type=jnp.float32
    ).astype(jnp.bfloat16)
    projected = (
        jnp.dot(attended.reshape(-1, channels), output_weight, preferred_element_type=jnp.float32)
        + output_bias
    ).astype(jnp.bfloat16)
    projected = projected.reshape(clip_count, frame_count, row_count, column_count, channels)
    residual_mine = lax.dynamic_slice_in_dim(residual, start, row_count, axis=2)
    live_mask = (jnp.arange(frame_count, dtype=jnp.int32)[None, :] < counts[:, None]).astype(
        jnp.float32
    )
    summed = residual_mine.astype(jnp.float32) + projected.astype(jnp.float32)
    return (summed * live_mask[:, :, None, None, None]).astype(jnp.bfloat16)


GATHER_LIMIT = 1 << 22


def chosen_body(segment_input, inner_input, *rest):
    gathered = inner_input.size * inner_input.dtype.itemsize * lax.axis_size("rows")
    if gathered <= GATHER_LIMIT:
        return gathered_body(segment_input, inner_input, *rest)
    return body(segment_input, inner_input, *rest)


def solution(mesh):
    placed = (
        P("clips", "tm", "rows", None, None),
        P("clips", "tm", "rows", None, None),
        P("clips", "tm"),
        P(),
        P(),
        P(),
        P(),
        P(),
        P(),
        P(),
        P(),
    )
    return jax.shard_map(
        chosen_body,
        mesh=mesh,
        in_specs=placed,
        out_specs=P("clips", "tm", "rows", None, None),
        check_vma=False,
    )
```

```python
import functools
import math

import jax
import jax.numpy as jnp
from jax import lax
from jax.sharding import PartitionSpec as P
from jax.experimental import pallas as pl
from jax.experimental.pallas import tpu as pltpu

EPSILON = 1e-06
UNUSED_MARK = -100.0


def prefix(part, axis, combine, identity):
    place = lax.axis_index(axis)
    gathered = jax.tree.map(lambda a: lax.all_gather(a, axis), part)
    state = jax.tree.map(lambda a, e: jnp.zeros_like(a) + jnp.asarray(e, a.dtype), part, identity)

    def one(step, state):
        return combine(
            state, jax.tree.map(lambda a: lax.dynamic_index_in_dim(a, step, 0, False), gathered)
        )

    return lax.fori_loop(0, place, one, state)


def as_sent(x):

    def short(part):
        return part.astype(jnp.bfloat16) if part.dtype == jnp.float32 else part

    return jax.tree.map(short, x)


def with_halo(cells, sides, width):
    for axis, dim in sides:
        count = lax.axis_size(axis)
        ends = count - 1
        head = lax.slice_in_dim(cells, 0, width, axis=dim)
        tail = lax.slice_in_dim(cells, cells.shape[dim] - width, cells.shape[dim], axis=dim)
        cells = jnp.concatenate(
            [
                lax.ppermute(tail, axis, [(i, (i + 1) % count) for i in range(ends)]),
                cells,
                lax.ppermute(head, axis, [((i + 1) % count, i) for i in range(ends)]),
            ],
            axis=dim,
        )
    return cells


def normalize(field, gain):
    widened = field.astype(jnp.float32)
    return widened * lax.rsqrt(jnp.mean(widened * widened, axis=-1, keepdims=True) + EPSILON) * gain


def last_two(extended, counts):
    slot_total = extended.shape[1]
    chosen = []
    for position in range(2):
        target = counts + position
        picked = jnp.zeros_like(extended[:, 0])
        for slot_index in range(slot_total):
            matches = (target == slot_index)[:, None, None, None]
            picked = jnp.where(matches, extended[:, slot_index], picked)
        chosen.append(picked)
    return jnp.stack(chosen, axis=1)


def summarize(activated, counts):
    blanks = jnp.zeros((activated.shape[0], 2) + activated.shape[2:], activated.dtype)
    summary = last_two(jnp.concatenate([blanks, activated], axis=1), counts)
    return (summary, jnp.minimum(counts, 2).astype(jnp.bfloat16))


def join_later(earlier, later):
    early_frames, early_count = earlier
    late_frames, late_count = later
    complete = (late_count > 1.5)[:, None, None, None, None]
    single = (late_count > 0.5)[:, None, None, None, None]
    shifted = jnp.concatenate([early_frames[:, 1:], late_frames[:, 1:]], axis=1)
    frames = jnp.where(complete, late_frames, jnp.where(single, shifted, early_frames))
    total_count = jnp.minimum(early_count + late_count, 2.0).astype(early_count.dtype)
    return (frames, total_count)


def incoming_cache(summary, counts):
    starting = (jnp.zeros_like(summary), jnp.zeros_like(counts))
    combined = prefix((summary, counts), "tm", join_later, starting)
    return combined[0]


def convolve(padded, causal_weight, causal_bias):
    clip_count, slot_total, rows_padded, column_count, channels = padded.shape
    frame_count = slot_total - 2
    row_count = rows_padded - 2
    widened = jnp.pad(padded, ((0, 0), (0, 0), (0, 0), (1, 1), (0, 0)))
    summed = jnp.zeros((clip_count * frame_count * row_count * column_count, channels), jnp.float32)
    for delta_time in range(3):
        for delta_row in range(3):
            window = widened[
                :, delta_time : delta_time + frame_count, delta_row : delta_row + row_count
            ]
            columns = jnp.concatenate(
                [window[:, :, :, delta_col : delta_col + column_count] for delta_col in range(3)],
                axis=-1,
            )
            kernel = causal_weight[delta_time, delta_row].reshape(3 * channels, channels)
            summed = summed + jnp.dot(
                columns.reshape(-1, 3 * channels), kernel, preferred_element_type=jnp.float32
            )
    return summed.reshape(clip_count, frame_count, row_count, column_count, channels) + causal_bias


def attend(normed, triple_weight, triple_bias, output_weight, output_bias):
    frame_count, places, channels = normed.shape
    packed = (
        jnp.dot(normed.reshape(-1, channels), triple_weight, preferred_element_type=jnp.float32)
        + triple_bias
    )
    packed = packed.reshape(frame_count, places, 3 * channels)
    queries = packed[:, :, :channels]
    key_vectors = packed[:, :, channels : 2 * channels]
    values = packed[:, :, 2 * channels :].astype(jnp.bfloat16)
    scores = jnp.einsum(
        "nqc,nkc->nqk", queries, key_vectors, precision=lax.Precision.HIGHEST
    ) / math.sqrt(channels)
    row_max = jnp.max(scores, axis=-1, keepdims=True)
    exponent = jnp.exp(scores - row_max)
    weights = (exponent / jnp.sum(exponent, axis=-1, keepdims=True)).astype(jnp.bfloat16)
    attended = jnp.einsum(
        "nqk,nkc->nqc", weights, values, preferred_element_type=jnp.float32
    ).astype(jnp.bfloat16)
    projected = (
        jnp.dot(attended.reshape(-1, channels), output_weight, preferred_element_type=jnp.float32)
        + output_bias
    )
    return projected.reshape(frame_count, places, channels).astype(jnp.bfloat16)


def body(
    segment_input,
    inner_input,
    lengths,
    inner_gain,
    causal_weight,
    causal_bias,
    attention_gain,
    triple_weight,
    triple_bias,
    output_weight,
    output_bias,
):
    clip_count, frame_count, row_count, column_count, channels = segment_input.shape
    activated = jax.nn.silu(normalize(inner_input, inner_gain)).astype(jnp.bfloat16)
    counts = lengths[:, 0]
    live_mask = (jnp.arange(frame_count, dtype=jnp.int32)[None, :] < counts[:, None]).astype(
        jnp.float32
    )
    carried = incoming_cache(*summarize(activated, counts))
    extended = jnp.concatenate([carried, activated], axis=1)
    padded = with_halo(as_sent(extended), (("rows", 2),), 1).astype(extended.dtype)
    convolved = convolve(padded, causal_weight, causal_bias)
    residual = (segment_input.astype(jnp.float32) + convolved).astype(jnp.bfloat16)
    residual = lax.optimization_barrier(residual)
    normed = normalize(residual, attention_gain).astype(jnp.bfloat16)
    row_devices = lax.axis_size("rows")
    per_device = clip_count * frame_count // row_devices
    grouped = normed.reshape(row_devices, per_device, row_count, column_count, channels)
    portion = lax.all_to_all(grouped, "rows", split_axis=0, concat_axis=2, tiled=True)
    owned = portion.shape[1]
    height = portion.shape[2]
    flat = portion.reshape(owned, height * column_count, channels)
    result = attend(flat, triple_weight, triple_bias, output_weight, output_bias)
    result = result.reshape(1, owned, height, column_count, channels)
    projected = lax.all_to_all(result, "rows", split_axis=2, concat_axis=0, tiled=True)
    projected = projected.reshape(clip_count, frame_count, row_count, column_count, channels)
    projected = lax.optimization_barrier(projected)
    summed = residual.astype(jnp.float32) + projected.astype(jnp.float32)
    return (summed * live_mask[:, :, None, None, None]).astype(jnp.bfloat16)


def activate(field, gain):
    return jax.nn.silu(normalize(field, gain)).astype(jnp.bfloat16)


def conv_part_kernel(plan, first_tap, x_ref, w_hbm, o_ref, w_vmem, sems):
    clips, held, rows, columns, width = x_ref.shape
    height = rows - 2
    places = height * columns
    channels = w_vmem.shape[-1]
    copies = []
    for index in range(len(plan)):
        for kh in range(3):
            slot_index = index * 3 + kh
            copy = pltpu.make_async_copy(
                w_hbm.at[first_tap + index, kh], w_vmem.at[slot_index], sems.at[slot_index]
            )
            copy.start()
            copies.append(copy)
    written = set()
    for index, (frame, slot, count) in enumerate(plan):
        for kh in (1, 0, 2):
            slot_index = index * 3 + kh
            copies[slot_index].wait()
            low = 1 if kh == 0 else 0
            high = height - 1 if kh == 2 else height
            if high <= low:
                continue
            weight = w_vmem[slot_index].reshape(width, channels)
            lhs = x_ref[:, frame : frame + count, low + kh : high + kh, :, :]
            lhs = lhs.reshape(clips * count * (high - low) * columns, width)
            term = jnp.dot(lhs, weight, preferred_element_type=jnp.float32)
            term = term.reshape(clips, count, (high - low) * columns, channels)
            rows_here = slice(low * columns, high * columns)
            for part in range(count):
                target = slot + part
                if target in written:
                    o_ref[:, target, rows_here] += term[:, part]
                else:
                    o_ref[:, target] = term[:, part]
                    written.add(target)


def column_taps(frames):
    columns = frames.shape[3]
    padded = jnp.pad(frames, ((0, 0), (0, 0), (1, 1), (1, 1), (0, 0)))
    return jnp.concatenate(
        [padded[:, :, :, kw : kw + columns] for kw in range(3)], axis=-1
    )


def conv_part(frames, causal_weight, plan, first_tap, slots, taps=None):
    clips, held, height, columns, channels = frames.shape
    if taps is None:
        taps = column_taps(frames)
    places = height * columns
    dots = sum(count for _, _, count in plan) * 3
    blocks = len(plan) * 3
    return pl.pallas_call(
        functools.partial(conv_part_kernel, plan, first_tap),
        in_specs=[
            pl.BlockSpec(memory_space=pltpu.VMEM),
            pl.BlockSpec(memory_space=pl.ANY),
        ],
        out_specs=pl.BlockSpec(memory_space=pltpu.VMEM),
        out_shape=jax.ShapeDtypeStruct((clips, slots, places, channels), jnp.float32),
        scratch_shapes=[
            pltpu.VMEM((blocks, 3, channels, channels), causal_weight.dtype),
            pltpu.SemaphoreType.DMA((blocks,)),
        ],
        compiler_params=pltpu.CompilerParams(vmem_limit_bytes=48 * 1024 * 1024),
        cost_estimate=pl.CostEstimate(
            flops=2 * clips * places * dots * 3 * channels * channels,
            transcendentals=0,
            bytes_accessed=blocks * 3 * channels * channels * 2
            + taps.size * 2
            + clips * slots * places * channels * 4,
        ),
    )(taps, causal_weight)


def conv_plans(slots):
    own, carried = {}, {}
    for kt in range(3):
        for slot in range(slots):
            source = slot + kt
            if source >= 2:
                own.setdefault(kt, []).append((source - 2, slot))
            else:
                carried.setdefault(kt, []).append((source, slot))
    return own, carried


def plan_of(table):
    taps = sorted(table)
    assert taps == list(range(taps[0], taps[-1] + 1))
    runs = []
    for kt in taps:
        pairs = sorted(table[kt], key=lambda pair: pair[1])
        frame, slot = pairs[0]
        assert pairs == [(frame + k, slot + k) for k in range(len(pairs))]
        runs.append((frame, slot, len(pairs)))
    return tuple(runs), taps[0]


def own_conv(own_frames, causal_weight, taps=None):
    own_table, _ = conv_plans(own_frames.shape[1])
    own_plan, own_first = plan_of(own_table)
    return conv_part(own_frames, causal_weight, own_plan, own_first, own_frames.shape[1], taps)


def carried_conv(carried_frames, causal_weight, slots):
    _, carried_table = conv_plans(slots)
    carried_plan, carried_first = plan_of(carried_table)
    return conv_part(carried_frames, causal_weight, carried_plan, carried_first, slots)


def frame_major(total, clips, height, columns):
    clips, slots, places, channels = total.shape
    return total.reshape(clips, slots, height, columns, channels)


def gathered_body(
    segment_input,
    inner_input,
    lengths,
    inner_gain,
    causal_weight,
    causal_bias,
    attention_gain,
    triple_weight,
    triple_bias,
    output_weight,
    output_bias,
):
    clip_count, frame_count, row_count, column_count, channels = segment_input.shape
    sections = lax.axis_size("tm")
    counts = lengths[:, 0]
    ahead = [(i, i + 1) for i in range(sections - 1)]
    both = jnp.concatenate([inner_input, segment_input], axis=0)
    both_all = lax.all_gather(both, "rows", axis=2, tiled=True)
    inner_all = both_all[:clip_count]
    segment_all = both_all[clip_count:]
    wide = (counts > 1)[:, None, None, None]
    last_raw = jnp.where(wide, inner_all[:, frame_count - 1], inner_all[:, 0])
    marked = jnp.concatenate(
        [
            inner_all[:, : frame_count - 1],
            jnp.where(wide, inner_all[:, frame_count - 1], UNUSED_MARK)[:, None],
        ],
        axis=1,
    )
    own = activate(inner_all, inner_gain)
    own_taps = column_taps(own)
    own_taps, last_raw, marked = lax.optimization_barrier((own_taps, last_raw, marked))
    prev_raw = lax.ppermute(marked, "tm", ahead)
    before_raw = lax.ppermute(last_raw, "tm", [(i, i + 2) for i in range(sections - 2)])
    own_sum = own_conv(own, causal_weight, own_taps)
    own_sum, prev_raw, before_raw = lax.optimization_barrier((own_sum, prev_raw, before_raw))
    prev = activate(prev_raw, inner_gain)
    before = activate(before_raw, inner_gain)
    prev_wide = (prev_raw[:, frame_count - 1, 0, 0, 0] > UNUSED_MARK / 2)[:, None, None, None]
    carried = jnp.stack(
        [
            jnp.where(prev_wide, prev[:, frame_count - 2], before),
            jnp.where(prev_wide, prev[:, frame_count - 1], prev[:, 0]),
        ],
        axis=1,
    )
    carried_sum = carried_conv(carried, causal_weight, frame_count)
    height = inner_all.shape[2]
    convolved = frame_major(own_sum + carried_sum, clip_count, height, column_count) + causal_bias
    residual = (segment_all.astype(jnp.float32) + convolved).astype(jnp.bfloat16)
    normed = normalize(residual, attention_gain).astype(jnp.bfloat16)
    height = normed.shape[2]
    frames = clip_count * frame_count
    places = height * column_count
    flat = normed.reshape(frames * places, channels)
    packed = (
        jnp.dot(flat, triple_weight[:, channels:], preferred_element_type=jnp.float32)
        + triple_bias[channels:]
    ).reshape(frames, places, 2 * channels)
    key_vectors = packed[:, :, :channels]
    values = packed[:, :, channels:].astype(jnp.bfloat16)
    start = lax.axis_index("rows") * row_count
    mine = lax.dynamic_slice_in_dim(normed, start, row_count, axis=2)
    queries = (
        jnp.dot(
            mine.reshape(-1, channels), triple_weight[:, :channels],
            preferred_element_type=jnp.float32,
        )
        + triple_bias[:channels]
    ).reshape(frames, row_count * column_count, channels)
    scores = jnp.einsum(
        "nqc,nkc->nqk", queries, key_vectors, precision=lax.Precision.HIGHEST
    ) / math.sqrt(channels)
    row_max = jnp.max(scores, axis=-1, keepdims=True)
    exponent = jnp.exp(scores - row_max)
    weights = (exponent / jnp.sum(exponent, axis=-1, keepdims=True)).astype(jnp.bfloat16)
    attended = jnp.einsum(
        "nqk,nkc->nqc", weights, values, preferred_element_type=jnp.float32
    ).astype(jnp.bfloat16)
    projected = (
        jnp.dot(attended.reshape(-1, channels), output_weight, preferred_element_type=jnp.float32)
        + output_bias
    ).astype(jnp.bfloat16)
    projected = projected.reshape(clip_count, frame_count, row_count, column_count, channels)
    residual_mine = lax.dynamic_slice_in_dim(residual, start, row_count, axis=2)
    live_mask = (jnp.arange(frame_count, dtype=jnp.int32)[None, :] < counts[:, None]).astype(
        jnp.float32
    )
    summed = residual_mine.astype(jnp.float32) + projected.astype(jnp.float32)
    return (summed * live_mask[:, :, None, None, None]).astype(jnp.bfloat16)


GATHER_LIMIT = 1 << 22


def chosen_body(segment_input, inner_input, *rest):
    gathered = inner_input.size * inner_input.dtype.itemsize * lax.axis_size("rows")
    if gathered <= GATHER_LIMIT:
        return gathered_body(segment_input, inner_input, *rest)
    return body(segment_input, inner_input, *rest)


def solution(mesh):
    placed = (
        P("clips", "tm", "rows", None, None),
        P("clips", "tm", "rows", None, None),
        P("clips", "tm"),
        P(),
        P(),
        P(),
        P(),
        P(),
        P(),
        P(),
        P(),
    )
    return jax.shard_map(
        chosen_body,
        mesh=mesh,
        in_specs=placed,
        out_specs=P("clips", "tm", "rows", None, None),
        check_vma=False,
    )
```

```python
import functools
import math

import jax
import jax.numpy as jnp
from jax import lax
from jax.sharding import PartitionSpec as P
from jax.experimental import pallas as pl
from jax.experimental.pallas import tpu as pltpu

EPSILON = 1e-06
UNUSED_MARK = -100.0


def prefix(part, axis, combine, identity):
    place = lax.axis_index(axis)
    gathered = jax.tree.map(lambda a: lax.all_gather(a, axis), part)
    state = jax.tree.map(lambda a, e: jnp.zeros_like(a) + jnp.asarray(e, a.dtype), part, identity)

    def one(step, state):
        return combine(
            state, jax.tree.map(lambda a: lax.dynamic_index_in_dim(a, step, 0, False), gathered)
        )

    return lax.fori_loop(0, place, one, state)


def as_sent(x):

    def short(part):
        return part.astype(jnp.bfloat16) if part.dtype == jnp.float32 else part

    return jax.tree.map(short, x)


def with_halo(cells, sides, width):
    for axis, dim in sides:
        count = lax.axis_size(axis)
        ends = count - 1
        head = lax.slice_in_dim(cells, 0, width, axis=dim)
        tail = lax.slice_in_dim(cells, cells.shape[dim] - width, cells.shape[dim], axis=dim)
        cells = jnp.concatenate(
            [
                lax.ppermute(tail, axis, [(i, (i + 1) % count) for i in range(ends)]),
                cells,
                lax.ppermute(head, axis, [((i + 1) % count, i) for i in range(ends)]),
            ],
            axis=dim,
        )
    return cells


def normalize(field, gain):
    widened = field.astype(jnp.float32)
    return widened * lax.rsqrt(jnp.mean(widened * widened, axis=-1, keepdims=True) + EPSILON) * gain


def last_two(extended, counts):
    slot_total = extended.shape[1]
    chosen = []
    for position in range(2):
        target = counts + position
        picked = jnp.zeros_like(extended[:, 0])
        for slot_index in range(slot_total):
            matches = (target == slot_index)[:, None, None, None]
            picked = jnp.where(matches, extended[:, slot_index], picked)
        chosen.append(picked)
    return jnp.stack(chosen, axis=1)


def summarize(activated, counts):
    blanks = jnp.zeros((activated.shape[0], 2) + activated.shape[2:], activated.dtype)
    summary = last_two(jnp.concatenate([blanks, activated], axis=1), counts)
    return (summary, jnp.minimum(counts, 2).astype(jnp.bfloat16))


def join_later(earlier, later):
    early_frames, early_count = earlier
    late_frames, late_count = later
    complete = (late_count > 1.5)[:, None, None, None, None]
    single = (late_count > 0.5)[:, None, None, None, None]
    shifted = jnp.concatenate([early_frames[:, 1:], late_frames[:, 1:]], axis=1)
    frames = jnp.where(complete, late_frames, jnp.where(single, shifted, early_frames))
    total_count = jnp.minimum(early_count + late_count, 2.0).astype(early_count.dtype)
    return (frames, total_count)


def incoming_cache(summary, counts):
    starting = (jnp.zeros_like(summary), jnp.zeros_like(counts))
    combined = prefix((summary, counts), "tm", join_later, starting)
    return combined[0]


def convolve(padded, causal_weight, causal_bias):
    clip_count, slot_total, rows_padded, column_count, channels = padded.shape
    frame_count = slot_total - 2
    row_count = rows_padded - 2
    widened = jnp.pad(padded, ((0, 0), (0, 0), (0, 0), (1, 1), (0, 0)))
    summed = jnp.zeros((clip_count * frame_count * row_count * column_count, channels), jnp.float32)
    for delta_time in range(3):
        for delta_row in range(3):
            window = widened[
                :, delta_time : delta_time + frame_count, delta_row : delta_row + row_count
            ]
            columns = jnp.concatenate(
                [window[:, :, :, delta_col : delta_col + column_count] for delta_col in range(3)],
                axis=-1,
            )
            kernel = causal_weight[delta_time, delta_row].reshape(3 * channels, channels)
            summed = summed + jnp.dot(
                columns.reshape(-1, 3 * channels), kernel, preferred_element_type=jnp.float32
            )
    return summed.reshape(clip_count, frame_count, row_count, column_count, channels) + causal_bias


def attend(normed, triple_weight, triple_bias, output_weight, output_bias):
    frame_count, places, channels = normed.shape
    packed = (
        jnp.dot(normed.reshape(-1, channels), triple_weight, preferred_element_type=jnp.float32)
        + triple_bias
    )
    packed = packed.reshape(frame_count, places, 3 * channels)
    queries = packed[:, :, :channels]
    key_vectors = packed[:, :, channels : 2 * channels]
    values = packed[:, :, 2 * channels :].astype(jnp.bfloat16)
    scores = jnp.einsum(
        "nqc,nkc->nqk", queries, key_vectors, precision=lax.Precision.HIGHEST
    ) / math.sqrt(channels)
    row_max = jnp.max(scores, axis=-1, keepdims=True)
    exponent = jnp.exp(scores - row_max)
    weights = (exponent / jnp.sum(exponent, axis=-1, keepdims=True)).astype(jnp.bfloat16)
    attended = jnp.einsum(
        "nqk,nkc->nqc", weights, values, preferred_element_type=jnp.float32
    ).astype(jnp.bfloat16)
    projected = (
        jnp.dot(attended.reshape(-1, channels), output_weight, preferred_element_type=jnp.float32)
        + output_bias
    )
    return projected.reshape(frame_count, places, channels).astype(jnp.bfloat16)


def body(
    segment_input,
    inner_input,
    lengths,
    inner_gain,
    causal_weight,
    causal_bias,
    attention_gain,
    triple_weight,
    triple_bias,
    output_weight,
    output_bias,
):
    clip_count, frame_count, row_count, column_count, channels = segment_input.shape
    activated = jax.nn.silu(normalize(inner_input, inner_gain)).astype(jnp.bfloat16)
    counts = lengths[:, 0]
    live_mask = (jnp.arange(frame_count, dtype=jnp.int32)[None, :] < counts[:, None]).astype(
        jnp.float32
    )
    carried = incoming_cache(*summarize(activated, counts))
    extended = jnp.concatenate([carried, activated], axis=1)
    padded = with_halo(as_sent(extended), (("rows", 2),), 1).astype(extended.dtype)
    convolved = convolve(padded, causal_weight, causal_bias)
    residual = (segment_input.astype(jnp.float32) + convolved).astype(jnp.bfloat16)
    residual = lax.optimization_barrier(residual)
    normed = normalize(residual, attention_gain).astype(jnp.bfloat16)
    row_devices = lax.axis_size("rows")
    per_device = clip_count * frame_count // row_devices
    grouped = normed.reshape(row_devices, per_device, row_count, column_count, channels)
    portion = lax.all_to_all(grouped, "rows", split_axis=0, concat_axis=2, tiled=True)
    owned = portion.shape[1]
    height = portion.shape[2]
    flat = portion.reshape(owned, height * column_count, channels)
    result = attend(flat, triple_weight, triple_bias, output_weight, output_bias)
    result = result.reshape(1, owned, height, column_count, channels)
    projected = lax.all_to_all(result, "rows", split_axis=2, concat_axis=0, tiled=True)
    projected = projected.reshape(clip_count, frame_count, row_count, column_count, channels)
    projected = lax.optimization_barrier(projected)
    summed = residual.astype(jnp.float32) + projected.astype(jnp.float32)
    return (summed * live_mask[:, :, None, None, None]).astype(jnp.bfloat16)


def activate(field, gain):
    return jax.nn.silu(normalize(field, gain)).astype(jnp.bfloat16)


def conv_part_kernel(plan, first_tap, x_ref, w_hbm, o_ref, w_vmem, sems):
    clips, held, rows, columns, width = x_ref.shape
    height = rows - 2
    places = height * columns
    channels = w_vmem.shape[-1]
    copies = []
    for index in range(len(plan)):
        for kh in range(3):
            slot_index = index * 3 + kh
            copy = pltpu.make_async_copy(
                w_hbm.at[first_tap + index, kh], w_vmem.at[slot_index], sems.at[slot_index]
            )
            copy.start()
            copies.append(copy)
    written = set()
    for index, (frame, slot, count) in enumerate(plan):
        for kh in (1, 0, 2):
            slot_index = index * 3 + kh
            copies[slot_index].wait()
            low = 1 if kh == 0 else 0
            high = height - 1 if kh == 2 else height
            if high <= low:
                continue
            weight = w_vmem[slot_index].reshape(width, channels)
            lhs = x_ref[:, frame : frame + count, low + kh : high + kh, :, :]
            lhs = lhs.reshape(clips * count * (high - low) * columns, width)
            term = jnp.dot(lhs, weight, preferred_element_type=jnp.float32)
            term = term.reshape(clips, count, (high - low) * columns, channels)
            rows_here = slice(low * columns, high * columns)
            for part in range(count):
                target = slot + part
                if target in written:
                    o_ref[:, target, rows_here] += term[:, part]
                else:
                    o_ref[:, target] = term[:, part]
                    written.add(target)


def column_taps(frames):
    columns = frames.shape[3]
    padded = jnp.pad(frames, ((0, 0), (0, 0), (1, 1), (1, 1), (0, 0)))
    return jnp.concatenate(
        [padded[:, :, :, kw : kw + columns] for kw in range(3)], axis=-1
    )


def conv_part(frames, causal_weight, plan, first_tap, slots, taps=None):
    clips, held, height, columns, channels = frames.shape
    if taps is None:
        taps = column_taps(frames)
    places = height * columns
    dots = sum(count for _, _, count in plan) * 3
    blocks = len(plan) * 3
    return pl.pallas_call(
        functools.partial(conv_part_kernel, plan, first_tap),
        in_specs=[
            pl.BlockSpec(memory_space=pltpu.VMEM),
            pl.BlockSpec(memory_space=pl.ANY),
        ],
        out_specs=pl.BlockSpec(memory_space=pltpu.VMEM),
        out_shape=jax.ShapeDtypeStruct((clips, slots, places, channels), jnp.float32),
        scratch_shapes=[
            pltpu.VMEM((blocks, 3, channels, channels), causal_weight.dtype),
            pltpu.SemaphoreType.DMA((blocks,)),
        ],
        compiler_params=pltpu.CompilerParams(vmem_limit_bytes=48 * 1024 * 1024),
        cost_estimate=pl.CostEstimate(
            flops=2 * clips * places * dots * 3 * channels * channels,
            transcendentals=0,
            bytes_accessed=blocks * 3 * channels * channels * 2
            + taps.size * 2
            + clips * slots * places * channels * 4,
        ),
    )(taps, causal_weight)


def conv_plans(slots):
    own, carried = {}, {}
    for kt in range(3):
        for slot in range(slots):
            source = slot + kt
            if source >= 2:
                own.setdefault(kt, []).append((source - 2, slot))
            else:
                carried.setdefault(kt, []).append((source, slot))
    return own, carried


def plan_of(table):
    taps = sorted(table)
    assert taps == list(range(taps[0], taps[-1] + 1))
    runs = []
    for kt in taps:
        pairs = sorted(table[kt], key=lambda pair: pair[1])
        frame, slot = pairs[0]
        assert pairs == [(frame + k, slot + k) for k in range(len(pairs))]
        runs.append((frame, slot, len(pairs)))
    return tuple(runs), taps[0]


def own_conv(own_frames, causal_weight, taps=None):
    own_table, _ = conv_plans(own_frames.shape[1])
    own_plan, own_first = plan_of(own_table)
    return conv_part(own_frames, causal_weight, own_plan, own_first, own_frames.shape[1], taps)


def carried_conv(carried_frames, causal_weight, slots):
    _, carried_table = conv_plans(slots)
    carried_plan, carried_first = plan_of(carried_table)
    return conv_part(carried_frames, causal_weight, carried_plan, carried_first, slots)


def frame_major(total, clips, height, columns):
    clips, slots, places, channels = total.shape
    return total.reshape(clips, slots, height, columns, channels)


def gathered_body(
    segment_input,
    inner_input,
    lengths,
    inner_gain,
    causal_weight,
    causal_bias,
    attention_gain,
    triple_weight,
    triple_bias,
    output_weight,
    output_bias,
):
    clip_count, frame_count, row_count, column_count, channels = segment_input.shape
    sections = lax.axis_size("tm")
    counts = lengths[:, 0]
    ahead = [(i, i + 1) for i in range(sections - 1)]
    both = jnp.concatenate([inner_input, segment_input], axis=0)
    both_all = lax.all_gather(both, "rows", axis=2, tiled=True)
    inner_all = both_all[:clip_count]
    segment_all = both_all[clip_count:]
    wide = (counts > 1)[:, None, None, None]
    last_raw = jnp.where(wide, inner_all[:, frame_count - 1], inner_all[:, 0])
    marked = jnp.concatenate(
        [
            inner_all[:, : frame_count - 1],
            jnp.where(wide, inner_all[:, frame_count - 1], UNUSED_MARK)[:, None],
        ],
        axis=1,
    )
    prev_raw = lax.ppermute(marked, "tm", ahead)
    own = activate(inner_all, inner_gain)
    own_taps = column_taps(own)
    own_taps, last_raw, _ = lax.optimization_barrier((own_taps, last_raw, marked))
    before_raw = lax.ppermute(last_raw, "tm", [(i, i + 2) for i in range(sections - 2)])
    own_sum = own_conv(own, causal_weight, own_taps)
    own_sum, prev_raw, before_raw = lax.optimization_barrier((own_sum, prev_raw, before_raw))
    prev = activate(prev_raw, inner_gain)
    before = activate(before_raw, inner_gain)
    prev_wide = (prev_raw[:, frame_count - 1, 0, 0, 0] > UNUSED_MARK / 2)[:, None, None, None]
    carried = jnp.stack(
        [
            jnp.where(prev_wide, prev[:, frame_count - 2], before),
            jnp.where(prev_wide, prev[:, frame_count - 1], prev[:, 0]),
        ],
        axis=1,
    )
    carried_sum = carried_conv(carried, causal_weight, frame_count)
    height = inner_all.shape[2]
    convolved = frame_major(own_sum + carried_sum, clip_count, height, column_count) + causal_bias
    residual = (segment_all.astype(jnp.float32) + convolved).astype(jnp.bfloat16)
    normed = normalize(residual, attention_gain).astype(jnp.bfloat16)
    height = normed.shape[2]
    frames = clip_count * frame_count
    places = height * column_count
    flat = normed.reshape(frames * places, channels)
    packed = (
        jnp.dot(flat, triple_weight[:, channels:], preferred_element_type=jnp.float32)
        + triple_bias[channels:]
    ).reshape(frames, places, 2 * channels)
    key_vectors = packed[:, :, :channels]
    values = packed[:, :, channels:].astype(jnp.bfloat16)
    start = lax.axis_index("rows") * row_count
    mine = lax.dynamic_slice_in_dim(normed, start, row_count, axis=2)
    queries = (
        jnp.dot(
            mine.reshape(-1, channels), triple_weight[:, :channels],
            preferred_element_type=jnp.float32,
        )
        + triple_bias[:channels]
    ).reshape(frames, row_count * column_count, channels)
    scores = jnp.einsum(
        "nqc,nkc->nqk", queries, key_vectors, precision=lax.Precision.HIGHEST
    ) / math.sqrt(channels)
    row_max = jnp.max(scores, axis=-1, keepdims=True)
    exponent = jnp.exp(scores - row_max)
    weights = (exponent / jnp.sum(exponent, axis=-1, keepdims=True)).astype(jnp.bfloat16)
    attended = jnp.einsum(
        "nqk,nkc->nqc", weights, values, preferred_element_type=jnp.float32
    ).astype(jnp.bfloat16)
    projected = (
        jnp.dot(attended.reshape(-1, channels), output_weight, preferred_element_type=jnp.float32)
        + output_bias
    ).astype(jnp.bfloat16)
    projected = projected.reshape(clip_count, frame_count, row_count, column_count, channels)
    residual_mine = lax.dynamic_slice_in_dim(residual, start, row_count, axis=2)
    live_mask = (jnp.arange(frame_count, dtype=jnp.int32)[None, :] < counts[:, None]).astype(
        jnp.float32
    )
    summed = residual_mine.astype(jnp.float32) + projected.astype(jnp.float32)
    return (summed * live_mask[:, :, None, None, None]).astype(jnp.bfloat16)


GATHER_LIMIT = 1 << 22


def chosen_body(segment_input, inner_input, *rest):
    gathered = inner_input.size * inner_input.dtype.itemsize * lax.axis_size("rows")
    if gathered <= GATHER_LIMIT:
        return gathered_body(segment_input, inner_input, *rest)
    return body(segment_input, inner_input, *rest)


def solution(mesh):
    placed = (
        P("clips", "tm", "rows", None, None),
        P("clips", "tm", "rows", None, None),
        P("clips", "tm"),
        P(),
        P(),
        P(),
        P(),
        P(),
        P(),
        P(),
        P(),
    )
    return jax.shard_map(
        chosen_body,
        mesh=mesh,
        in_specs=placed,
        out_specs=P("clips", "tm", "rows", None, None),
        check_vma=False,
    )
```

```python
import functools
import math

import jax
import jax.numpy as jnp
from jax import lax
from jax.sharding import PartitionSpec as P
from jax.experimental import pallas as pl
from jax.experimental.pallas import tpu as pltpu

EPSILON = 1e-06
UNUSED_MARK = -100.0


def prefix(part, axis, combine, identity):
    place = lax.axis_index(axis)
    gathered = jax.tree.map(lambda a: lax.all_gather(a, axis), part)
    state = jax.tree.map(lambda a, e: jnp.zeros_like(a) + jnp.asarray(e, a.dtype), part, identity)

    def one(step, state):
        return combine(
            state, jax.tree.map(lambda a: lax.dynamic_index_in_dim(a, step, 0, False), gathered)
        )

    return lax.fori_loop(0, place, one, state)


def as_sent(x):

    def short(part):
        return part.astype(jnp.bfloat16) if part.dtype == jnp.float32 else part

    return jax.tree.map(short, x)


def with_halo(cells, sides, width):
    for axis, dim in sides:
        count = lax.axis_size(axis)
        ends = count - 1
        head = lax.slice_in_dim(cells, 0, width, axis=dim)
        tail = lax.slice_in_dim(cells, cells.shape[dim] - width, cells.shape[dim], axis=dim)
        cells = jnp.concatenate(
            [
                lax.ppermute(tail, axis, [(i, (i + 1) % count) for i in range(ends)]),
                cells,
                lax.ppermute(head, axis, [((i + 1) % count, i) for i in range(ends)]),
            ],
            axis=dim,
        )
    return cells


def normalize(field, gain):
    widened = field.astype(jnp.float32)
    return widened * lax.rsqrt(jnp.mean(widened * widened, axis=-1, keepdims=True) + EPSILON) * gain


def last_two(extended, counts):
    slot_total = extended.shape[1]
    chosen = []
    for position in range(2):
        target = counts + position
        picked = jnp.zeros_like(extended[:, 0])
        for slot_index in range(slot_total):
            matches = (target == slot_index)[:, None, None, None]
            picked = jnp.where(matches, extended[:, slot_index], picked)
        chosen.append(picked)
    return jnp.stack(chosen, axis=1)


def summarize(activated, counts):
    blanks = jnp.zeros((activated.shape[0], 2) + activated.shape[2:], activated.dtype)
    summary = last_two(jnp.concatenate([blanks, activated], axis=1), counts)
    return (summary, jnp.minimum(counts, 2).astype(jnp.bfloat16))


def join_later(earlier, later):
    early_frames, early_count = earlier
    late_frames, late_count = later
    complete = (late_count > 1.5)[:, None, None, None, None]
    single = (late_count > 0.5)[:, None, None, None, None]
    shifted = jnp.concatenate([early_frames[:, 1:], late_frames[:, 1:]], axis=1)
    frames = jnp.where(complete, late_frames, jnp.where(single, shifted, early_frames))
    total_count = jnp.minimum(early_count + late_count, 2.0).astype(early_count.dtype)
    return (frames, total_count)


def incoming_cache(summary, counts):
    starting = (jnp.zeros_like(summary), jnp.zeros_like(counts))
    combined = prefix((summary, counts), "tm", join_later, starting)
    return combined[0]


def convolve(padded, causal_weight, causal_bias):
    clip_count, slot_total, rows_padded, column_count, channels = padded.shape
    frame_count = slot_total - 2
    row_count = rows_padded - 2
    widened = jnp.pad(padded, ((0, 0), (0, 0), (0, 0), (1, 1), (0, 0)))
    summed = jnp.zeros((clip_count * frame_count * row_count * column_count, channels), jnp.float32)
    for delta_time in range(3):
        for delta_row in range(3):
            window = widened[
                :, delta_time : delta_time + frame_count, delta_row : delta_row + row_count
            ]
            columns = jnp.concatenate(
                [window[:, :, :, delta_col : delta_col + column_count] for delta_col in range(3)],
                axis=-1,
            )
            kernel = causal_weight[delta_time, delta_row].reshape(3 * channels, channels)
            summed = summed + jnp.dot(
                columns.reshape(-1, 3 * channels), kernel, preferred_element_type=jnp.float32
            )
    return summed.reshape(clip_count, frame_count, row_count, column_count, channels) + causal_bias


def attend(normed, triple_weight, triple_bias, output_weight, output_bias):
    frame_count, places, channels = normed.shape
    packed = (
        jnp.dot(normed.reshape(-1, channels), triple_weight, preferred_element_type=jnp.float32)
        + triple_bias
    )
    packed = packed.reshape(frame_count, places, 3 * channels)
    queries = packed[:, :, :channels]
    key_vectors = packed[:, :, channels : 2 * channels]
    values = packed[:, :, 2 * channels :].astype(jnp.bfloat16)
    scores = jnp.einsum(
        "nqc,nkc->nqk", queries, key_vectors, precision=lax.Precision.HIGHEST
    ) / math.sqrt(channels)
    row_max = jnp.max(scores, axis=-1, keepdims=True)
    exponent = jnp.exp(scores - row_max)
    weights = (exponent / jnp.sum(exponent, axis=-1, keepdims=True)).astype(jnp.bfloat16)
    attended = jnp.einsum(
        "nqk,nkc->nqc", weights, values, preferred_element_type=jnp.float32
    ).astype(jnp.bfloat16)
    projected = (
        jnp.dot(attended.reshape(-1, channels), output_weight, preferred_element_type=jnp.float32)
        + output_bias
    )
    return projected.reshape(frame_count, places, channels).astype(jnp.bfloat16)


def body(
    segment_input,
    inner_input,
    lengths,
    inner_gain,
    causal_weight,
    causal_bias,
    attention_gain,
    triple_weight,
    triple_bias,
    output_weight,
    output_bias,
):
    clip_count, frame_count, row_count, column_count, channels = segment_input.shape
    activated = jax.nn.silu(normalize(inner_input, inner_gain)).astype(jnp.bfloat16)
    counts = lengths[:, 0]
    live_mask = (jnp.arange(frame_count, dtype=jnp.int32)[None, :] < counts[:, None]).astype(
        jnp.float32
    )
    carried = incoming_cache(*summarize(activated, counts))
    extended = jnp.concatenate([carried, activated], axis=1)
    padded = with_halo(as_sent(extended), (("rows", 2),), 1).astype(extended.dtype)
    convolved = convolve(padded, causal_weight, causal_bias)
    residual = (segment_input.astype(jnp.float32) + convolved).astype(jnp.bfloat16)
    residual = lax.optimization_barrier(residual)
    normed = normalize(residual, attention_gain).astype(jnp.bfloat16)
    row_devices = lax.axis_size("rows")
    per_device = clip_count * frame_count // row_devices
    grouped = normed.reshape(row_devices, per_device, row_count, column_count, channels)
    portion = lax.all_to_all(grouped, "rows", split_axis=0, concat_axis=2, tiled=True)
    owned = portion.shape[1]
    height = portion.shape[2]
    flat = portion.reshape(owned, height * column_count, channels)
    result = attend(flat, triple_weight, triple_bias, output_weight, output_bias)
    result = result.reshape(1, owned, height, column_count, channels)
    projected = lax.all_to_all(result, "rows", split_axis=2, concat_axis=0, tiled=True)
    projected = projected.reshape(clip_count, frame_count, row_count, column_count, channels)
    projected = lax.optimization_barrier(projected)
    summed = residual.astype(jnp.float32) + projected.astype(jnp.float32)
    return (summed * live_mask[:, :, None, None, None]).astype(jnp.bfloat16)


def activate(field, gain):
    return jax.nn.silu(normalize(field, gain)).astype(jnp.bfloat16)


def conv_part_kernel(plan, first_tap, x_hbm, w_hbm, o_ref, x_ref, w_vmem, sems, x_sem):
    clips, held, rows, columns, width = x_ref.shape
    height = rows - 2
    places = height * columns
    channels = w_vmem.shape[-1]
    x_copy = pltpu.make_async_copy(x_hbm, x_ref, x_sem)
    x_copy.start()
    copies = []
    for index in range(len(plan)):
        for kh in range(3):
            slot_index = index * 3 + kh
            copy = pltpu.make_async_copy(
                w_hbm.at[first_tap + index, kh], w_vmem.at[slot_index], sems.at[slot_index]
            )
            copy.start()
            copies.append(copy)
    x_copy.wait()
    written = set()
    for index, (frame, slot, count) in enumerate(plan):
        for kh in (1, 0, 2):
            slot_index = index * 3 + kh
            copies[slot_index].wait()
            low = 1 if kh == 0 else 0
            high = height - 1 if kh == 2 else height
            if high <= low:
                continue
            weight = w_vmem[slot_index].reshape(width, channels)
            lhs = x_ref[:, frame : frame + count, low + kh : high + kh, :, :]
            lhs = lhs.reshape(clips * count * (high - low) * columns, width)
            term = jnp.dot(lhs, weight, preferred_element_type=jnp.float32)
            term = term.reshape(clips, count, (high - low) * columns, channels)
            rows_here = slice(low * columns, high * columns)
            for part in range(count):
                target = slot + part
                if target in written:
                    o_ref[:, target, rows_here] += term[:, part]
                else:
                    o_ref[:, target] = term[:, part]
                    written.add(target)


def column_taps(frames):
    columns = frames.shape[3]
    padded = jnp.pad(frames, ((0, 0), (0, 0), (1, 1), (1, 1), (0, 0)))
    return jnp.concatenate(
        [padded[:, :, :, kw : kw + columns] for kw in range(3)], axis=-1
    )


def conv_part(frames, causal_weight, plan, first_tap, slots, taps=None):
    clips, held, height, columns, channels = frames.shape
    if taps is None:
        taps = column_taps(frames)
    places = height * columns
    dots = sum(count for _, _, count in plan) * 3
    blocks = len(plan) * 3
    return pl.pallas_call(
        functools.partial(conv_part_kernel, plan, first_tap),
        in_specs=[
            pl.BlockSpec(memory_space=pl.ANY),
            pl.BlockSpec(memory_space=pl.ANY),
        ],
        out_specs=pl.BlockSpec(memory_space=pltpu.VMEM),
        out_shape=jax.ShapeDtypeStruct((clips, slots, places, channels), jnp.float32),
        scratch_shapes=[
            pltpu.VMEM(taps.shape, taps.dtype),
            pltpu.VMEM((blocks, 3, channels, channels), causal_weight.dtype),
            pltpu.SemaphoreType.DMA((blocks,)),
            pltpu.SemaphoreType.DMA(()),
        ],
        compiler_params=pltpu.CompilerParams(vmem_limit_bytes=48 * 1024 * 1024),
        cost_estimate=pl.CostEstimate(
            flops=2 * clips * places * dots * 3 * channels * channels,
            transcendentals=0,
            bytes_accessed=blocks * 3 * channels * channels * 2
            + taps.size * 2
            + clips * slots * places * channels * 4,
        ),
    )(taps, causal_weight)


def conv_plans(slots):
    own, carried = {}, {}
    for kt in range(3):
        for slot in range(slots):
            source = slot + kt
            if source >= 2:
                own.setdefault(kt, []).append((source - 2, slot))
            else:
                carried.setdefault(kt, []).append((source, slot))
    return own, carried


def plan_of(table):
    taps = sorted(table)
    assert taps == list(range(taps[0], taps[-1] + 1))
    runs = []
    for kt in taps:
        pairs = sorted(table[kt], key=lambda pair: pair[1])
        frame, slot = pairs[0]
        assert pairs == [(frame + k, slot + k) for k in range(len(pairs))]
        runs.append((frame, slot, len(pairs)))
    return tuple(runs), taps[0]


def own_conv(own_frames, causal_weight, taps=None):
    own_table, _ = conv_plans(own_frames.shape[1])
    own_plan, own_first = plan_of(own_table)
    return conv_part(own_frames, causal_weight, own_plan, own_first, own_frames.shape[1], taps)


def carried_conv(carried_frames, causal_weight, slots):
    _, carried_table = conv_plans(slots)
    carried_plan, carried_first = plan_of(carried_table)
    return conv_part(carried_frames, causal_weight, carried_plan, carried_first, slots)


def frame_major(total, clips, height, columns):
    clips, slots, places, channels = total.shape
    return total.reshape(clips, slots, height, columns, channels)


def gathered_body(
    segment_input,
    inner_input,
    lengths,
    inner_gain,
    causal_weight,
    causal_bias,
    attention_gain,
    triple_weight,
    triple_bias,
    output_weight,
    output_bias,
):
    clip_count, frame_count, row_count, column_count, channels = segment_input.shape
    sections = lax.axis_size("tm")
    counts = lengths[:, 0]
    ahead = [(i, i + 1) for i in range(sections - 1)]
    both = jnp.concatenate([inner_input, segment_input], axis=0)
    both_all = lax.all_gather(both, "rows", axis=2, tiled=True)
    inner_all = both_all[:clip_count]
    segment_all = both_all[clip_count:]
    wide = (counts > 1)[:, None, None, None]
    last_raw = jnp.where(wide, inner_all[:, frame_count - 1], inner_all[:, 0])
    marked = jnp.concatenate(
        [
            inner_all[:, : frame_count - 1],
            jnp.where(wide, inner_all[:, frame_count - 1], UNUSED_MARK)[:, None],
        ],
        axis=1,
    )
    prev_raw = lax.ppermute(marked, "tm", ahead)
    own = activate(inner_all, inner_gain)
    own_taps = column_taps(own)
    own_taps, last_raw = lax.optimization_barrier((own_taps, last_raw))
    before_raw = lax.ppermute(last_raw, "tm", [(i, i + 2) for i in range(sections - 2)])
    own_sum = own_conv(own, causal_weight, own_taps)
    own_sum, prev_raw, before_raw = lax.optimization_barrier((own_sum, prev_raw, before_raw))
    prev = activate(prev_raw, inner_gain)
    before = activate(before_raw, inner_gain)
    prev_wide = (prev_raw[:, frame_count - 1, 0, 0, 0] > UNUSED_MARK / 2)[:, None, None, None]
    carried = jnp.stack(
        [
            jnp.where(prev_wide, prev[:, frame_count - 2], before),
            jnp.where(prev_wide, prev[:, frame_count - 1], prev[:, 0]),
        ],
        axis=1,
    )
    carried_sum = carried_conv(carried, causal_weight, frame_count)
    height = inner_all.shape[2]
    convolved = frame_major(own_sum + carried_sum, clip_count, height, column_count) + causal_bias
    residual = (segment_all.astype(jnp.float32) + convolved).astype(jnp.bfloat16)
    normed = normalize(residual, attention_gain).astype(jnp.bfloat16)
    height = normed.shape[2]
    frames = clip_count * frame_count
    places = height * column_count
    flat = normed.reshape(frames * places, channels)
    packed = (
        jnp.dot(flat, triple_weight[:, channels:], preferred_element_type=jnp.float32)
        + triple_bias[channels:]
    ).reshape(frames, places, 2 * channels)
    key_vectors = packed[:, :, :channels]
    values = packed[:, :, channels:].astype(jnp.bfloat16)
    start = lax.axis_index("rows") * row_count
    mine = lax.dynamic_slice_in_dim(normed, start, row_count, axis=2)
    queries = (
        jnp.dot(
            mine.reshape(-1, channels), triple_weight[:, :channels],
            preferred_element_type=jnp.float32,
        )
        + triple_bias[:channels]
    ).reshape(frames, row_count * column_count, channels)
    scores = jnp.einsum(
        "nqc,nkc->nqk", queries, key_vectors, precision=lax.Precision.HIGHEST
    ) / math.sqrt(channels)
    row_max = jnp.max(scores, axis=-1, keepdims=True)
    exponent = jnp.exp(scores - row_max)
    weights = (exponent / jnp.sum(exponent, axis=-1, keepdims=True)).astype(jnp.bfloat16)
    attended = jnp.einsum(
        "nqk,nkc->nqc", weights, values, preferred_element_type=jnp.float32
    ).astype(jnp.bfloat16)
    projected = (
        jnp.dot(attended.reshape(-1, channels), output_weight, preferred_element_type=jnp.float32)
        + output_bias
    ).astype(jnp.bfloat16)
    projected = projected.reshape(clip_count, frame_count, row_count, column_count, channels)
    residual_mine = lax.dynamic_slice_in_dim(residual, start, row_count, axis=2)
    live_mask = (jnp.arange(frame_count, dtype=jnp.int32)[None, :] < counts[:, None]).astype(
        jnp.float32
    )
    summed = residual_mine.astype(jnp.float32) + projected.astype(jnp.float32)
    return (summed * live_mask[:, :, None, None, None]).astype(jnp.bfloat16)


GATHER_LIMIT = 1 << 22


def chosen_body(segment_input, inner_input, *rest):
    gathered = inner_input.size * inner_input.dtype.itemsize * lax.axis_size("rows")
    if gathered <= GATHER_LIMIT:
        return gathered_body(segment_input, inner_input, *rest)
    return body(segment_input, inner_input, *rest)


def solution(mesh):
    placed = (
        P("clips", "tm", "rows", None, None),
        P("clips", "tm", "rows", None, None),
        P("clips", "tm"),
        P(),
        P(),
        P(),
        P(),
        P(),
        P(),
        P(),
        P(),
    )
    return jax.shard_map(
        chosen_body,
        mesh=mesh,
        in_specs=placed,
        out_specs=P("clips", "tm", "rows", None, None),
        check_vma=False,
    )
```
